32 devices in a mesh: groups: 2 (over y), seq: 4 (over z), tensor: 4 (over x, core).
Axes of the slice: x: 2, y: 2, z: 4, core: 2. Of those that a mesh axis runs over, the one named last changes fastest.
Arguments:
- x_in: bfloat16 [4096, 5120], P(('groups', 'seq'), 'tensor'), parts along dimension 0, may hold values from -6 to 6
- z_gate: bfloat16 [4096, 5120], P(('groups', 'seq'), 'tensor'), parts along dimension 0, may hold values from -32 to 32
- bc_in: bfloat16 [4096, 256], P(('groups', 'seq')), parts along dimension 0, may hold values from -6 to 6
- step_size: float32 [80, 4096], P('tensor', ('groups', 'seq')), parts along dimension 1, may hold values from 0 to 0.4
- log_keep: float32 [80, 4096], P('tensor', ('groups', 'seq')), parts along dimension 1, may hold values from -1 to 0
- skip_gain: float32 [80], P('tensor'), may hold values from 0.5 to 2
- conv_x: bfloat16 [4, 5120], P(None, 'tensor'), may hold values from -3 to 3
- conv_bc: bfloat16 [4, 256], replicated, may hold values from -3 to 3
- norm_gain: float32 [5120], P('tensor'), may hold values from 0.1 to 1.9
- seg_ends: int32 [1024], P(('groups', 'seq')), parts along dimension 0, may hold values from 0 to 2047, as said below
- pool_query: bfloat16 [320, 5120], P(('groups', 'seq'), 'tensor'), parts along dimension 0, may hold values from -64 to 64
- pool_start: int32 [320], P(('groups', 'seq')), parts along dimension 0, may hold values from 0 to 255, as said below
- pool_stop: int32 [320], P(('groups', 'seq')), parts along dimension 0, may hold values from 64 to 512
Outputs:
- mixed_seq: bfloat16 [4096, 5120], P(('groups', 'seq'), 'tensor'), parts along dimension 0
- pooled: float32 [320, 5120], P(('groups', 'seq'), 'tensor'), parts along dimension 0
The draws below stay inside these ranges and needn't reach their ends.
There are 2 independent parts, one for each index of `groups`. The reference program is written for one: setup_inputs(seed, part) draws one part's arguments, and reference() takes and returns one part's arrays. A program takes and returns all parts, laid end to end along the dimension named above; an argument that names none is the same for every part. Nothing has to cross between parts.
Inputs may be any that keep to these rules, and one draw needn't show every extreme that they name: The tokens fall into blocks of 512; block b holds exactly the 128 segment ends seg_ends[b * 128] to seg_ends[(b + 1) * 128 - 1], strictly increasing. pool_start < pool_stop for every pooled row.
All inputs are finite; a program needn't handle non-finite values.
Results may differ from the reference program's by a relative error of at most 0.039.
Values may be sent and summed in bfloat16 or wider, within the bound.
No kernel may reach another device: no remote copies, remote signals or barrier semaphores. Data moves between devices by JAX's collectives and lax.ppermute only.
A program may use at most 64 MiB of HBM per device.

```python
import math
import jax
import jax.numpy as jnp
from jax import lax

HEADS = 80
HEAD_DIM = 64
STATE = 128
CONV = 4
STRETCH = 256
POOL_HEADS = 32
TOK_DEV = 512
SEG_DEV = 128
POOL_DEV = 40
INNER = 5120
POOL_DIM = 160
RECORD_ITEMS = 2048
SEGS = 512
POOLS = 160


def decay_plan(key):
    head_key = jax.random.fold_in(key, 11)
    head_pick = jax.random.uniform(jax.random.fold_in(head_key, 1), (HEADS,))
    share_slow = 0.5
    slow_head = head_pick < share_slow
    slow_rate = jnp.exp(jax.random.uniform(jax.random.fold_in(head_key, 2), (HEADS,), minval=math.log(0.1), maxval=math.log(0.3))) / RECORD_ITEMS
    fast_rate = jnp.exp(jax.random.uniform(jax.random.fold_in(head_key, 3), (HEADS,), minval=math.log(1.0 / 50.0), maxval=math.log(1.0 / 30.0)))
    return jnp.where(slow_head, slow_rate, fast_rate)


def draw_step_size(key, part):
    reference_frequency = decay_plan(key)
    roughness_measure = jax.random.uniform(jax.random.fold_in(key, 21), (HEADS, RECORD_ITEMS), minval=0.5, maxval=1.5)
    return jnp.sqrt(2.0 * reference_frequency)[:, None] * roughness_measure


def draw_log_keep(key, part):
    reference_frequency = decay_plan(key)
    roughness_measure = jax.random.uniform(jax.random.fold_in(key, 31), (HEADS, RECORD_ITEMS), minval=0.5, maxval=1.5)
    device_factor = jnp.exp(jax.random.uniform(jax.random.fold_in(key, 32), (RECORD_ITEMS // TOK_DEV,), minval=math.log(0.5), maxval=math.log(2.0)))
    element_amounts = jnp.repeat(device_factor, TOK_DEV)
    spike_location = jax.random.randint(jax.random.fold_in(key, 33), (2,), 0, RECORD_ITEMS)
    spike_cost_factor = jax.random.uniform(jax.random.fold_in(key, 34), (2,), minval=-math.log(0.8), maxval=-math.log(0.5))
    element_locations = jnp.arange(RECORD_ITEMS, dtype=jnp.int32)
    spike_occurrences = jnp.sum(jnp.where(element_locations[None, :] == spike_location[:, None], spike_cost_factor[:, None], 0.0), axis=0)
    return -(reference_frequency[:, None] * roughness_measure * element_amounts[None, :] + spike_occurrences[None, :])


def draw_z_gate(key, part):
    position = jnp.arange(INNER, dtype=jnp.float32) / INNER
    channel_scale = jnp.exp(jax.random.uniform(jax.random.fold_in(key, 42), (INNER,), minval=math.log(0.5), maxval=math.log(2.0)))
    base_rows = jnp.clip(jax.random.normal(jax.random.fold_in(key, 41), (RECORD_ITEMS, INNER)), -5.0, 5.0)
    channel_trend = 3.0 ** position
    return (base_rows * (channel_trend * channel_scale)[None, :]).astype(jnp.bfloat16)


def draw_pool_query(key, part):
    return (2.5 * jnp.clip(jax.random.normal(jax.random.fold_in(key, 93), (POOLS, INNER)), -6.0, 6.0)).astype(jnp.bfloat16)


def draw_seg_ends(key, part):
    blocks_count = RECORD_ITEMS // TOK_DEV
    scores = jax.random.randint(jax.random.fold_in(key, 71), (blocks_count, TOK_DEV), 0, 2 ** 19)
    distinct = scores * TOK_DEV + jnp.arange(TOK_DEV, dtype=jnp.int32)[None, :]
    unused, chosen = lax.top_k(distinct, SEG_DEV)
    ordered = jnp.sort(chosen, axis=1)
    starts = (jnp.arange(blocks_count, dtype=jnp.int32) * TOK_DEV)[:, None]
    return (ordered + starts).reshape(SEGS).astype(jnp.int32)


def span_plan(key):
    starts = jax.random.randint(jax.random.fold_in(key, 81), (POOLS,), 0, SEGS // 2)
    lengths = jax.random.randint(jax.random.fold_in(key, 82), (POOLS,), SEGS // 8, SEGS + 1)
    return (starts.astype(jnp.int32), jnp.minimum(starts + lengths, SEGS).astype(jnp.int32))


def draw_pool_start(key, part):
    return span_plan(key)[0]


def draw_pool_stop(key, part):
    return span_plan(key)[1]


def steps_of(stream_key, dims, cuts, least, high):
    def one(dim, parts):
        draws = jax.random.uniform(jax.random.fold_in(jax.random.fold_in(stream_key, 6), dim), (parts,), jnp.float32, least / len(cuts), high / len(cuts))
        return jnp.repeat(jnp.exp(draws), dims[dim] // parts).reshape((-1,) + (1,) * (len(dims) - dim - 1))

    factor_of = one(*cuts[0])
    for cut in cuts[1:]:
        factor_of = factor_of * one(*cut)
    return factor_of


def noise(key, dims, scale, most, cuts=(), kind=jnp.bfloat16):
    gain = steps_of(key, dims, cuts, -0.22, 0.18) if cuts else 1.0
    result = jax.random.normal(key, dims, jnp.float32) * scale * gain
    return jnp.minimum(jnp.maximum(result, -most), most).astype(kind)


def setup_inputs(seed: int = 0, part: int = 0) -> dict:
    key_list = jax.random.split(jax.random.key(seed), 14)
    part_splits = jax.random.split(jax.random.fold_in(key_list[13], part), 14)
    x_in = noise(part_splits[0], (RECORD_ITEMS, INNER), 1.0, 6.0, ((0, 4), (1, 4)))
    z_gate = draw_z_gate(jax.random.fold_in(jax.random.fold_in(key_list[13], part), 71), part)
    bc_in = noise(part_splits[2], (RECORD_ITEMS, 2 * STATE), 1.0, 6.0, ((0, 4),))
    step_size = draw_step_size(jax.random.fold_in(jax.random.fold_in(key_list[13], part), 71), part)
    log_keep = draw_log_keep(jax.random.fold_in(jax.random.fold_in(key_list[13], part), 71), part)
    skip_gain = jnp.clip(0.5 + 1.5 * jax.random.uniform(key_list[5], (HEADS,), jnp.float32) ** steps_of(key_list[5], (HEADS,), ((0, 4),), -0.2, 0.2), 0.5, 2.0)
    conv_x = noise(key_list[6], (CONV, INNER), CONV ** -0.5, 3.0, ((1, 4),))
    conv_bc = noise(key_list[7], (CONV, 2 * STATE), CONV ** -0.5, 3.0)
    norm_gain = jnp.clip(1.0 + 0.18 * jax.random.normal(key_list[8], (INNER,), jnp.float32), 0.1, 1.9)
    seg_ends = draw_seg_ends(jax.random.fold_in(jax.random.fold_in(key_list[13], part), 71), part)
    pool_query = draw_pool_query(jax.random.fold_in(jax.random.fold_in(key_list[13], part), 71), part)
    pool_start = draw_pool_start(jax.random.fold_in(jax.random.fold_in(key_list[13], part), 71), part)
    pool_stop = draw_pool_stop(jax.random.fold_in(jax.random.fold_in(key_list[13], part), 71), part)
    return dict(x_in=x_in, z_gate=z_gate, bc_in=bc_in, step_size=step_size, log_keep=log_keep, skip_gain=skip_gain, conv_x=conv_x, conv_bc=conv_bc, norm_gain=norm_gain, seg_ends=seg_ends, pool_query=pool_query, pool_start=pool_start, pool_stop=pool_stop)


EPSILON = 1e-05
MASKED = -1e+30

def silu_act(values):
    return values / (1.0 + jnp.exp(-values))

def causal_conv(before, current, weights):
    kernel_width = weights.shape[0]
    length = current.shape[0]
    padded = jnp.concatenate([before, current], axis=0)
    summed = jnp.zeros(current.shape, jnp.float32)
    for offset in range(kernel_width):
        summed = summed + padded[offset:offset + length].astype(jnp.float32) * weights[offset].astype(jnp.float32)
    return silu_act(summed).astype(jnp.bfloat16)

def stretch_local(x_block, b_block, c_block, step_block, keep_block):
    block_len = x_block.shape[0]
    cumul_keep = jnp.cumsum(keep_block, axis=1)
    lower_mask = lax.broadcasted_iota(jnp.int32, (block_len, block_len), 0) >= lax.broadcasted_iota(jnp.int32, (block_len, block_len), 1)
    inner_prod = jnp.dot(c_block, b_block.T, preferred_element_type=jnp.float32)
    spread = cumul_keep[:, :, None] - cumul_keep[:, None, :]
    decay_mask = jnp.where(lower_mask[None], jnp.exp(jnp.where(lower_mask[None], spread, 0.0)), 0.0)
    mixing = (decay_mask * inner_prod[None] * step_block[:, None, :]).astype(jnp.bfloat16)
    mixing = lax.optimization_barrier(mixing).astype(jnp.float32)
    intra_part = jnp.einsum('hij,jhp->ihp', mixing, x_block.astype(jnp.float32), precision=lax.Precision.HIGHEST)
    tail_weight = jnp.exp(cumul_keep[:, -1:] - cumul_keep) * step_block
    weighted = (tail_weight.T[:, :, None] * x_block.astype(jnp.float32)).astype(jnp.bfloat16)
    weighted = lax.optimization_barrier(weighted).astype(jnp.float32)
    stretch_state = jnp.einsum('jhp,js->hps', weighted, b_block.astype(jnp.float32), precision=lax.Precision.HIGHEST)
    return (intra_part, stretch_state, cumul_keep)

def reference(x_in, z_gate, bc_in, step_size, log_keep, skip_gain, conv_x, conv_bc, norm_gain, seg_ends, pool_query, pool_start, pool_stop):
    rim_rows = CONV - 1
    x_conv = causal_conv(jnp.zeros((rim_rows, INNER), jnp.bfloat16), x_in, conv_x)
    bc_conv = causal_conv(jnp.zeros((rim_rows, 2 * STATE), jnp.bfloat16), bc_in, conv_bc)
    stretch_count = RECORD_ITEMS // STRETCH
    x_blocks = x_conv.reshape(stretch_count, STRETCH, HEADS, HEAD_DIM)
    b_blocks = bc_conv[:, :STATE].reshape(stretch_count, STRETCH, STATE)
    c_blocks = bc_conv[:, STATE:].reshape(stretch_count, STRETCH, STATE)
    step_blocks = step_size.reshape(HEADS, stretch_count, STRETCH).transpose(1, 0, 2)
    keep_blocks = log_keep.reshape(HEADS, stretch_count, STRETCH).transpose(1, 0, 2)

    def advance(state_in, pieces):
        x_block, b_block, c_block, step_block, keep_block = pieces
        intra_part, stretch_state, cumul_keep = stretch_local(x_block, b_block, c_block, step_block, keep_block)
        from_state = jnp.einsum('is,hps->ihp', c_block.astype(jnp.float32), state_in, precision=lax.Precision.HIGHEST)
        block_out = intra_part + jnp.exp(cumul_keep).T[:, :, None] * from_state
        state_next = jnp.exp(cumul_keep[:, -1])[:, None, None] * state_in + stretch_state
        return (state_next, block_out)
    initial = jnp.zeros((HEADS, HEAD_DIM, STATE), jnp.float32)
    unused, block_outs = lax.scan(advance, initial, (x_blocks, b_blocks, c_blocks, step_blocks, keep_blocks))
    ssd_out = block_outs.reshape(RECORD_ITEMS, HEADS, HEAD_DIM) + skip_gain[None, :, None] * x_conv.reshape(RECORD_ITEMS, HEADS, HEAD_DIM).astype(jnp.float32)
    gated = ssd_out.reshape(RECORD_ITEMS, INNER) * silu_act(z_gate.astype(jnp.float32))
    square_mean = lax.optimization_barrier(jnp.sum(gated * gated, axis=1)) / INNER
    mixed_seq = (gated * lax.rsqrt(square_mean + EPSILON)[:, None] * norm_gain[None, :]).astype(jnp.bfloat16)
    summaries = jnp.take(mixed_seq, seg_ends, axis=0)
    keys_all = summaries.reshape(SEGS, POOL_HEADS, POOL_DIM).astype(jnp.float32)
    seg_index = jnp.arange(SEGS, dtype=jnp.int32)
    scale_factor = 1.0 / math.sqrt(POOL_DIM)

    def attend(block):
        query_block, start_block, stop_block = block
        query_heads = query_block.reshape(POOL_DEV, POOL_HEADS, POOL_DIM).astype(jnp.float32)
        logits = jnp.einsum('pad,sad->aps', query_heads, keys_all, precision=lax.Precision.HIGHEST) * scale_factor
        inside = (seg_index[None, :] >= start_block[:, None]) & (seg_index[None, :] < stop_block[:, None])
        logits = jnp.where(inside[None], logits, MASKED)
        peak = lax.optimization_barrier(jnp.max(logits, axis=2, keepdims=True))
        expo = jnp.where(inside[None], jnp.exp(logits - peak), 0.0)
        denom = lax.optimization_barrier(jnp.sum(expo, axis=2))
        weights = lax.optimization_barrier(expo.astype(jnp.bfloat16)).astype(jnp.float32)
        numer = jnp.einsum('aps,sad->pad', weights, keys_all, precision=lax.Precision.HIGHEST)
        return (numer / denom.T[:, :, None]).reshape(POOL_DEV, INNER)
    block_total = POOLS // POOL_DEV
    pooled = lax.map(attend, (pool_query.reshape(block_total, POOL_DEV, INNER), pool_start.reshape(block_total, POOL_DEV), pool_stop.reshape(block_total, POOL_DEV)))
    return (mixed_seq, pooled.reshape(POOLS, INNER))
```

```python
import math

import jax
import jax.numpy as jnp
from jax import lax
from jax.sharding import PartitionSpec as P

STRETCH = 256
POOL_HEADS = 32


EPSILON = 1e-05
MASKED = -1e30


def passed_along(value, axis, steps):
    count = lax.axis_size(axis)
    leading, last = (max(0, -steps), min(count, count - steps))
    return lax.ppermute(value, axis, [(source, source + steps) for source in range(leading, last)])


def silu_act(values):
    return values / (1.0 + jnp.exp(-values))


def causal_conv(before, current, weights):
    kernel_width = weights.shape[0]
    length = current.shape[0]
    padded = jnp.concatenate([before, current], axis=0)
    summed = jnp.zeros(current.shape, jnp.float32)
    for offset in range(kernel_width):
        summed = summed + padded[offset : offset + length].astype(jnp.float32) * weights[
            offset
        ].astype(jnp.float32)
    return silu_act(summed).astype(jnp.bfloat16)


def stretch_local(x_block, b_block, c_block, step_block, keep_block):
    block_len = x_block.shape[0]
    cumul_keep = jnp.cumsum(keep_block, axis=1)
    lower_mask = lax.broadcasted_iota(jnp.int32, (block_len, block_len), 0) >= lax.broadcasted_iota(
        jnp.int32, (block_len, block_len), 1
    )
    inner_prod = jnp.einsum("is,js->ij", c_block, b_block, preferred_element_type=jnp.float32)
    spread = cumul_keep[:, :, None] - cumul_keep[:, None, :]
    decay_mask = jnp.where(lower_mask[None], jnp.exp(jnp.where(lower_mask[None], spread, 0.0)), 0.0)
    mixing = (decay_mask * inner_prod[None] * step_block[:, None, :]).astype(jnp.bfloat16)
    intra_part = jnp.einsum("hij,jhp->ihp", mixing, x_block, preferred_element_type=jnp.float32)
    tail_weight = jnp.exp(cumul_keep[:, -1:] - cumul_keep) * step_block
    weighted = (tail_weight.T[:, :, None] * x_block.astype(jnp.float32)).astype(jnp.bfloat16)
    stretch_state = jnp.einsum("jhp,js->hps", weighted, b_block, preferred_element_type=jnp.float32)
    return (intra_part, stretch_state, cumul_keep)


def combine(earlier, later):
    return (earlier[0] * jnp.exp(later[1])[:, None, None] + later[0], earlier[1] + later[1])


def exclusive_scan(state, decay, axis):
    count = lax.axis_size(axis)
    window = (state, decay)
    before = (jnp.zeros_like(state), jnp.zeros_like(decay))
    shift = 1
    while shift < count:
        sent_state = passed_along(window[0].astype(jnp.bfloat16), axis, shift)
        sent_decay = passed_along(window[1], axis, shift)
        received = (sent_state.astype(jnp.float32), sent_decay)
        before = combine(received, before)
        if shift * 2 < count:
            window = combine(received, window)
        shift *= 2
    return before[0]


def read_state(c_block, state_in):
    state_high = state_in.astype(jnp.bfloat16)
    state_low = (state_in - state_high.astype(jnp.float32)).astype(jnp.bfloat16)
    high_part = jnp.einsum("is,hps->ihp", c_block, state_high, preferred_element_type=jnp.float32)
    low_part = jnp.einsum("is,hps->ihp", c_block, state_low, preferred_element_type=jnp.float32)
    return high_part + low_part


def local(
    x_in,
    z_gate,
    bc_in,
    step_size,
    log_keep,
    skip_gain,
    conv_x,
    conv_bc,
    norm_gain,
    seg_ends,
    pool_query,
    pool_start,
    pool_stop,
):
    tok_rows = x_in.shape[0]
    channels = x_in.shape[1]
    heads_local = step_size.shape[0]
    head_width = channels // heads_local
    state_width = bc_in.shape[1] // 2
    rim_rows = conv_x.shape[0] - 1
    seq_count = lax.axis_size("seq")
    queries_all = lax.all_gather(pool_query, "seq", axis=0, tiled=True)
    start_all = lax.all_gather(pool_start, "seq", axis=0, tiled=True)
    stop_all = lax.all_gather(pool_stop, "seq", axis=0, tiled=True)
    edge_rows = jnp.concatenate([x_in[tok_rows - rim_rows :], bc_in[tok_rows - rim_rows :]], axis=1)
    before = passed_along(edge_rows, "seq", 1)
    x_conv = causal_conv(before[:, :channels], x_in, conv_x)
    bc_conv = causal_conv(before[:, channels:], bc_in, conv_bc)
    b_mat = bc_conv[:, :state_width]
    c_mat = bc_conv[:, state_width:]
    x_heads = x_conv.reshape(tok_rows, heads_local, head_width)
    stretch_count = tok_rows // STRETCH
    entry_state = jnp.zeros((heads_local, head_width, state_width), jnp.float32)
    decay_total = jnp.zeros((heads_local,), jnp.float32)
    saved_parts = []
    for block_index in range(stretch_count):
        first_row = block_index * STRETCH
        last_row = first_row + STRETCH
        intra_part, stretch_state, cumul_keep = stretch_local(
            x_heads[first_row:last_row],
            b_mat[first_row:last_row],
            c_mat[first_row:last_row],
            step_size[:, first_row:last_row],
            log_keep[:, first_row:last_row],
        )
        saved_parts.append((intra_part, cumul_keep, entry_state, decay_total))
        entry_state = jnp.exp(cumul_keep[:, -1])[:, None, None] * entry_state + stretch_state
        decay_total = decay_total + cumul_keep[:, -1]
    incoming = exclusive_scan(entry_state, decay_total, "seq")
    pieces_out = []
    for block_index in range(stretch_count):
        intra_part, cumul_keep, entry_part, decay_part = saved_parts[block_index]
        first_row = block_index * STRETCH
        state_in = entry_part + jnp.exp(decay_part)[:, None, None] * incoming
        from_state = read_state(c_mat[first_row : first_row + STRETCH], state_in)
        pieces_out.append(intra_part + jnp.exp(cumul_keep).T[:, :, None] * from_state)
    ssd_out = jnp.concatenate(pieces_out, axis=0) + skip_gain[None, :, None] * x_heads.astype(
        jnp.float32
    )
    gated = ssd_out.reshape(tok_rows, channels) * silu_act(z_gate.astype(jnp.float32))
    square_sum = lax.psum(jnp.sum(gated * gated, axis=1), "tensor")
    width_all = channels * lax.axis_size("tensor")
    mixed_seq = (
        gated * lax.rsqrt(square_sum / width_all + EPSILON)[:, None] * norm_gain[None, :]
    ).astype(jnp.bfloat16)
    local_ends = seg_ends - lax.axis_index("seq") * tok_rows
    summaries = jnp.take(mixed_seq, local_ends, axis=0)
    pool_heads_local = POOL_HEADS // lax.axis_size("tensor")
    pool_width = channels // pool_heads_local
    scale_factor = 1.0 / math.sqrt(pool_width)
    pools_local = pool_query.shape[0]
    pools_all = queries_all.shape[0]
    segs_local = summaries.shape[0]
    queries = queries_all.reshape(pools_all, pool_heads_local, pool_width)
    seg_index = lax.axis_index("seq") * segs_local + lax.iota(jnp.int32, segs_local)
    inside = (seg_index[None, :] >= start_all[:, None]) & (seg_index[None, :] < stop_all[:, None])
    keys_block = summaries.reshape(segs_local, pool_heads_local, pool_width)
    logits = (
        jnp.einsum("pad,rad->apr", queries, keys_block, preferred_element_type=jnp.float32)
        * scale_factor
    )
    logits = jnp.where(inside[None], logits, MASKED)
    peak = jnp.max(logits, axis=2)
    expo = jnp.where(inside[None], jnp.exp(logits - peak[:, :, None]), 0.0)
    denom = jnp.sum(expo, axis=2)
    numer = jnp.einsum(
        "apr,rad->pad", expo.astype(jnp.bfloat16), keys_block, preferred_element_type=jnp.float32
    )
    numer_sent = lax.all_to_all(
        numer.reshape(pools_all, channels).astype(jnp.bfloat16), "seq", 0, 0, tiled=True
    )
    stats = jnp.concatenate([peak.T, denom.T], axis=1)
    stats_sent = lax.all_to_all(stats, "seq", 0, 0, tiled=True)
    numer_parts = numer_sent.astype(jnp.float32).reshape(
        seq_count, pools_local, pool_heads_local, pool_width
    )
    stats_parts = stats_sent.reshape(seq_count, pools_local, 2, pool_heads_local)
    peak_parts = stats_parts[:, :, 0]
    denom_parts = stats_parts[:, :, 1]
    peak_all = jnp.max(peak_parts, axis=0)
    rescale = jnp.exp(peak_parts - peak_all[None])
    denom_all = jnp.sum(rescale * denom_parts, axis=0)
    numer_all = jnp.sum(rescale[:, :, :, None] * numer_parts, axis=0)
    pooled = (numer_all / denom_all[:, :, None]).reshape(pools_local, channels)
    return (mixed_seq, pooled)


def solution(mesh):
    in_specs = (
        P(("groups", "seq"), "tensor"),
        P(("groups", "seq"), "tensor"),
        P(("groups", "seq"), None),
        P("tensor", ("groups", "seq")),
        P("tensor", ("groups", "seq")),
        P("tensor"),
        P(None, "tensor"),
        P(),
        P("tensor"),
        P(("groups", "seq")),
        P(("groups", "seq"), "tensor"),
        P(("groups", "seq")),
        P(("groups", "seq")),
    )
    out_specs = (P(("groups", "seq"), "tensor"), P(("groups", "seq"), "tensor"))
    return jax.shard_map(local, mesh=mesh, in_specs=in_specs, out_specs=out_specs, check_vma=False)
```

```python
import math

import jax
import jax.numpy as jnp
from jax import lax
from jax.sharding import PartitionSpec as P

STRETCH = 256
POOL_HEADS = 32


EPSILON = 1e-05
MASKED = -1e30


def passed_along(value, axis, steps):
    count = lax.axis_size(axis)
    leading, last = (max(0, -steps), min(count, count - steps))
    return lax.ppermute(value, axis, [(source, source + steps) for source in range(leading, last)])


def silu_act(values):
    return values / (1.0 + jnp.exp(-values))


def causal_conv(before, current, weights):
    kernel_width = weights.shape[0]
    length = current.shape[0]
    padded = jnp.concatenate([before, current], axis=0)
    summed = jnp.zeros(current.shape, jnp.float32)
    for offset in range(kernel_width):
        summed = summed + padded[offset : offset + length].astype(jnp.float32) * weights[
            offset
        ].astype(jnp.float32)
    return silu_act(summed).astype(jnp.bfloat16)


def stretch_local(x_block, b_block, c_block, step_block, keep_block):
    block_len = x_block.shape[0]
    cumul_keep = jnp.cumsum(keep_block, axis=1)
    lower_mask = lax.broadcasted_iota(jnp.int32, (block_len, block_len), 0) >= lax.broadcasted_iota(
        jnp.int32, (block_len, block_len), 1
    )
    inner_prod = jnp.einsum("is,js->ij", c_block, b_block, preferred_element_type=jnp.float32)
    spread = cumul_keep[:, :, None] - cumul_keep[:, None, :]
    decay_mask = jnp.where(lower_mask[None], jnp.exp(jnp.where(lower_mask[None], spread, 0.0)), 0.0)
    mixing = (decay_mask * inner_prod[None] * step_block[:, None, :]).astype(jnp.bfloat16)
    intra_part = jnp.einsum("hij,jhp->ihp", mixing, x_block, preferred_element_type=jnp.float32)
    tail_weight = jnp.exp(cumul_keep[:, -1:] - cumul_keep) * step_block
    weighted = (tail_weight.T[:, :, None] * x_block.astype(jnp.float32)).astype(jnp.bfloat16)
    stretch_state = jnp.einsum("jhp,js->hps", weighted, b_block, preferred_element_type=jnp.float32)
    return (intra_part, stretch_state, cumul_keep)


def combine(earlier, later):
    return (earlier[0] * jnp.exp(later[1])[:, None, None] + later[0], earlier[1] + later[1])


def exclusive_scan(state, decay, axis):
    count = lax.axis_size(axis)
    window = (state, decay)
    before = (jnp.zeros_like(state), jnp.zeros_like(decay))
    shift = 1
    while shift < count:
        sent_state = passed_along(window[0].astype(jnp.bfloat16), axis, shift)
        sent_decay = passed_along(window[1], axis, shift)
        received = (sent_state.astype(jnp.float32), sent_decay)
        before = combine(received, before)
        if shift * 2 < count:
            window = combine(received, window)
        shift *= 2
    return before[0]


def read_state(c_block, state_in):
    state_high = state_in.astype(jnp.bfloat16)
    state_low = (state_in - state_high.astype(jnp.float32)).astype(jnp.bfloat16)
    high_part = jnp.einsum("is,hps->ihp", c_block, state_high, preferred_element_type=jnp.float32)
    low_part = jnp.einsum("is,hps->ihp", c_block, state_low, preferred_element_type=jnp.float32)
    return high_part + low_part


def local(
    x_in,
    z_gate,
    bc_in,
    step_size,
    log_keep,
    skip_gain,
    conv_x,
    conv_bc,
    norm_gain,
    seg_ends,
    pool_query,
    pool_start,
    pool_stop,
):
    tok_rows = x_in.shape[0]
    channels = x_in.shape[1]
    heads_local = step_size.shape[0]
    head_width = channels // heads_local
    state_width = bc_in.shape[1] // 2
    rim_rows = conv_x.shape[0] - 1
    seq_count = lax.axis_size("seq")
    pools_local = pool_query.shape[0]
    bounds = jnp.stack([pool_start, pool_stop], axis=1)
    bounds_split = jnp.concatenate([bounds // 64, bounds % 64], axis=1).astype(jnp.bfloat16)
    query_rows = jnp.concatenate([pool_query, bounds_split], axis=1)
    query_rows = jnp.broadcast_to(query_rows[None], (seq_count,) + query_rows.shape)
    query_rows = lax.all_to_all(
        query_rows.reshape(seq_count * pools_local, -1), "seq", 0, 0, tiled=True
    )
    queries_all = query_rows[:, :channels]
    bounds_all = query_rows[:, channels:].astype(jnp.int32)
    start_all = bounds_all[:, 0] * 64 + bounds_all[:, 2]
    stop_all = bounds_all[:, 1] * 64 + bounds_all[:, 3]
    edge_rows = jnp.concatenate([x_in[tok_rows - rim_rows :], bc_in[tok_rows - rim_rows :]], axis=1)
    before = passed_along(edge_rows, "seq", 1)
    x_conv = causal_conv(before[:, :channels], x_in, conv_x)
    bc_conv = causal_conv(before[:, channels:], bc_in, conv_bc)
    b_mat = bc_conv[:, :state_width]
    c_mat = bc_conv[:, state_width:]
    x_heads = x_conv.reshape(tok_rows, heads_local, head_width)
    stretch_count = tok_rows // STRETCH
    entry_state = jnp.zeros((heads_local, head_width, state_width), jnp.float32)
    decay_total = jnp.zeros((heads_local,), jnp.float32)
    saved_parts = []
    for block_index in range(stretch_count):
        first_row = block_index * STRETCH
        last_row = first_row + STRETCH
        intra_part, stretch_state, cumul_keep = stretch_local(
            x_heads[first_row:last_row],
            b_mat[first_row:last_row],
            c_mat[first_row:last_row],
            step_size[:, first_row:last_row],
            log_keep[:, first_row:last_row],
        )
        saved_parts.append((intra_part, cumul_keep, entry_state, decay_total))
        entry_state = jnp.exp(cumul_keep[:, -1])[:, None, None] * entry_state + stretch_state
        decay_total = decay_total + cumul_keep[:, -1]
    incoming = exclusive_scan(entry_state, decay_total, "seq")
    pieces_out = []
    for block_index in range(stretch_count):
        intra_part, cumul_keep, entry_part, decay_part = saved_parts[block_index]
        first_row = block_index * STRETCH
        state_in = entry_part + jnp.exp(decay_part)[:, None, None] * incoming
        from_state = read_state(c_mat[first_row : first_row + STRETCH], state_in)
        pieces_out.append(intra_part + jnp.exp(cumul_keep).T[:, :, None] * from_state)
    ssd_out = jnp.concatenate(pieces_out, axis=0) + skip_gain[None, :, None] * x_heads.astype(
        jnp.float32
    )
    gated = ssd_out.reshape(tok_rows, channels) * silu_act(z_gate.astype(jnp.float32))
    square_sum = lax.psum(jnp.sum(gated * gated, axis=1), "tensor")
    width_all = channels * lax.axis_size("tensor")
    mixed_seq = (
        gated * lax.rsqrt(square_sum / width_all + EPSILON)[:, None] * norm_gain[None, :]
    ).astype(jnp.bfloat16)
    local_ends = seg_ends - lax.axis_index("seq") * tok_rows
    summaries = jnp.take(mixed_seq, local_ends, axis=0)
    pool_heads_local = POOL_HEADS // lax.axis_size("tensor")
    pool_width = channels // pool_heads_local
    scale_factor = 1.0 / math.sqrt(pool_width)
    pools_all = queries_all.shape[0]
    segs_local = summaries.shape[0]
    queries = queries_all.reshape(pools_all, pool_heads_local, pool_width)
    seg_index = lax.axis_index("seq") * segs_local + lax.iota(jnp.int32, segs_local)
    inside = (seg_index[None, :] >= start_all[:, None]) & (seg_index[None, :] < stop_all[:, None])
    keys_block = summaries.reshape(segs_local, pool_heads_local, pool_width)
    logits = (
        jnp.einsum("pad,rad->apr", queries, keys_block, preferred_element_type=jnp.float32)
        * scale_factor
    )
    logits = jnp.where(inside[None], logits, MASKED)
    peak = jnp.max(logits, axis=2).astype(jnp.bfloat16).astype(jnp.float32)
    expo = jnp.where(inside[None], jnp.exp(logits - peak[:, :, None]), 0.0)
    denom = jnp.sum(expo, axis=2)
    numer = jnp.einsum(
        "apr,rad->pad", expo.astype(jnp.bfloat16), keys_block, preferred_element_type=jnp.float32
    )
    denom_high = denom.astype(jnp.bfloat16)
    denom_low = (denom - denom_high.astype(jnp.float32)).astype(jnp.bfloat16)
    parts = jnp.concatenate(
        [
            numer.reshape(pools_all, channels).astype(jnp.bfloat16),
            peak.T.astype(jnp.bfloat16),
            denom_high.T,
            denom_low.T,
        ],
        axis=1,
    )
    parts = lax.all_to_all(parts, "seq", 0, 0, tiled=True).astype(jnp.float32)
    parts = parts.reshape(seq_count, pools_local, channels + 3 * pool_heads_local)
    numer_parts = parts[:, :, :channels].reshape(
        seq_count, pools_local, pool_heads_local, pool_width
    )
    stats_parts = parts[:, :, channels:].reshape(seq_count, pools_local, 3, pool_heads_local)
    peak_parts = stats_parts[:, :, 0]
    denom_parts = stats_parts[:, :, 1] + stats_parts[:, :, 2]
    peak_all = jnp.max(peak_parts, axis=0)
    rescale = jnp.exp(peak_parts - peak_all[None])
    denom_all = jnp.sum(rescale * denom_parts, axis=0)
    numer_all = jnp.sum(rescale[:, :, :, None] * numer_parts, axis=0)
    pooled = (numer_all / denom_all[:, :, None]).reshape(pools_local, channels)
    return (mixed_seq, pooled)


def solution(mesh):
    in_specs = (
        P(("groups", "seq"), "tensor"),
        P(("groups", "seq"), "tensor"),
        P(("groups", "seq"), None),
        P("tensor", ("groups", "seq")),
        P("tensor", ("groups", "seq")),
        P("tensor"),
        P(None, "tensor"),
        P(),
        P("tensor"),
        P(("groups", "seq")),
        P(("groups", "seq"), "tensor"),
        P(("groups", "seq")),
        P(("groups", "seq")),
    )
    out_specs = (P(("groups", "seq"), "tensor"), P(("groups", "seq"), "tensor"))
    return jax.shard_map(local, mesh=mesh, in_specs=in_specs, out_specs=out_specs, check_vma=False)
```

```python
import math

import jax
import jax.numpy as jnp
from jax import lax
from jax.sharding import PartitionSpec as P

STRETCH = 256
POOL_HEADS = 32


EPSILON = 1e-05
MASKED = -1e30


def passed_along(value, axis, steps):
    count = lax.axis_size(axis)
    leading, last = (max(0, -steps), min(count, count - steps))
    return lax.ppermute(value, axis, [(source, source + steps) for source in range(leading, last)])


def silu_act(values):
    return values / (1.0 + jnp.exp(-values))


def causal_conv(before, current, weights):
    kernel_width = weights.shape[0]
    length = current.shape[0]
    padded = jnp.concatenate([before, current], axis=0)
    summed = jnp.zeros(current.shape, jnp.float32)
    for offset in range(kernel_width):
        summed = summed + padded[offset : offset + length].astype(jnp.float32) * weights[
            offset
        ].astype(jnp.float32)
    return silu_act(summed).astype(jnp.bfloat16)


def stretch_local(x_block, b_block, c_block, step_block, keep_block):
    block_len = x_block.shape[0]
    cumul_keep = jnp.cumsum(keep_block, axis=1)
    lower_mask = lax.broadcasted_iota(jnp.int32, (block_len, block_len), 0) >= lax.broadcasted_iota(
        jnp.int32, (block_len, block_len), 1
    )
    inner_prod = jnp.einsum("is,js->ij", c_block, b_block, preferred_element_type=jnp.float32)
    spread = cumul_keep[:, :, None] - cumul_keep[:, None, :]
    decay_mask = jnp.where(lower_mask[None], jnp.exp(jnp.where(lower_mask[None], spread, 0.0)), 0.0)
    mixing = (decay_mask * inner_prod[None] * step_block[:, None, :]).astype(jnp.bfloat16)
    intra_part = jnp.einsum("hij,jhp->ihp", mixing, x_block, preferred_element_type=jnp.float32)
    tail_weight = jnp.exp(cumul_keep[:, -1:] - cumul_keep) * step_block
    weighted = (tail_weight.T[:, :, None] * x_block.astype(jnp.float32)).astype(jnp.bfloat16)
    stretch_state = jnp.einsum("jhp,js->hps", weighted, b_block, preferred_element_type=jnp.float32)
    return (intra_part, stretch_state, cumul_keep)


def combine(earlier, later):
    return (earlier[0] * jnp.exp(later[1])[:, None, None] + later[0], earlier[1] + later[1])


def exclusive_scan(state, decay, axis):
    count = lax.axis_size(axis)
    window = (state, decay)
    before = (jnp.zeros_like(state), jnp.zeros_like(decay))
    shift = 1
    while shift < count:
        sent_state = passed_along(window[0].astype(jnp.bfloat16), axis, shift)
        sent_decay = passed_along(window[1], axis, shift)
        received = (sent_state.astype(jnp.float32), sent_decay)
        before = combine(received, before)
        if shift * 2 < count:
            window = combine(received, window)
        shift *= 2
    return before[0]


def read_state(c_block, state_in):
    flat = state_in.reshape(-1, state_in.shape[-1])
    state_high = flat.astype(jnp.bfloat16)
    state_low = (flat - state_high.astype(jnp.float32)).astype(jnp.bfloat16)
    high_part = jnp.einsum("is,cs->ic", c_block, state_high, preferred_element_type=jnp.float32)
    low_part = jnp.einsum("is,cs->ic", c_block, state_low, preferred_element_type=jnp.float32)
    return (high_part + low_part).reshape(c_block.shape[0], state_in.shape[0], state_in.shape[1])


def local(
    x_in,
    z_gate,
    bc_in,
    step_size,
    log_keep,
    skip_gain,
    conv_x,
    conv_bc,
    norm_gain,
    seg_ends,
    pool_query,
    pool_start,
    pool_stop,
):
    tok_rows = x_in.shape[0]
    channels = x_in.shape[1]
    heads_local = step_size.shape[0]
    head_width = channels // heads_local
    state_width = bc_in.shape[1] // 2
    rim_rows = conv_x.shape[0] - 1
    seq_count = lax.axis_size("seq")
    pools_local = pool_query.shape[0]
    bounds = jnp.stack([pool_start, pool_stop], axis=1)
    bounds_split = jnp.concatenate([bounds // 64, bounds % 64], axis=1).astype(jnp.bfloat16)
    query_rows = jnp.concatenate([pool_query, bounds_split], axis=1)
    edge_rows = jnp.concatenate([x_in[tok_rows - rim_rows :], bc_in[tok_rows - rim_rows :]], axis=1)
    query_width = query_rows.shape[1]
    payload = jnp.concatenate([query_rows.reshape(-1), edge_rows.reshape(-1)])
    payload = jnp.broadcast_to(payload[None], (seq_count,) + payload.shape)
    payload = lax.all_to_all(payload, "seq", 0, 0, tiled=True)
    query_size = pools_local * query_width
    query_rows = payload[:, :query_size].reshape(seq_count * pools_local, query_width)
    queries_all = query_rows[:, :channels]
    bounds_all = query_rows[:, channels:].astype(jnp.int32)
    start_all = bounds_all[:, 0] * 64 + bounds_all[:, 2]
    stop_all = bounds_all[:, 1] * 64 + bounds_all[:, 3]
    place = lax.axis_index("seq")
    edges_all = payload[:, query_size:].reshape(seq_count, rim_rows, edge_rows.shape[1])
    before = lax.dynamic_index_in_dim(edges_all, jnp.maximum(place - 1, 0), 0, False)
    before = jnp.where(place > 0, before, jnp.zeros_like(before))
    x_conv = causal_conv(before[:, :channels], x_in, conv_x)
    bc_conv = causal_conv(before[:, channels:], bc_in, conv_bc)
    b_mat = bc_conv[:, :state_width]
    c_mat = bc_conv[:, state_width:]
    x_heads = x_conv.reshape(tok_rows, heads_local, head_width)
    stretch_count = tok_rows // STRETCH
    entry_state = jnp.zeros((heads_local, head_width, state_width), jnp.float32)
    decay_total = jnp.zeros((heads_local,), jnp.float32)
    saved_parts = []
    for block_index in range(stretch_count):
        first_row = block_index * STRETCH
        last_row = first_row + STRETCH
        intra_part, stretch_state, cumul_keep = stretch_local(
            x_heads[first_row:last_row],
            b_mat[first_row:last_row],
            c_mat[first_row:last_row],
            step_size[:, first_row:last_row],
            log_keep[:, first_row:last_row],
        )
        saved_parts.append((intra_part, cumul_keep, entry_state, decay_total))
        entry_state = jnp.exp(cumul_keep[:, -1])[:, None, None] * entry_state + stretch_state
        decay_total = decay_total + cumul_keep[:, -1]
    base = jnp.concatenate([part[0] for part in saved_parts], axis=0) + skip_gain[
        None, :, None
    ] * x_heads.astype(jnp.float32)
    base = lax.optimization_barrier(base.reshape(tok_rows, channels))
    incoming = exclusive_scan(entry_state, decay_total, "seq")
    pieces_out = []
    for block_index in range(stretch_count):
        intra_part, cumul_keep, entry_part, decay_part = saved_parts[block_index]
        first_row = block_index * STRETCH
        state_in = entry_part + jnp.exp(decay_part)[:, None, None] * incoming
        from_state = read_state(c_mat[first_row : first_row + STRETCH], state_in)
        pieces_out.append(
            (jnp.exp(cumul_keep).T[:, :, None] * from_state).reshape(STRETCH, channels)
        )
    ssd_out = jnp.concatenate(pieces_out, axis=0) + base
    gated = ssd_out.reshape(tok_rows, channels) * silu_act(z_gate.astype(jnp.float32))
    square_sum = lax.psum(jnp.sum(gated * gated, axis=1), "tensor")
    width_all = channels * lax.axis_size("tensor")
    mixed_seq = (
        gated * lax.rsqrt(square_sum / width_all + EPSILON)[:, None] * norm_gain[None, :]
    ).astype(jnp.bfloat16)
    local_ends = seg_ends - lax.axis_index("seq") * tok_rows
    summaries = jnp.take(mixed_seq, local_ends, axis=0)
    pool_heads_local = POOL_HEADS // lax.axis_size("tensor")
    pool_width = channels // pool_heads_local
    scale_factor = 1.0 / math.sqrt(pool_width)
    pools_all = queries_all.shape[0]
    segs_local = summaries.shape[0]
    queries = queries_all.reshape(pools_all, pool_heads_local, pool_width)
    seg_index = lax.axis_index("seq") * segs_local + lax.iota(jnp.int32, segs_local)
    inside = (seg_index[None, :] >= start_all[:, None]) & (seg_index[None, :] < stop_all[:, None])
    keys_block = summaries.reshape(segs_local, pool_heads_local, pool_width)
    logits = (
        jnp.einsum("pad,rad->apr", queries, keys_block, preferred_element_type=jnp.float32)
        * scale_factor
    )
    logits = jnp.where(inside[None], logits, MASKED)
    peak = jnp.max(logits, axis=2).astype(jnp.bfloat16).astype(jnp.float32)
    expo = jnp.where(inside[None], jnp.exp(logits - peak[:, :, None]), 0.0)
    denom = jnp.sum(expo, axis=2)
    numer = jnp.einsum(
        "apr,rad->pad", expo.astype(jnp.bfloat16), keys_block, preferred_element_type=jnp.float32
    )
    denom_high = denom.astype(jnp.bfloat16)
    denom_low = (denom - denom_high.astype(jnp.float32)).astype(jnp.bfloat16)
    parts = jnp.concatenate(
        [
            numer.reshape(pools_all, channels).astype(jnp.bfloat16),
            peak.T.astype(jnp.bfloat16),
            denom_high.T,
            denom_low.T,
        ],
        axis=1,
    )
    parts = lax.all_to_all(parts, "seq", 0, 0, tiled=True).astype(jnp.float32)
    parts = parts.reshape(seq_count, pools_local, channels + 3 * pool_heads_local)
    numer_parts = parts[:, :, :channels].reshape(
        seq_count, pools_local, pool_heads_local, pool_width
    )
    stats_parts = parts[:, :, channels:].reshape(seq_count, pools_local, 3, pool_heads_local)
    peak_parts = stats_parts[:, :, 0]
    denom_parts = stats_parts[:, :, 1] + stats_parts[:, :, 2]
    peak_all = jnp.max(peak_parts, axis=0)
    rescale = jnp.exp(peak_parts - peak_all[None])
    denom_all = jnp.sum(rescale * denom_parts, axis=0)
    numer_all = jnp.sum(rescale[:, :, :, None] * numer_parts, axis=0)
    pooled = (numer_all / denom_all[:, :, None]).reshape(pools_local, channels)
    return (mixed_seq, pooled)


def solution(mesh):
    in_specs = (
        P(("groups", "seq"), "tensor"),
        P(("groups", "seq"), "tensor"),
        P(("groups", "seq"), None),
        P("tensor", ("groups", "seq")),
        P("tensor", ("groups", "seq")),
        P("tensor"),
        P(None, "tensor"),
        P(),
        P("tensor"),
        P(("groups", "seq")),
        P(("groups", "seq"), "tensor"),
        P(("groups", "seq")),
        P(("groups", "seq")),
    )
    out_specs = (P(("groups", "seq"), "tensor"), P(("groups", "seq"), "tensor"))
    return jax.shard_map(local, mesh=mesh, in_specs=in_specs, out_specs=out_specs, check_vma=False)
```

```python
import math

import jax
import jax.numpy as jnp
from jax import lax
from jax.sharding import PartitionSpec as P

STRETCH = 256
POOL_HEADS = 32


EPSILON = 1e-05
MASKED = -1e30


def passed_along(value, axis, steps):
    count = lax.axis_size(axis)
    leading, last = (max(0, -steps), min(count, count - steps))
    return lax.ppermute(value, axis, [(source, source + steps) for source in range(leading, last)])


def silu_act(values):
    return values / (1.0 + jnp.exp(-values))


def causal_conv(before, current, weights):
    kernel_width = weights.shape[0]
    length = current.shape[0]
    padded = jnp.concatenate([before, current], axis=0)
    summed = jnp.zeros(current.shape, jnp.float32)
    for offset in range(kernel_width):
        summed = summed + padded[offset : offset + length].astype(jnp.float32) * weights[
            offset
        ].astype(jnp.float32)
    return silu_act(summed).astype(jnp.bfloat16)


def stretch_local(x_block, b_block, c_block, step_block, keep_block):
    block_len = x_block.shape[0]
    cumul_keep = jnp.cumsum(keep_block, axis=1)
    lower_mask = lax.broadcasted_iota(jnp.int32, (block_len, block_len), 0) >= lax.broadcasted_iota(
        jnp.int32, (block_len, block_len), 1
    )
    inner_prod = jnp.einsum("is,js->ij", c_block, b_block, preferred_element_type=jnp.float32)
    spread = cumul_keep[:, :, None] - cumul_keep[:, None, :]
    decay_mask = jnp.where(lower_mask[None], jnp.exp(jnp.where(lower_mask[None], spread, 0.0)), 0.0)
    mixing = (decay_mask * inner_prod[None] * step_block[:, None, :]).astype(jnp.bfloat16)
    intra_part = jnp.einsum("hij,jhp->ihp", mixing, x_block, preferred_element_type=jnp.float32)
    tail_weight = jnp.exp(cumul_keep[:, -1:] - cumul_keep) * step_block
    weighted = (tail_weight.T[:, :, None] * x_block.astype(jnp.float32)).astype(jnp.bfloat16)
    stretch_state = jnp.einsum("jhp,js->hps", weighted, b_block, preferred_element_type=jnp.float32)
    return (intra_part, stretch_state, cumul_keep)


def combine(earlier, later):
    return (earlier[0] * jnp.exp(later[1])[:, None, None] + later[0], earlier[1] + later[1])


def exclusive_scan(state, decay, axis, rider):
    count = lax.axis_size(axis)
    window = (state, decay)
    before = (jnp.zeros_like(state), jnp.zeros_like(decay))
    shift = 1
    while shift < count:
        sent_state = passed_along(window[0].astype(jnp.bfloat16), axis, shift)
        sent_decay = passed_along(window[1], axis, shift)
        if shift == 1:
            sent_state, rider = lax.optimization_barrier((sent_state, rider))
        received = (sent_state.astype(jnp.float32), sent_decay)
        before = combine(received, before)
        if shift * 2 < count:
            window = combine(received, window)
        shift *= 2
    return before[0], rider


def read_state(c_block, state_in):
    flat = state_in.reshape(-1, state_in.shape[-1])
    state_high = flat.astype(jnp.bfloat16)
    state_low = (flat - state_high.astype(jnp.float32)).astype(jnp.bfloat16)
    high_part = jnp.einsum("is,cs->ic", c_block, state_high, preferred_element_type=jnp.float32)
    low_part = jnp.einsum("is,cs->ic", c_block, state_low, preferred_element_type=jnp.float32)
    return (high_part + low_part).reshape(c_block.shape[0], state_in.shape[0], state_in.shape[1])


def local(
    x_in,
    z_gate,
    bc_in,
    step_size,
    log_keep,
    skip_gain,
    conv_x,
    conv_bc,
    norm_gain,
    seg_ends,
    pool_query,
    pool_start,
    pool_stop,
):
    tok_rows = x_in.shape[0]
    channels = x_in.shape[1]
    heads_local = step_size.shape[0]
    head_width = channels // heads_local
    state_width = bc_in.shape[1] // 2
    rim_rows = conv_x.shape[0] - 1
    seq_count = lax.axis_size("seq")
    pools_local = pool_query.shape[0]
    bounds = jnp.stack([pool_start, pool_stop], axis=1)
    bounds_split = jnp.concatenate([bounds // 64, bounds % 64], axis=1).astype(jnp.bfloat16)
    query_rows = jnp.concatenate([pool_query, bounds_split], axis=1)
    edge_rows = jnp.concatenate([x_in[tok_rows - rim_rows :], bc_in[tok_rows - rim_rows :]], axis=1)
    query_width = query_rows.shape[1]
    payload = jnp.concatenate([query_rows.reshape(-1), edge_rows.reshape(-1)])
    payload = jnp.broadcast_to(payload[None], (seq_count,) + payload.shape)
    payload = lax.all_to_all(payload, "seq", 0, 0, tiled=True)
    query_size = pools_local * query_width
    query_rows = payload[:, :query_size].reshape(seq_count * pools_local, query_width)
    queries_all = query_rows[:, :channels]
    bounds_all = query_rows[:, channels:].astype(jnp.int32)
    start_all = bounds_all[:, 0] * 64 + bounds_all[:, 2]
    stop_all = bounds_all[:, 1] * 64 + bounds_all[:, 3]
    place = lax.axis_index("seq")
    edges_all = payload[:, query_size:].reshape(seq_count, rim_rows, edge_rows.shape[1])
    before = lax.dynamic_index_in_dim(edges_all, jnp.maximum(place - 1, 0), 0, False)
    before = jnp.where(place > 0, before, jnp.zeros_like(before))
    x_conv = causal_conv(before[:, :channels], x_in, conv_x)
    bc_conv = causal_conv(before[:, channels:], bc_in, conv_bc)
    b_mat = bc_conv[:, :state_width]
    c_mat = bc_conv[:, state_width:]
    x_heads = x_conv.reshape(tok_rows, heads_local, head_width)
    stretch_count = tok_rows // STRETCH
    entry_state = jnp.zeros((heads_local, head_width, state_width), jnp.float32)
    decay_total = jnp.zeros((heads_local,), jnp.float32)
    saved_parts = []
    for block_index in range(stretch_count):
        first_row = block_index * STRETCH
        last_row = first_row + STRETCH
        cumul_keep = jnp.cumsum(log_keep[:, first_row:last_row], axis=1)
        step_block = step_size[:, first_row:last_row]
        tail_weight = jnp.exp(cumul_keep[:, -1:] - cumul_keep) * step_block
        weighted = (
            tail_weight.T[:, :, None] * x_heads[first_row:last_row].astype(jnp.float32)
        ).astype(jnp.bfloat16)
        stretch_state = jnp.einsum(
            "jhp,js->hps", weighted, b_mat[first_row:last_row], preferred_element_type=jnp.float32
        )
        saved_parts.append((cumul_keep, entry_state, decay_total))
        entry_state = jnp.exp(cumul_keep[:, -1])[:, None, None] * entry_state + stretch_state
        decay_total = decay_total + cumul_keep[:, -1]
    incoming, rider = exclusive_scan(
        entry_state, decay_total, "seq", (x_heads, b_mat, c_mat, step_size, log_keep)
    )
    x_late, b_late, c_late, step_late, keep_late = rider
    intra_parts = []
    for block_index in range(stretch_count):
        first_row = block_index * STRETCH
        last_row = first_row + STRETCH
        intra_part, unused_state, unused_cumul = stretch_local(
            x_late[first_row:last_row],
            b_late[first_row:last_row],
            c_late[first_row:last_row],
            step_late[:, first_row:last_row],
            keep_late[:, first_row:last_row],
        )
        intra_parts.append(intra_part)
    base = jnp.concatenate(intra_parts, axis=0) + skip_gain[None, :, None] * x_late.astype(
        jnp.float32
    )
    base = lax.optimization_barrier(base.reshape(tok_rows, channels))
    pieces_out = []
    for block_index in range(stretch_count):
        cumul_keep, entry_part, decay_part = saved_parts[block_index]
        first_row = block_index * STRETCH
        state_in = entry_part + jnp.exp(decay_part)[:, None, None] * incoming
        from_state = read_state(c_mat[first_row : first_row + STRETCH], state_in)
        pieces_out.append(
            (jnp.exp(cumul_keep).T[:, :, None] * from_state).reshape(STRETCH, channels)
        )
    ssd_out = jnp.concatenate(pieces_out, axis=0) + base
    gated = ssd_out.reshape(tok_rows, channels) * silu_act(z_gate.astype(jnp.float32))
    square_sum = lax.psum(jnp.sum(gated * gated, axis=1), "tensor")
    width_all = channels * lax.axis_size("tensor")
    mixed_seq = (
        gated * lax.rsqrt(square_sum / width_all + EPSILON)[:, None] * norm_gain[None, :]
    ).astype(jnp.bfloat16)
    local_ends = seg_ends - lax.axis_index("seq") * tok_rows
    summaries = jnp.take(mixed_seq, local_ends, axis=0)
    pool_heads_local = POOL_HEADS // lax.axis_size("tensor")
    pool_width = channels // pool_heads_local
    scale_factor = 1.0 / math.sqrt(pool_width)
    pools_all = queries_all.shape[0]
    segs_local = summaries.shape[0]
    queries = queries_all.reshape(pools_all, pool_heads_local, pool_width)
    seg_index = lax.axis_index("seq") * segs_local + lax.iota(jnp.int32, segs_local)
    inside = (seg_index[None, :] >= start_all[:, None]) & (seg_index[None, :] < stop_all[:, None])
    keys_block = summaries.reshape(segs_local, pool_heads_local, pool_width)
    logits = (
        jnp.einsum("pad,rad->apr", queries, keys_block, preferred_element_type=jnp.float32)
        * scale_factor
    )
    logits = jnp.where(inside[None], logits, MASKED)
    peak = jnp.max(logits, axis=2).astype(jnp.bfloat16).astype(jnp.float32)
    expo = jnp.where(inside[None], jnp.exp(logits - peak[:, :, None]), 0.0)
    denom = jnp.sum(expo, axis=2)
    numer = jnp.einsum(
        "apr,rad->pad", expo.astype(jnp.bfloat16), keys_block, preferred_element_type=jnp.float32
    )
    denom_high = denom.astype(jnp.bfloat16)
    denom_low = (denom - denom_high.astype(jnp.float32)).astype(jnp.bfloat16)
    parts = jnp.concatenate(
        [
            numer.reshape(pools_all, channels).astype(jnp.bfloat16),
            peak.T.astype(jnp.bfloat16),
            denom_high.T,
            denom_low.T,
        ],
        axis=1,
    )
    parts = lax.all_to_all(parts, "seq", 0, 0, tiled=True).astype(jnp.float32)
    parts = parts.reshape(seq_count, pools_local, channels + 3 * pool_heads_local)
    numer_parts = parts[:, :, :channels].reshape(
        seq_count, pools_local, pool_heads_local, pool_width
    )
    stats_parts = parts[:, :, channels:].reshape(seq_count, pools_local, 3, pool_heads_local)
    peak_parts = stats_parts[:, :, 0]
    denom_parts = stats_parts[:, :, 1] + stats_parts[:, :, 2]
    peak_all = jnp.max(peak_parts, axis=0)
    rescale = jnp.exp(peak_parts - peak_all[None])
    denom_all = jnp.sum(rescale * denom_parts, axis=0)
    numer_all = jnp.sum(rescale[:, :, :, None] * numer_parts, axis=0)
    pooled = (numer_all / denom_all[:, :, None]).reshape(pools_local, channels)
    return (mixed_seq, pooled)


def solution(mesh):
    in_specs = (
        P(("groups", "seq"), "tensor"),
        P(("groups", "seq"), "tensor"),
        P(("groups", "seq"), None),
        P("tensor", ("groups", "seq")),
        P("tensor", ("groups", "seq")),
        P("tensor"),
        P(None, "tensor"),
        P(),
        P("tensor"),
        P(("groups", "seq")),
        P(("groups", "seq"), "tensor"),
        P(("groups", "seq")),
        P(("groups", "seq")),
    )
    out_specs = (P(("groups", "seq"), "tensor"), P(("groups", "seq"), "tensor"))
    return jax.shard_map(local, mesh=mesh, in_specs=in_specs, out_specs=out_specs, check_vma=False)
```

```python
import math

import jax
import jax.numpy as jnp
from jax import lax
from jax.sharding import PartitionSpec as P

STRETCH = 256
POOL_HEADS = 32


EPSILON = 1e-05
MASKED = -1e30


def passed_along(value, axis, steps):
    count = lax.axis_size(axis)
    leading, last = (max(0, -steps), min(count, count - steps))
    return lax.ppermute(value, axis, [(source, source + steps) for source in range(leading, last)])


def silu_act(values):
    return values / (1.0 + jnp.exp(-values))


def causal_conv(before, current, weights):
    kernel_width = weights.shape[0]
    length = current.shape[0]
    padded = jnp.concatenate([before, current], axis=0)
    summed = jnp.zeros(current.shape, jnp.float32)
    for offset in range(kernel_width):
        summed = summed + padded[offset : offset + length].astype(jnp.float32) * weights[
            offset
        ].astype(jnp.float32)
    return silu_act(summed).astype(jnp.bfloat16)


def stretch_local(x_block, b_block, c_block, step_block, keep_block):
    block_len = x_block.shape[0]
    cumul_keep = jnp.cumsum(keep_block, axis=1)
    lower_mask = lax.broadcasted_iota(jnp.int32, (block_len, block_len), 0) >= lax.broadcasted_iota(
        jnp.int32, (block_len, block_len), 1
    )
    inner_prod = jnp.einsum("is,js->ij", c_block, b_block, preferred_element_type=jnp.float32)
    spread = cumul_keep[:, :, None] - cumul_keep[:, None, :]
    decay_mask = jnp.where(lower_mask[None], jnp.exp(jnp.where(lower_mask[None], spread, 0.0)), 0.0)
    mixing = (decay_mask * inner_prod[None] * step_block[:, None, :]).astype(jnp.bfloat16)
    intra_part = jnp.einsum("hij,jhp->ihp", mixing, x_block, preferred_element_type=jnp.float32)
    tail_weight = jnp.exp(cumul_keep[:, -1:] - cumul_keep) * step_block
    weighted = (tail_weight.T[:, :, None] * x_block.astype(jnp.float32)).astype(jnp.bfloat16)
    stretch_state = jnp.einsum("jhp,js->hps", weighted, b_block, preferred_element_type=jnp.float32)
    return (intra_part, stretch_state, cumul_keep)


def combine(earlier, later):
    return (earlier[0] * jnp.exp(later[1])[:, None, None] + later[0], earlier[1] + later[1])


def exclusive_scan(state, decay, axis, rider):
    count = lax.axis_size(axis)
    window = (state, decay)
    before = (jnp.zeros_like(state), jnp.zeros_like(decay))
    shift = 1
    while shift < count:
        sent_state = passed_along(window[0].astype(jnp.bfloat16), axis, shift)
        sent_decay = passed_along(window[1], axis, shift)
        if shift == 1:
            sent_state, rider = lax.optimization_barrier((sent_state, rider))
        received = (sent_state.astype(jnp.float32), sent_decay)
        before = combine(received, before)
        if shift * 2 < count:
            window = combine(received, window)
        shift *= 2
    return before[0], rider


def read_state(c_block, state_in):
    flat = state_in.reshape(-1, state_in.shape[-1])
    state_high = flat.astype(jnp.bfloat16)
    state_low = (flat - state_high.astype(jnp.float32)).astype(jnp.bfloat16)
    high_part = jnp.einsum("is,cs->ic", c_block, state_high, preferred_element_type=jnp.float32)
    low_part = jnp.einsum("is,cs->ic", c_block, state_low, preferred_element_type=jnp.float32)
    return (high_part + low_part).reshape(c_block.shape[0], state_in.shape[0], state_in.shape[1])


def local(
    x_in,
    z_gate,
    bc_in,
    step_size,
    log_keep,
    skip_gain,
    conv_x,
    conv_bc,
    norm_gain,
    seg_ends,
    pool_query,
    pool_start,
    pool_stop,
):
    tok_rows = x_in.shape[0]
    channels = x_in.shape[1]
    heads_local = step_size.shape[0]
    head_width = channels // heads_local
    state_width = bc_in.shape[1] // 2
    rim_rows = conv_x.shape[0] - 1
    seq_count = lax.axis_size("seq")
    pools_local = pool_query.shape[0]
    bounds = jnp.stack([pool_start, pool_stop], axis=1)
    bounds_split = jnp.concatenate([bounds // 64, bounds % 64], axis=1).astype(jnp.bfloat16)
    query_rows = jnp.concatenate([pool_query, bounds_split], axis=1)
    query_rows = jnp.broadcast_to(query_rows[None], (seq_count,) + query_rows.shape)
    query_rows = lax.all_to_all(
        query_rows.reshape(seq_count * pools_local, -1), "seq", 0, 0, tiled=True
    )
    queries_all = query_rows[:, :channels]
    bounds_all = query_rows[:, channels:].astype(jnp.int32)
    start_all = bounds_all[:, 0] * 64 + bounds_all[:, 2]
    stop_all = bounds_all[:, 1] * 64 + bounds_all[:, 3]
    edge_rows = jnp.concatenate([x_in[tok_rows - rim_rows :], bc_in[tok_rows - rim_rows :]], axis=1)
    before = passed_along(edge_rows, "seq", 1)
    x_conv = causal_conv(before[:, :channels], x_in, conv_x)
    bc_conv = causal_conv(before[:, channels:], bc_in, conv_bc)
    b_mat = bc_conv[:, :state_width]
    c_mat = bc_conv[:, state_width:]
    x_heads = x_conv.reshape(tok_rows, heads_local, head_width)
    stretch_count = tok_rows // STRETCH
    entry_state = jnp.zeros((heads_local, head_width, state_width), jnp.float32)
    decay_total = jnp.zeros((heads_local,), jnp.float32)
    saved_parts = []
    for block_index in range(stretch_count):
        first_row = block_index * STRETCH
        last_row = first_row + STRETCH
        cumul_keep = jnp.cumsum(log_keep[:, first_row:last_row], axis=1)
        step_block = step_size[:, first_row:last_row]
        tail_weight = jnp.exp(cumul_keep[:, -1:] - cumul_keep) * step_block
        weighted = (
            tail_weight.T[:, :, None] * x_heads[first_row:last_row].astype(jnp.float32)
        ).astype(jnp.bfloat16)
        stretch_state = jnp.einsum(
            "jhp,js->hps", weighted, b_mat[first_row:last_row], preferred_element_type=jnp.float32
        )
        saved_parts.append((cumul_keep, entry_state, decay_total))
        entry_state = jnp.exp(cumul_keep[:, -1])[:, None, None] * entry_state + stretch_state
        decay_total = decay_total + cumul_keep[:, -1]
    incoming, rider = exclusive_scan(
        entry_state, decay_total, "seq", (x_heads, b_mat, c_mat, step_size, log_keep)
    )
    x_late, b_late, c_late, step_late, keep_late = rider
    intra_parts = []
    for block_index in range(stretch_count):
        first_row = block_index * STRETCH
        last_row = first_row + STRETCH
        intra_part, unused_state, unused_cumul = stretch_local(
            x_late[first_row:last_row],
            b_late[first_row:last_row],
            c_late[first_row:last_row],
            step_late[:, first_row:last_row],
            keep_late[:, first_row:last_row],
        )
        intra_parts.append(intra_part)
    base = jnp.concatenate(intra_parts, axis=0) + skip_gain[None, :, None] * x_late.astype(
        jnp.float32
    )
    base = lax.optimization_barrier(base.reshape(tok_rows, channels))
    pieces_out = []
    for block_index in range(stretch_count):
        cumul_keep, entry_part, decay_part = saved_parts[block_index]
        first_row = block_index * STRETCH
        state_in = entry_part + jnp.exp(decay_part)[:, None, None] * incoming
        from_state = read_state(c_mat[first_row : first_row + STRETCH], state_in)
        pieces_out.append(
            (jnp.exp(cumul_keep).T[:, :, None] * from_state).reshape(STRETCH, channels)
        )
    ssd_out = jnp.concatenate(pieces_out, axis=0) + base
    gated = ssd_out.reshape(tok_rows, channels) * silu_act(z_gate.astype(jnp.float32))
    square_sum = lax.psum(jnp.sum(gated * gated, axis=1), "tensor")
    width_all = channels * lax.axis_size("tensor")
    mixed_seq = (
        gated * lax.rsqrt(square_sum / width_all + EPSILON)[:, None] * norm_gain[None, :]
    ).astype(jnp.bfloat16)
    local_ends = seg_ends - lax.axis_index("seq") * tok_rows
    summaries = jnp.take(mixed_seq, local_ends, axis=0)
    pool_heads_local = POOL_HEADS // lax.axis_size("tensor")
    pool_width = channels // pool_heads_local
    scale_factor = 1.0 / math.sqrt(pool_width)
    pools_all = queries_all.shape[0]
    segs_local = summaries.shape[0]
    queries = queries_all.reshape(pools_all, pool_heads_local, pool_width)
    seg_index = lax.axis_index("seq") * segs_local + lax.iota(jnp.int32, segs_local)
    inside = (seg_index[None, :] >= start_all[:, None]) & (seg_index[None, :] < stop_all[:, None])
    keys_block = summaries.reshape(segs_local, pool_heads_local, pool_width)
    logits = (
        jnp.einsum("pad,rad->apr", queries, keys_block, preferred_element_type=jnp.float32)
        * scale_factor
    )
    logits = jnp.where(inside[None], logits, MASKED)
    peak = jnp.max(logits, axis=2).astype(jnp.bfloat16).astype(jnp.float32)
    expo = jnp.where(inside[None], jnp.exp(logits - peak[:, :, None]), 0.0)
    denom = jnp.sum(expo, axis=2)
    numer = jnp.einsum(
        "apr,rad->pad", expo.astype(jnp.bfloat16), keys_block, preferred_element_type=jnp.float32
    )
    denom_high = denom.astype(jnp.bfloat16)
    denom_low = (denom - denom_high.astype(jnp.float32)).astype(jnp.bfloat16)
    parts = jnp.concatenate(
        [
            numer.reshape(pools_all, channels).astype(jnp.bfloat16),
            peak.T.astype(jnp.bfloat16),
            denom_high.T,
            denom_low.T,
        ],
        axis=1,
    )
    parts = lax.all_to_all(parts, "seq", 0, 0, tiled=True).astype(jnp.float32)
    parts = parts.reshape(seq_count, pools_local, channels + 3 * pool_heads_local)
    numer_parts = parts[:, :, :channels].reshape(
        seq_count, pools_local, pool_heads_local, pool_width
    )
    stats_parts = parts[:, :, channels:].reshape(seq_count, pools_local, 3, pool_heads_local)
    peak_parts = stats_parts[:, :, 0]
    denom_parts = stats_parts[:, :, 1] + stats_parts[:, :, 2]
    peak_all = jnp.max(peak_parts, axis=0)
    rescale = jnp.exp(peak_parts - peak_all[None])
    denom_all = jnp.sum(rescale * denom_parts, axis=0)
    numer_all = jnp.sum(rescale[:, :, :, None] * numer_parts, axis=0)
    pooled = (numer_all / denom_all[:, :, None]).reshape(pools_local, channels)
    return (mixed_seq, pooled)


def solution(mesh):
    in_specs = (
        P(("groups", "seq"), "tensor"),
        P(("groups", "seq"), "tensor"),
        P(("groups", "seq"), None),
        P("tensor", ("groups", "seq")),
        P("tensor", ("groups", "seq")),
        P("tensor"),
        P(None, "tensor"),
        P(),
        P("tensor"),
        P(("groups", "seq")),
        P(("groups", "seq"), "tensor"),
        P(("groups", "seq")),
        P(("groups", "seq")),
    )
    out_specs = (P(("groups", "seq"), "tensor"), P(("groups", "seq"), "tensor"))
    return jax.shard_map(local, mesh=mesh, in_specs=in_specs, out_specs=out_specs, check_vma=False)
```

```python
import math

import jax
import jax.numpy as jnp
from jax import lax
from jax.sharding import PartitionSpec as P

STRETCH = 256
POOL_HEADS = 32


EPSILON = 1e-05
MASKED = -1e30


def passed_along(value, axis, steps):
    count = lax.axis_size(axis)
    leading, last = (max(0, -steps), min(count, count - steps))
    return lax.ppermute(value, axis, [(source, source + steps) for source in range(leading, last)])


def silu_act(values):
    return values / (1.0 + jnp.exp(-values))


def causal_conv(before, current, weights):
    kernel_width = weights.shape[0]
    length = current.shape[0]
    padded = jnp.concatenate([before, current], axis=0)
    summed = jnp.zeros(current.shape, jnp.float32)
    for offset in range(kernel_width):
        summed = summed + padded[offset : offset + length].astype(jnp.float32) * weights[
            offset
        ].astype(jnp.float32)
    return silu_act(summed).astype(jnp.bfloat16)


def stretch_local(x_block, b_block, c_block, step_block, keep_block):
    block_len = x_block.shape[0]
    cumul_keep = jnp.cumsum(keep_block, axis=1)
    lower_mask = lax.broadcasted_iota(jnp.int32, (block_len, block_len), 0) >= lax.broadcasted_iota(
        jnp.int32, (block_len, block_len), 1
    )
    inner_prod = jnp.einsum("is,js->ij", c_block, b_block, preferred_element_type=jnp.float32)
    spread = cumul_keep[:, :, None] - cumul_keep[:, None, :]
    decay_mask = jnp.where(lower_mask[None], jnp.exp(jnp.where(lower_mask[None], spread, 0.0)), 0.0)
    mixing = (decay_mask * inner_prod[None] * step_block[:, None, :]).astype(jnp.bfloat16)
    intra_part = jnp.einsum("hij,jhp->ihp", mixing, x_block, preferred_element_type=jnp.float32)
    tail_weight = jnp.exp(cumul_keep[:, -1:] - cumul_keep) * step_block
    weighted = (tail_weight.T[:, :, None] * x_block.astype(jnp.float32)).astype(jnp.bfloat16)
    stretch_state = jnp.einsum("jhp,js->hps", weighted, b_block, preferred_element_type=jnp.float32)
    return (intra_part, stretch_state, cumul_keep)


def combine(earlier, later):
    return (earlier[0] * jnp.exp(later[1])[:, None, None] + later[0], earlier[1] + later[1])


def exclusive_scan(state, decay, axis):
    count = lax.axis_size(axis)
    heads, rows, cols = state.shape
    window = (state, decay)
    before = (jnp.zeros_like(state), jnp.zeros_like(decay))
    shift = 1
    while shift < count:
        decay_high = window[1].astype(jnp.bfloat16)
        decay_low = (window[1] - decay_high.astype(jnp.float32)).astype(jnp.bfloat16)
        decay_rows = jnp.zeros((1, rows, cols), jnp.bfloat16)
        decay_rows = decay_rows.at[0, 0, :heads].set(decay_high).at[0, 1, :heads].set(decay_low)
        sent = jnp.concatenate([window[0].astype(jnp.bfloat16), decay_rows], axis=0)
        sent = passed_along(sent, axis, shift).astype(jnp.float32)
        received = (sent[:heads], sent[heads, 0, :heads] + sent[heads, 1, :heads])
        before = combine(received, before)
        if shift * 2 < count:
            window = combine(received, window)
        shift *= 2
    return before[0]


def read_state(c_block, state_in):
    state_high = state_in.astype(jnp.bfloat16)
    state_low = (state_in - state_high.astype(jnp.float32)).astype(jnp.bfloat16)
    high_part = jnp.einsum("is,hps->ihp", c_block, state_high, preferred_element_type=jnp.float32)
    low_part = jnp.einsum("is,hps->ihp", c_block, state_low, preferred_element_type=jnp.float32)
    return high_part + low_part


def local(
    x_in,
    z_gate,
    bc_in,
    step_size,
    log_keep,
    skip_gain,
    conv_x,
    conv_bc,
    norm_gain,
    seg_ends,
    pool_query,
    pool_start,
    pool_stop,
):
    tok_rows = x_in.shape[0]
    channels = x_in.shape[1]
    heads_local = step_size.shape[0]
    head_width = channels // heads_local
    state_width = bc_in.shape[1] // 2
    rim_rows = conv_x.shape[0] - 1
    seq_count = lax.axis_size("seq")
    pools_local = pool_query.shape[0]
    bounds = jnp.stack([pool_start, pool_stop], axis=1)
    bounds_split = jnp.concatenate([bounds // 64, bounds % 64], axis=1).astype(jnp.bfloat16)
    query_rows = jnp.concatenate([pool_query, bounds_split], axis=1)
    query_rows = jnp.broadcast_to(query_rows[None], (seq_count,) + query_rows.shape)
    query_rows = lax.all_to_all(
        query_rows.reshape(seq_count * pools_local, -1), "seq", 0, 0, tiled=True
    )
    queries_all = query_rows[:, :channels]
    bounds_all = query_rows[:, channels:].astype(jnp.int32)
    start_all = bounds_all[:, 0] * 64 + bounds_all[:, 2]
    stop_all = bounds_all[:, 1] * 64 + bounds_all[:, 3]
    edge_rows = jnp.concatenate([x_in[tok_rows - rim_rows :], bc_in[tok_rows - rim_rows :]], axis=1)
    before = passed_along(edge_rows, "seq", 1)
    x_conv = causal_conv(before[:, :channels], x_in, conv_x)
    bc_conv = causal_conv(before[:, channels:], bc_in, conv_bc)
    b_mat = bc_conv[:, :state_width]
    c_mat = bc_conv[:, state_width:]
    x_heads = x_conv.reshape(tok_rows, heads_local, head_width)
    stretch_count = tok_rows // STRETCH
    entry_state = jnp.zeros((heads_local, head_width, state_width), jnp.float32)
    decay_total = jnp.zeros((heads_local,), jnp.float32)
    saved_parts = []
    for block_index in range(stretch_count):
        first_row = block_index * STRETCH
        last_row = first_row + STRETCH
        intra_part, stretch_state, cumul_keep = stretch_local(
            x_heads[first_row:last_row],
            b_mat[first_row:last_row],
            c_mat[first_row:last_row],
            step_size[:, first_row:last_row],
            log_keep[:, first_row:last_row],
        )
        saved_parts.append((intra_part, cumul_keep, entry_state, decay_total))
        entry_state = jnp.exp(cumul_keep[:, -1])[:, None, None] * entry_state + stretch_state
        decay_total = decay_total + cumul_keep[:, -1]
    incoming = exclusive_scan(entry_state, decay_total, "seq")
    pieces_out = []
    for block_index in range(stretch_count):
        intra_part, cumul_keep, entry_part, decay_part = saved_parts[block_index]
        first_row = block_index * STRETCH
        state_in = entry_part + jnp.exp(decay_part)[:, None, None] * incoming
        from_state = read_state(c_mat[first_row : first_row + STRETCH], state_in)
        pieces_out.append(intra_part + jnp.exp(cumul_keep).T[:, :, None] * from_state)
    ssd_out = jnp.concatenate(pieces_out, axis=0) + skip_gain[None, :, None] * x_heads.astype(
        jnp.float32
    )
    gated = ssd_out.reshape(tok_rows, channels) * silu_act(z_gate.astype(jnp.float32))
    square_sum = lax.psum(jnp.sum(gated * gated, axis=1), "tensor")
    width_all = channels * lax.axis_size("tensor")
    mixed_seq = (
        gated * lax.rsqrt(square_sum / width_all + EPSILON)[:, None] * norm_gain[None, :]
    ).astype(jnp.bfloat16)
    local_ends = seg_ends - lax.axis_index("seq") * tok_rows
    summaries = jnp.take(mixed_seq, local_ends, axis=0)
    pool_heads_local = POOL_HEADS // lax.axis_size("tensor")
    pool_width = channels // pool_heads_local
    scale_factor = 1.0 / math.sqrt(pool_width)
    pools_all = queries_all.shape[0]
    segs_local = summaries.shape[0]
    queries = queries_all.reshape(pools_all, pool_heads_local, pool_width)
    seg_index = lax.axis_index("seq") * segs_local + lax.iota(jnp.int32, segs_local)
    inside = (seg_index[None, :] >= start_all[:, None]) & (seg_index[None, :] < stop_all[:, None])
    keys_block = summaries.reshape(segs_local, pool_heads_local, pool_width)
    logits = (
        jnp.einsum("pad,rad->apr", queries, keys_block, preferred_element_type=jnp.float32)
        * scale_factor
    )
    logits = jnp.where(inside[None], logits, MASKED)
    peak = jnp.max(logits, axis=2).astype(jnp.bfloat16).astype(jnp.float32)
    expo = jnp.where(inside[None], jnp.exp(logits - peak[:, :, None]), 0.0)
    denom = jnp.sum(expo, axis=2)
    numer = jnp.einsum(
        "apr,rad->pad", expo.astype(jnp.bfloat16), keys_block, preferred_element_type=jnp.float32
    )
    denom_high = denom.astype(jnp.bfloat16)
    denom_low = (denom - denom_high.astype(jnp.float32)).astype(jnp.bfloat16)
    parts = jnp.concatenate(
        [
            numer.reshape(pools_all, channels).astype(jnp.bfloat16),
            peak.T.astype(jnp.bfloat16),
            denom_high.T,
            denom_low.T,
        ],
        axis=1,
    )
    parts = lax.all_to_all(parts, "seq", 0, 0, tiled=True).astype(jnp.float32)
    parts = parts.reshape(seq_count, pools_local, channels + 3 * pool_heads_local)
    numer_parts = parts[:, :, :channels].reshape(
        seq_count, pools_local, pool_heads_local, pool_width
    )
    stats_parts = parts[:, :, channels:].reshape(seq_count, pools_local, 3, pool_heads_local)
    peak_parts = stats_parts[:, :, 0]
    denom_parts = stats_parts[:, :, 1] + stats_parts[:, :, 2]
    peak_all = jnp.max(peak_parts, axis=0)
    rescale = jnp.exp(peak_parts - peak_all[None])
    denom_all = jnp.sum(rescale * denom_parts, axis=0)
    numer_all = jnp.sum(rescale[:, :, :, None] * numer_parts, axis=0)
    pooled = (numer_all / denom_all[:, :, None]).reshape(pools_local, channels)
    return (mixed_seq, pooled)


def solution(mesh):
    in_specs = (
        P(("groups", "seq"), "tensor"),
        P(("groups", "seq"), "tensor"),
        P(("groups", "seq"), None),
        P("tensor", ("groups", "seq")),
        P("tensor", ("groups", "seq")),
        P("tensor"),
        P(None, "tensor"),
        P(),
        P("tensor"),
        P(("groups", "seq")),
        P(("groups", "seq"), "tensor"),
        P(("groups", "seq")),
        P(("groups", "seq")),
    )
    out_specs = (P(("groups", "seq"), "tensor"), P(("groups", "seq"), "tensor"))
    return jax.shard_map(local, mesh=mesh, in_specs=in_specs, out_specs=out_specs, check_vma=False)
```

```python
import math

import jax
import jax.numpy as jnp
from jax import lax
from jax.sharding import PartitionSpec as P

STRETCH = 256
POOL_HEADS = 32


EPSILON = 1e-05
MASKED = -1e30


def passed_along(value, axis, steps):
    count = lax.axis_size(axis)
    leading, last = (max(0, -steps), min(count, count - steps))
    return lax.ppermute(value, axis, [(source, source + steps) for source in range(leading, last)])


def silu_act(values):
    return values / (1.0 + jnp.exp(-values))


def causal_conv(before, current, weights):
    kernel_width = weights.shape[0]
    length = current.shape[0]
    padded = jnp.concatenate([before, current], axis=0)
    summed = jnp.zeros(current.shape, jnp.float32)
    for offset in range(kernel_width):
        summed = summed + padded[offset : offset + length].astype(jnp.float32) * weights[
            offset
        ].astype(jnp.float32)
    return silu_act(summed).astype(jnp.bfloat16)


def stretch_local(x_block, b_block, c_block, step_block, keep_block):
    block_len = x_block.shape[0]
    cumul_keep = jnp.cumsum(keep_block, axis=1)
    lower_mask = lax.broadcasted_iota(jnp.int32, (block_len, block_len), 0) >= lax.broadcasted_iota(
        jnp.int32, (block_len, block_len), 1
    )
    inner_prod = jnp.einsum("is,js->ij", c_block, b_block, preferred_element_type=jnp.float32)
    spread = cumul_keep[:, :, None] - cumul_keep[:, None, :]
    decay_mask = jnp.where(lower_mask[None], jnp.exp(jnp.where(lower_mask[None], spread, 0.0)), 0.0)
    mixing = (decay_mask * inner_prod[None] * step_block[:, None, :]).astype(jnp.bfloat16)
    intra_part = jnp.einsum("hij,jhp->ihp", mixing, x_block, preferred_element_type=jnp.float32)
    tail_weight = jnp.exp(cumul_keep[:, -1:] - cumul_keep) * step_block
    weighted = (tail_weight.T[:, :, None] * x_block.astype(jnp.float32)).astype(jnp.bfloat16)
    stretch_state = jnp.einsum("jhp,js->hps", weighted, b_block, preferred_element_type=jnp.float32)
    return (intra_part, stretch_state, cumul_keep)


def combine(earlier, later):
    return (earlier[0] * jnp.exp(later[1])[:, None, None] + later[0], earlier[1] + later[1])


def exclusive_scan(state, decay, axis):
    count = lax.axis_size(axis)
    window = (state, decay)
    before = (jnp.zeros_like(state), jnp.zeros_like(decay))
    shift = 1
    while shift < count:
        sent_state = passed_along(window[0].astype(jnp.bfloat16), axis, shift)
        sent_decay = passed_along(window[1], axis, shift)
        received = (sent_state.astype(jnp.float32), sent_decay)
        before = combine(received, before)
        if shift * 2 < count:
            window = combine(received, window)
        shift *= 2
    return before[0]


def butterfly_sum(value, axis):
    count = lax.axis_size(axis)
    if count & (count - 1):
        return lax.psum(value, axis)
    stride = 1
    while stride < count:
        partner = lax.ppermute(value, axis, [(i, i ^ stride) for i in range(count)])
        value = value + partner
        stride *= 2
    return value


def read_state(c_block, state_in):
    state_high = state_in.astype(jnp.bfloat16)
    state_low = (state_in - state_high.astype(jnp.float32)).astype(jnp.bfloat16)
    high_part = jnp.einsum("is,hps->ihp", c_block, state_high, preferred_element_type=jnp.float32)
    low_part = jnp.einsum("is,hps->ihp", c_block, state_low, preferred_element_type=jnp.float32)
    return high_part + low_part


def local(
    x_in,
    z_gate,
    bc_in,
    step_size,
    log_keep,
    skip_gain,
    conv_x,
    conv_bc,
    norm_gain,
    seg_ends,
    pool_query,
    pool_start,
    pool_stop,
):
    tok_rows = x_in.shape[0]
    channels = x_in.shape[1]
    heads_local = step_size.shape[0]
    head_width = channels // heads_local
    state_width = bc_in.shape[1] // 2
    rim_rows = conv_x.shape[0] - 1
    seq_count = lax.axis_size("seq")
    pools_local = pool_query.shape[0]
    bounds = jnp.stack([pool_start, pool_stop], axis=1)
    bounds_split = jnp.concatenate([bounds // 64, bounds % 64], axis=1).astype(jnp.bfloat16)
    query_rows = jnp.concatenate([pool_query, bounds_split], axis=1)
    query_rows = jnp.broadcast_to(query_rows[None], (seq_count,) + query_rows.shape)
    query_rows = lax.all_to_all(
        query_rows.reshape(seq_count * pools_local, -1), "seq", 0, 0, tiled=True
    )
    queries_all = query_rows[:, :channels]
    bounds_all = query_rows[:, channels:].astype(jnp.int32)
    start_all = bounds_all[:, 0] * 64 + bounds_all[:, 2]
    stop_all = bounds_all[:, 1] * 64 + bounds_all[:, 3]
    edge_rows = jnp.concatenate([x_in[tok_rows - rim_rows :], bc_in[tok_rows - rim_rows :]], axis=1)
    before = passed_along(edge_rows, "seq", 1)
    x_conv = causal_conv(before[:, :channels], x_in, conv_x)
    bc_conv = causal_conv(before[:, channels:], bc_in, conv_bc)
    b_mat = bc_conv[:, :state_width]
    c_mat = bc_conv[:, state_width:]
    x_heads = x_conv.reshape(tok_rows, heads_local, head_width)
    stretch_count = tok_rows // STRETCH
    entry_state = jnp.zeros((heads_local, head_width, state_width), jnp.float32)
    decay_total = jnp.zeros((heads_local,), jnp.float32)
    saved_parts = []
    for block_index in range(stretch_count):
        first_row = block_index * STRETCH
        last_row = first_row + STRETCH
        intra_part, stretch_state, cumul_keep = stretch_local(
            x_heads[first_row:last_row],
            b_mat[first_row:last_row],
            c_mat[first_row:last_row],
            step_size[:, first_row:last_row],
            log_keep[:, first_row:last_row],
        )
        saved_parts.append((intra_part, cumul_keep, entry_state, decay_total))
        entry_state = jnp.exp(cumul_keep[:, -1])[:, None, None] * entry_state + stretch_state
        decay_total = decay_total + cumul_keep[:, -1]
    incoming = exclusive_scan(entry_state, decay_total, "seq")
    pieces_out = []
    for block_index in range(stretch_count):
        intra_part, cumul_keep, entry_part, decay_part = saved_parts[block_index]
        first_row = block_index * STRETCH
        state_in = entry_part + jnp.exp(decay_part)[:, None, None] * incoming
        from_state = read_state(c_mat[first_row : first_row + STRETCH], state_in)
        pieces_out.append(intra_part + jnp.exp(cumul_keep).T[:, :, None] * from_state)
    ssd_out = jnp.concatenate(pieces_out, axis=0) + skip_gain[None, :, None] * x_heads.astype(
        jnp.float32
    )
    gated = ssd_out.reshape(tok_rows, channels) * silu_act(z_gate.astype(jnp.float32))
    square_sum = butterfly_sum(jnp.sum(gated * gated, axis=1), "tensor")
    width_all = channels * lax.axis_size("tensor")
    mixed_seq = (
        gated * lax.rsqrt(square_sum / width_all + EPSILON)[:, None] * norm_gain[None, :]
    ).astype(jnp.bfloat16)
    local_ends = seg_ends - lax.axis_index("seq") * tok_rows
    summaries = jnp.take(mixed_seq, local_ends, axis=0)
    pool_heads_local = POOL_HEADS // lax.axis_size("tensor")
    pool_width = channels // pool_heads_local
    scale_factor = 1.0 / math.sqrt(pool_width)
    pools_all = queries_all.shape[0]
    segs_local = summaries.shape[0]
    queries = queries_all.reshape(pools_all, pool_heads_local, pool_width)
    seg_index = lax.axis_index("seq") * segs_local + lax.iota(jnp.int32, segs_local)
    inside = (seg_index[None, :] >= start_all[:, None]) & (seg_index[None, :] < stop_all[:, None])
    keys_block = summaries.reshape(segs_local, pool_heads_local, pool_width)
    logits = (
        jnp.einsum("pad,rad->apr", queries, keys_block, preferred_element_type=jnp.float32)
        * scale_factor
    )
    logits = jnp.where(inside[None], logits, MASKED)
    peak = jnp.max(logits, axis=2).astype(jnp.bfloat16).astype(jnp.float32)
    expo = jnp.where(inside[None], jnp.exp(logits - peak[:, :, None]), 0.0)
    denom = jnp.sum(expo, axis=2)
    numer = jnp.einsum(
        "apr,rad->pad", expo.astype(jnp.bfloat16), keys_block, preferred_element_type=jnp.float32
    )
    denom_high = denom.astype(jnp.bfloat16)
    denom_low = (denom - denom_high.astype(jnp.float32)).astype(jnp.bfloat16)
    parts = jnp.concatenate(
        [
            numer.reshape(pools_all, channels).astype(jnp.bfloat16),
            peak.T.astype(jnp.bfloat16),
            denom_high.T,
            denom_low.T,
        ],
        axis=1,
    )
    parts = lax.all_to_all(parts, "seq", 0, 0, tiled=True).astype(jnp.float32)
    parts = parts.reshape(seq_count, pools_local, channels + 3 * pool_heads_local)
    numer_parts = parts[:, :, :channels].reshape(
        seq_count, pools_local, pool_heads_local, pool_width
    )
    stats_parts = parts[:, :, channels:].reshape(seq_count, pools_local, 3, pool_heads_local)
    peak_parts = stats_parts[:, :, 0]
    denom_parts = stats_parts[:, :, 1] + stats_parts[:, :, 2]
    peak_all = jnp.max(peak_parts, axis=0)
    rescale = jnp.exp(peak_parts - peak_all[None])
    denom_all = jnp.sum(rescale * denom_parts, axis=0)
    numer_all = jnp.sum(rescale[:, :, :, None] * numer_parts, axis=0)
    pooled = (numer_all / denom_all[:, :, None]).reshape(pools_local, channels)
    return (mixed_seq, pooled)


def solution(mesh):
    in_specs = (
        P(("groups", "seq"), "tensor"),
        P(("groups", "seq"), "tensor"),
        P(("groups", "seq"), None),
        P("tensor", ("groups", "seq")),
        P("tensor", ("groups", "seq")),
        P("tensor"),
        P(None, "tensor"),
        P(),
        P("tensor"),
        P(("groups", "seq")),
        P(("groups", "seq"), "tensor"),
        P(("groups", "seq")),
        P(("groups", "seq")),
    )
    out_specs = (P(("groups", "seq"), "tensor"), P(("groups", "seq"), "tensor"))
    return jax.shard_map(local, mesh=mesh, in_specs=in_specs, out_specs=out_specs, check_vma=False)
```

```python
import math

import jax
import jax.numpy as jnp
from jax import lax
from jax.experimental.layout import Layout, with_layout_constraint
from jax.sharding import PartitionSpec as P

STRETCH = 256
POOL_HEADS = 32


EPSILON = 1e-05
MASKED = -1e30


def passed_along(value, axis, steps):
    count = lax.axis_size(axis)
    leading, last = (max(0, -steps), min(count, count - steps))
    return lax.ppermute(value, axis, [(source, source + steps) for source in range(leading, last)])


def silu_act(values):
    return values / (1.0 + jnp.exp(-values))


def causal_conv(before, current, weights):
    kernel_width = weights.shape[0]
    length = current.shape[0]
    padded = jnp.concatenate([before, current], axis=0)
    summed = jnp.zeros(current.shape, jnp.float32)
    for offset in range(kernel_width):
        summed = summed + padded[offset : offset + length].astype(jnp.float32) * weights[
            offset
        ].astype(jnp.float32)
    return silu_act(summed).astype(jnp.bfloat16)


def stretch_local(x_block, b_block, c_block, step_block, keep_block):
    block_len = x_block.shape[0]
    cumul_keep = jnp.cumsum(keep_block, axis=1)
    lower_mask = lax.broadcasted_iota(jnp.int32, (block_len, block_len), 0) >= lax.broadcasted_iota(
        jnp.int32, (block_len, block_len), 1
    )
    inner_prod = jnp.einsum("is,js->ij", c_block, b_block, preferred_element_type=jnp.float32)
    spread = cumul_keep[:, :, None] - cumul_keep[:, None, :]
    decay_mask = jnp.where(lower_mask[None], jnp.exp(jnp.where(lower_mask[None], spread, 0.0)), 0.0)
    mixing = (decay_mask * inner_prod[None] * step_block[:, None, :]).astype(jnp.bfloat16)
    intra_part = jnp.einsum("hij,jhp->hpi", mixing, x_block, preferred_element_type=jnp.float32)
    tail_weight = jnp.exp(cumul_keep[:, -1:] - cumul_keep) * step_block
    weighted = (tail_weight.T[:, :, None] * x_block.astype(jnp.float32)).astype(jnp.bfloat16)
    stretch_state = jnp.einsum("jhp,js->hps", weighted, b_block, preferred_element_type=jnp.float32)
    return (intra_part, stretch_state, cumul_keep)


def combine(earlier, later):
    return (earlier[0] * jnp.exp(later[1])[:, None, None] + later[0], earlier[1] + later[1])


def exclusive_scan(state, decay, axis):
    count = lax.axis_size(axis)
    window = (state, decay)
    before = (jnp.zeros_like(state), jnp.zeros_like(decay))
    shift = 1
    while shift < count:
        sent_state = passed_along(window[0].astype(jnp.bfloat16), axis, shift)
        sent_decay = passed_along(window[1], axis, shift)
        received = (sent_state.astype(jnp.float32), sent_decay)
        before = combine(received, before)
        if shift * 2 < count:
            window = combine(received, window)
        shift *= 2
    return before[0]


def butterfly_sum(value, axis):
    count = lax.axis_size(axis)
    if count & (count - 1):
        return lax.psum(value, axis)
    stride = 1
    while stride < count:
        partner = lax.ppermute(value, axis, [(i, i ^ stride) for i in range(count)])
        value = value + partner
        stride *= 2
    return value


def read_state(c_block, state_in):
    state_high = state_in.astype(jnp.bfloat16)
    state_low = (state_in - state_high.astype(jnp.float32)).astype(jnp.bfloat16)
    high_part = jnp.einsum("hps,is->hpi", state_high, c_block, preferred_element_type=jnp.float32)
    low_part = jnp.einsum("hps,is->hpi", state_low, c_block, preferred_element_type=jnp.float32)
    return high_part + low_part


def local(
    x_in,
    z_gate,
    bc_in,
    step_size,
    log_keep,
    skip_gain,
    conv_x,
    conv_bc,
    norm_gain,
    seg_ends,
    pool_query,
    pool_start,
    pool_stop,
):
    tok_rows = x_in.shape[0]
    channels = x_in.shape[1]
    heads_local = step_size.shape[0]
    head_width = channels // heads_local
    state_width = bc_in.shape[1] // 2
    rim_rows = conv_x.shape[0] - 1
    seq_count = lax.axis_size("seq")
    pools_local = pool_query.shape[0]
    bounds = jnp.stack([pool_start, pool_stop], axis=1)
    bounds_split = jnp.concatenate([bounds // 64, bounds % 64], axis=1).astype(jnp.bfloat16)
    query_rows = jnp.concatenate([pool_query, bounds_split], axis=1)
    query_rows = jnp.broadcast_to(query_rows[None], (seq_count,) + query_rows.shape)
    query_rows = lax.all_to_all(
        query_rows.reshape(seq_count * pools_local, -1), "seq", 0, 0, tiled=True
    )
    queries_all = query_rows[:, :channels]
    bounds_all = query_rows[:, channels:].astype(jnp.int32)
    start_all = bounds_all[:, 0] * 64 + bounds_all[:, 2]
    stop_all = bounds_all[:, 1] * 64 + bounds_all[:, 3]
    edge_rows = jnp.concatenate([x_in[tok_rows - rim_rows :], bc_in[tok_rows - rim_rows :]], axis=1)
    before = passed_along(edge_rows, "seq", 1)
    x_conv = causal_conv(before[:, :channels], x_in, conv_x)
    bc_conv = causal_conv(before[:, channels:], bc_in, conv_bc)
    b_mat = bc_conv[:, :state_width]
    c_mat = bc_conv[:, state_width:]
    x_heads = x_conv.reshape(tok_rows, heads_local, head_width)
    stretch_count = tok_rows // STRETCH
    entry_state = jnp.zeros((heads_local, head_width, state_width), jnp.float32)
    decay_total = jnp.zeros((heads_local,), jnp.float32)
    saved_parts = []
    for block_index in range(stretch_count):
        first_row = block_index * STRETCH
        last_row = first_row + STRETCH
        intra_part, stretch_state, cumul_keep = stretch_local(
            x_heads[first_row:last_row],
            b_mat[first_row:last_row],
            c_mat[first_row:last_row],
            step_size[:, first_row:last_row],
            log_keep[:, first_row:last_row],
        )
        saved_parts.append((intra_part, cumul_keep, entry_state, decay_total))
        entry_state = jnp.exp(cumul_keep[:, -1])[:, None, None] * entry_state + stretch_state
        decay_total = decay_total + cumul_keep[:, -1]
    incoming = exclusive_scan(entry_state, decay_total, "seq")
    x_major = x_conv.T.reshape(heads_local, head_width, tok_rows)
    z_major = z_gate.T
    pieces_out = []
    for block_index in range(stretch_count):
        intra_part, cumul_keep, entry_part, decay_part = saved_parts[block_index]
        first_row = block_index * STRETCH
        state_in = entry_part + jnp.exp(decay_part)[:, None, None] * incoming
        from_state = read_state(c_mat[first_row : first_row + STRETCH], state_in)
        pieces_out.append(intra_part + jnp.exp(cumul_keep)[:, None, :] * from_state)
    ssd_out = jnp.concatenate(pieces_out, axis=2) + skip_gain[:, None, None] * x_major.astype(
        jnp.float32
    )
    gated = ssd_out.reshape(channels, tok_rows) * silu_act(z_major.astype(jnp.float32))
    gated = with_layout_constraint(gated, Layout(major_to_minor=(0, 1)))
    square_sum = butterfly_sum(jnp.sum(gated * gated, axis=0), "tensor")
    width_all = channels * lax.axis_size("tensor")
    mixed_major = (
        gated * lax.rsqrt(square_sum / width_all + EPSILON)[None, :] * norm_gain[:, None]
    ).astype(jnp.bfloat16)
    mixed_seq = mixed_major.T
    local_ends = seg_ends - lax.axis_index("seq") * tok_rows
    summaries = jnp.take(mixed_seq, local_ends, axis=0)
    pool_heads_local = POOL_HEADS // lax.axis_size("tensor")
    pool_width = channels // pool_heads_local
    scale_factor = 1.0 / math.sqrt(pool_width)
    pools_all = queries_all.shape[0]
    segs_local = summaries.shape[0]
    queries = queries_all.reshape(pools_all, pool_heads_local, pool_width)
    seg_index = lax.axis_index("seq") * segs_local + lax.iota(jnp.int32, segs_local)
    inside = (seg_index[None, :] >= start_all[:, None]) & (seg_index[None, :] < stop_all[:, None])
    keys_block = summaries.reshape(segs_local, pool_heads_local, pool_width)
    logits = (
        jnp.einsum("pad,rad->apr", queries, keys_block, preferred_element_type=jnp.float32)
        * scale_factor
    )
    logits = jnp.where(inside[None], logits, MASKED)
    peak = jnp.max(logits, axis=2).astype(jnp.bfloat16).astype(jnp.float32)
    expo = jnp.where(inside[None], jnp.exp(logits - peak[:, :, None]), 0.0)
    denom = jnp.sum(expo, axis=2)
    numer = jnp.einsum(
        "apr,rad->pad", expo.astype(jnp.bfloat16), keys_block, preferred_element_type=jnp.float32
    )
    denom_high = denom.astype(jnp.bfloat16)
    denom_low = (denom - denom_high.astype(jnp.float32)).astype(jnp.bfloat16)
    parts = jnp.concatenate(
        [
            numer.reshape(pools_all, channels).astype(jnp.bfloat16),
            peak.T.astype(jnp.bfloat16),
            denom_high.T,
            denom_low.T,
        ],
        axis=1,
    )
    parts = lax.all_to_all(parts, "seq", 0, 0, tiled=True).astype(jnp.float32)
    parts = parts.reshape(seq_count, pools_local, channels + 3 * pool_heads_local)
    numer_parts = parts[:, :, :channels].reshape(
        seq_count, pools_local, pool_heads_local, pool_width
    )
    stats_parts = parts[:, :, channels:].reshape(seq_count, pools_local, 3, pool_heads_local)
    peak_parts = stats_parts[:, :, 0]
    denom_parts = stats_parts[:, :, 1] + stats_parts[:, :, 2]
    peak_all = jnp.max(peak_parts, axis=0)
    rescale = jnp.exp(peak_parts - peak_all[None])
    denom_all = jnp.sum(rescale * denom_parts, axis=0)
    numer_all = jnp.sum(rescale[:, :, :, None] * numer_parts, axis=0)
    pooled = (numer_all / denom_all[:, :, None]).reshape(pools_local, channels)
    return (mixed_seq, pooled)


def solution(mesh):
    in_specs = (
        P(("groups", "seq"), "tensor"),
        P(("groups", "seq"), "tensor"),
        P(("groups", "seq"), None),
        P("tensor", ("groups", "seq")),
        P("tensor", ("groups", "seq")),
        P("tensor"),
        P(None, "tensor"),
        P(),
        P("tensor"),
        P(("groups", "seq")),
        P(("groups", "seq"), "tensor"),
        P(("groups", "seq")),
        P(("groups", "seq")),
    )
    out_specs = (P(("groups", "seq"), "tensor"), P(("groups", "seq"), "tensor"))
    return jax.shard_map(local, mesh=mesh, in_specs=in_specs, out_specs=out_specs, check_vma=False)
```

```python
import math

import jax
import jax.numpy as jnp
from jax import lax
from jax.experimental.layout import Layout, with_layout_constraint
from jax.sharding import PartitionSpec as P

STRETCH = 256
POOL_HEADS = 32


EPSILON = 1e-05
MASKED = -1e30


def passed_along(value, axis, steps):
    count = lax.axis_size(axis)
    leading, last = (max(0, -steps), min(count, count - steps))
    return lax.ppermute(value, axis, [(source, source + steps) for source in range(leading, last)])


def silu_act(values):
    return values / (1.0 + jnp.exp(-values))


def causal_conv(before, current, weights):
    kernel_width = weights.shape[0]
    length = current.shape[0]
    padded = jnp.concatenate([before, current], axis=0)
    summed = jnp.zeros(current.shape, jnp.float32)
    for offset in range(kernel_width):
        summed = summed + padded[offset : offset + length].astype(jnp.float32) * weights[
            offset
        ].astype(jnp.float32)
    return silu_act(summed).astype(jnp.bfloat16)


def stretch_local(x_block, b_block, c_block, step_block, keep_block):
    block_len = x_block.shape[0]
    cumul_keep = jnp.cumsum(keep_block, axis=1)
    lower_mask = lax.broadcasted_iota(jnp.int32, (block_len, block_len), 0) >= lax.broadcasted_iota(
        jnp.int32, (block_len, block_len), 1
    )
    inner_prod = jnp.einsum("is,js->ij", c_block, b_block, preferred_element_type=jnp.float32)
    spread = cumul_keep[:, :, None] - cumul_keep[:, None, :]
    decay_mask = jnp.where(lower_mask[None], jnp.exp(jnp.where(lower_mask[None], spread, 0.0)), 0.0)
    mixing = (decay_mask * inner_prod[None] * step_block[:, None, :]).astype(jnp.bfloat16)
    intra_part = jnp.einsum("hij,jhp->hpi", mixing, x_block, preferred_element_type=jnp.float32)
    tail_weight = jnp.exp(cumul_keep[:, -1:] - cumul_keep) * step_block
    weighted = (tail_weight.T[:, :, None] * x_block.astype(jnp.float32)).astype(jnp.bfloat16)
    stretch_state = jnp.einsum("jhp,js->hps", weighted, b_block, preferred_element_type=jnp.float32)
    return (intra_part, stretch_state, cumul_keep)


def combine(earlier, later):
    return (earlier[0] * jnp.exp(later[1])[:, None, None] + later[0], earlier[1] + later[1])


def exclusive_scan(state, decay, axis, rider):
    count = lax.axis_size(axis)
    window = (state, decay)
    before = (jnp.zeros_like(state), jnp.zeros_like(decay))
    shift = 1
    while shift < count:
        sent_state = passed_along(window[0].astype(jnp.bfloat16), axis, shift)
        sent_decay = passed_along(window[1], axis, shift)
        if shift == 1:
            sent_state, rider = lax.optimization_barrier((sent_state, rider))
        received = (sent_state.astype(jnp.float32), sent_decay)
        before = combine(received, before)
        if shift * 2 < count:
            window = combine(received, window)
        shift *= 2
    return before[0], rider


def butterfly_sum(value, axis):
    count = lax.axis_size(axis)
    if count & (count - 1):
        return lax.psum(value, axis)
    stride = 1
    while stride < count:
        partner = lax.ppermute(value, axis, [(i, i ^ stride) for i in range(count)])
        value = value + partner
        stride *= 2
    return value


def read_state(c_block, state_in):
    state_high = state_in.astype(jnp.bfloat16)
    state_low = (state_in - state_high.astype(jnp.float32)).astype(jnp.bfloat16)
    high_part = jnp.einsum("hps,is->hpi", state_high, c_block, preferred_element_type=jnp.float32)
    low_part = jnp.einsum("hps,is->hpi", state_low, c_block, preferred_element_type=jnp.float32)
    return high_part + low_part


def local(
    x_in,
    z_gate,
    bc_in,
    step_size,
    log_keep,
    skip_gain,
    conv_x,
    conv_bc,
    norm_gain,
    seg_ends,
    pool_query,
    pool_start,
    pool_stop,
):
    tok_rows = x_in.shape[0]
    channels = x_in.shape[1]
    heads_local = step_size.shape[0]
    head_width = channels // heads_local
    state_width = bc_in.shape[1] // 2
    rim_rows = conv_x.shape[0] - 1
    seq_count = lax.axis_size("seq")
    pools_local = pool_query.shape[0]
    bounds = jnp.stack([pool_start, pool_stop], axis=1)
    bounds_split = jnp.concatenate([bounds // 64, bounds % 64], axis=1).astype(jnp.bfloat16)
    query_rows = jnp.concatenate([pool_query, bounds_split], axis=1)
    query_rows = jnp.broadcast_to(query_rows[None], (seq_count,) + query_rows.shape)
    query_rows = lax.all_to_all(
        query_rows.reshape(seq_count * pools_local, -1), "seq", 0, 0, tiled=True
    )
    queries_all = query_rows[:, :channels]
    bounds_all = query_rows[:, channels:].astype(jnp.int32)
    start_all = bounds_all[:, 0] * 64 + bounds_all[:, 2]
    stop_all = bounds_all[:, 1] * 64 + bounds_all[:, 3]
    edge_rows = jnp.concatenate([x_in[tok_rows - rim_rows :], bc_in[tok_rows - rim_rows :]], axis=1)
    before = passed_along(edge_rows, "seq", 1)
    x_conv = causal_conv(before[:, :channels], x_in, conv_x)
    x_conv = with_layout_constraint(x_conv, Layout(major_to_minor=(0, 1)))
    bc_conv = causal_conv(before[:, channels:], bc_in, conv_bc)
    b_mat = bc_conv[:, :state_width]
    c_mat = bc_conv[:, state_width:]
    x_heads = x_conv.reshape(tok_rows, heads_local, head_width)
    stretch_count = tok_rows // STRETCH
    entry_state = jnp.zeros((heads_local, head_width, state_width), jnp.float32)
    decay_total = jnp.zeros((heads_local,), jnp.float32)
    saved_parts = []
    for block_index in range(stretch_count):
        first_row = block_index * STRETCH
        last_row = first_row + STRETCH
        intra_part, stretch_state, cumul_keep = stretch_local(
            x_heads[first_row:last_row],
            b_mat[first_row:last_row],
            c_mat[first_row:last_row],
            step_size[:, first_row:last_row],
            log_keep[:, first_row:last_row],
        )
        saved_parts.append((intra_part, cumul_keep, entry_state, decay_total))
        entry_state = jnp.exp(cumul_keep[:, -1])[:, None, None] * entry_state + stretch_state
        decay_total = decay_total + cumul_keep[:, -1]
    incoming, z_late = exclusive_scan(entry_state, decay_total, "seq", z_gate)
    x_major = x_conv.T.reshape(heads_local, head_width, tok_rows)
    z_major = z_late.T
    pieces_out = []
    for block_index in range(stretch_count):
        intra_part, cumul_keep, entry_part, decay_part = saved_parts[block_index]
        first_row = block_index * STRETCH
        state_in = entry_part + jnp.exp(decay_part)[:, None, None] * incoming
        from_state = read_state(c_mat[first_row : first_row + STRETCH], state_in)
        pieces_out.append(intra_part + jnp.exp(cumul_keep)[:, None, :] * from_state)
    ssd_out = jnp.concatenate(pieces_out, axis=2) + skip_gain[:, None, None] * x_major.astype(
        jnp.float32
    )
    gated = ssd_out.reshape(channels, tok_rows) * silu_act(z_major.astype(jnp.float32))
    gated = with_layout_constraint(gated, Layout(major_to_minor=(0, 1)))
    square_sum = butterfly_sum(jnp.sum(gated * gated, axis=0), "tensor")
    width_all = channels * lax.axis_size("tensor")
    mixed_major = (
        gated * lax.rsqrt(square_sum / width_all + EPSILON)[None, :] * norm_gain[:, None]
    ).astype(jnp.bfloat16)
    mixed_seq = mixed_major.T
    local_ends = seg_ends - lax.axis_index("seq") * tok_rows
    summaries = jnp.take(mixed_seq, local_ends, axis=0)
    pool_heads_local = POOL_HEADS // lax.axis_size("tensor")
    pool_width = channels // pool_heads_local
    scale_factor = 1.0 / math.sqrt(pool_width)
    pools_all = queries_all.shape[0]
    segs_local = summaries.shape[0]
    queries = queries_all.reshape(pools_all, pool_heads_local, pool_width)
    seg_index = lax.axis_index("seq") * segs_local + lax.iota(jnp.int32, segs_local)
    inside = (seg_index[None, :] >= start_all[:, None]) & (seg_index[None, :] < stop_all[:, None])
    keys_block = summaries.reshape(segs_local, pool_heads_local, pool_width)
    logits = (
        jnp.einsum("pad,rad->apr", queries, keys_block, preferred_element_type=jnp.float32)
        * scale_factor
    )
    logits = jnp.where(inside[None], logits, MASKED)
    peak = jnp.max(logits, axis=2).astype(jnp.bfloat16).astype(jnp.float32)
    expo = jnp.where(inside[None], jnp.exp(logits - peak[:, :, None]), 0.0)
    denom = jnp.sum(expo, axis=2)
    numer = jnp.einsum(
        "apr,rad->pad", expo.astype(jnp.bfloat16), keys_block, preferred_element_type=jnp.float32
    )
    denom_high = denom.astype(jnp.bfloat16)
    denom_low = (denom - denom_high.astype(jnp.float32)).astype(jnp.bfloat16)
    parts = jnp.concatenate(
        [
            numer.reshape(pools_all, channels).astype(jnp.bfloat16),
            peak.T.astype(jnp.bfloat16),
            denom_high.T,
            denom_low.T,
        ],
        axis=1,
    )
    parts = lax.all_to_all(parts, "seq", 0, 0, tiled=True).astype(jnp.float32)
    parts = parts.reshape(seq_count, pools_local, channels + 3 * pool_heads_local)
    numer_parts = parts[:, :, :channels].reshape(
        seq_count, pools_local, pool_heads_local, pool_width
    )
    stats_parts = parts[:, :, channels:].reshape(seq_count, pools_local, 3, pool_heads_local)
    peak_parts = stats_parts[:, :, 0]
    denom_parts = stats_parts[:, :, 1] + stats_parts[:, :, 2]
    peak_all = jnp.max(peak_parts, axis=0)
    rescale = jnp.exp(peak_parts - peak_all[None])
    denom_all = jnp.sum(rescale * denom_parts, axis=0)
    numer_all = jnp.sum(rescale[:, :, :, None] * numer_parts, axis=0)
    pooled = (numer_all / denom_all[:, :, None]).reshape(pools_local, channels)
    return (mixed_seq, pooled)


def solution(mesh):
    in_specs = (
        P(("groups", "seq"), "tensor"),
        P(("groups", "seq"), "tensor"),
        P(("groups", "seq"), None),
        P("tensor", ("groups", "seq")),
        P("tensor", ("groups", "seq")),
        P("tensor"),
        P(None, "tensor"),
        P(),
        P("tensor"),
        P(("groups", "seq")),
        P(("groups", "seq"), "tensor"),
        P(("groups", "seq")),
        P(("groups", "seq")),
    )
    out_specs = (P(("groups", "seq"), "tensor"), P(("groups", "seq"), "tensor"))
    return jax.shard_map(local, mesh=mesh, in_specs=in_specs, out_specs=out_specs, check_vma=False)
```

```python
import math

import jax
import jax.numpy as jnp
from jax import lax
from jax.experimental.layout import Layout, with_layout_constraint
from jax.sharding import PartitionSpec as P

STRETCH = 256
POOL_HEADS = 32


EPSILON = 1e-05
MASKED = -1e30


def passed_along(value, axis, steps):
    count = lax.axis_size(axis)
    leading, last = (max(0, -steps), min(count, count - steps))
    return lax.ppermute(value, axis, [(source, source + steps) for source in range(leading, last)])


def silu_act(values):
    return values / (1.0 + jnp.exp(-values))


def causal_conv(before, current, weights):
    kernel_width = weights.shape[0]
    length = current.shape[0]
    padded = jnp.concatenate([before, current], axis=0)
    summed = jnp.zeros(current.shape, jnp.float32)
    for offset in range(kernel_width):
        summed = summed + padded[offset : offset + length].astype(jnp.float32) * weights[
            offset
        ].astype(jnp.float32)
    return silu_act(summed).astype(jnp.bfloat16)


def stretch_local(x_block, b_block, c_block, step_block, keep_block):
    block_len = x_block.shape[0]
    cumul_keep = jnp.cumsum(keep_block, axis=1)
    lower_mask = lax.broadcasted_iota(jnp.int32, (block_len, block_len), 0) >= lax.broadcasted_iota(
        jnp.int32, (block_len, block_len), 1
    )
    inner_prod = jnp.einsum("is,js->ij", c_block, b_block, preferred_element_type=jnp.float32)
    spread = cumul_keep[:, :, None] - cumul_keep[:, None, :]
    decay_mask = jnp.where(lower_mask[None], jnp.exp(jnp.where(lower_mask[None], spread, 0.0)), 0.0)
    mixing = (decay_mask * inner_prod[None] * step_block[:, None, :]).astype(jnp.bfloat16)
    intra_part = jnp.einsum("hij,jhp->hpi", mixing, x_block, preferred_element_type=jnp.float32)
    tail_weight = jnp.exp(cumul_keep[:, -1:] - cumul_keep) * step_block
    weighted = (tail_weight.T[:, :, None] * x_block.astype(jnp.float32)).astype(jnp.bfloat16)
    stretch_state = jnp.einsum("jhp,js->hps", weighted, b_block, preferred_element_type=jnp.float32)
    return (intra_part, stretch_state, cumul_keep)


def combine(earlier, later):
    return (earlier[0] * jnp.exp(later[1])[:, None, None] + later[0], earlier[1] + later[1])


def exclusive_scan(state, decay, axis, rider):
    count = lax.axis_size(axis)
    window = (state, decay)
    before = (jnp.zeros_like(state), jnp.zeros_like(decay))
    shift = 1
    while shift < count:
        sent_state = passed_along(window[0].astype(jnp.bfloat16), axis, shift)
        sent_decay = passed_along(window[1], axis, shift)
        if shift == 1:
            sent_state, rider = lax.optimization_barrier((sent_state, rider))
        received = (sent_state.astype(jnp.float32), sent_decay)
        before = combine(received, before)
        if shift * 2 < count:
            window = combine(received, window)
        shift *= 2
    return before[0], rider


def butterfly_sum(value, axis):
    count = lax.axis_size(axis)
    if count & (count - 1):
        return lax.psum(value, axis)
    stride = 1
    while stride < count:
        partner = lax.ppermute(value, axis, [(i, i ^ stride) for i in range(count)])
        value = value + partner
        stride *= 2
    return value


def read_state(c_block, state_in):
    state_high = state_in.astype(jnp.bfloat16)
    state_low = (state_in - state_high.astype(jnp.float32)).astype(jnp.bfloat16)
    high_part = jnp.einsum("hps,is->hpi", state_high, c_block, preferred_element_type=jnp.float32)
    low_part = jnp.einsum("hps,is->hpi", state_low, c_block, preferred_element_type=jnp.float32)
    return high_part + low_part


def local(
    x_in,
    z_gate,
    bc_in,
    step_size,
    log_keep,
    skip_gain,
    conv_x,
    conv_bc,
    norm_gain,
    seg_ends,
    pool_query,
    pool_start,
    pool_stop,
):
    tok_rows = x_in.shape[0]
    channels = x_in.shape[1]
    heads_local = step_size.shape[0]
    head_width = channels // heads_local
    state_width = bc_in.shape[1] // 2
    rim_rows = conv_x.shape[0] - 1
    seq_count = lax.axis_size("seq")
    pools_local = pool_query.shape[0]
    bounds = jnp.stack([pool_start, pool_stop], axis=1)
    bounds_split = jnp.concatenate([bounds // 64, bounds % 64], axis=1).astype(jnp.bfloat16)
    query_rows = jnp.concatenate([pool_query, bounds_split], axis=1)
    query_rows = jnp.broadcast_to(query_rows[None], (seq_count,) + query_rows.shape)
    query_rows = lax.all_to_all(
        query_rows.reshape(seq_count * pools_local, -1), "seq", 0, 0, tiled=True
    )
    queries_all = query_rows[:, :channels]
    bounds_all = query_rows[:, channels:].astype(jnp.int32)
    start_all = bounds_all[:, 0] * 64 + bounds_all[:, 2]
    stop_all = bounds_all[:, 1] * 64 + bounds_all[:, 3]
    edge_rows = jnp.concatenate([x_in[tok_rows - rim_rows :], bc_in[tok_rows - rim_rows :]], axis=1)
    before = passed_along(edge_rows, "seq", 1)
    x_conv = causal_conv(before[:, :channels], x_in, conv_x)
    x_conv = with_layout_constraint(x_conv, Layout(major_to_minor=(0, 1)))
    bc_conv = causal_conv(before[:, channels:], bc_in, conv_bc)
    b_mat = bc_conv[:, :state_width]
    c_mat = bc_conv[:, state_width:]
    x_heads = x_conv.reshape(tok_rows, heads_local, head_width)
    stretch_count = tok_rows // STRETCH
    entry_state = jnp.zeros((heads_local, head_width, state_width), jnp.float32)
    decay_total = jnp.zeros((heads_local,), jnp.float32)
    saved_parts = []
    for block_index in range(stretch_count):
        first_row = block_index * STRETCH
        last_row = first_row + STRETCH
        intra_part, stretch_state, cumul_keep = stretch_local(
            x_heads[first_row:last_row],
            b_mat[first_row:last_row],
            c_mat[first_row:last_row],
            step_size[:, first_row:last_row],
            log_keep[:, first_row:last_row],
        )
        saved_parts.append((intra_part, cumul_keep, entry_state, decay_total))
        entry_state = jnp.exp(cumul_keep[:, -1])[:, None, None] * entry_state + stretch_state
        decay_total = decay_total + cumul_keep[:, -1]
    incoming, z_late = exclusive_scan(entry_state, decay_total, "seq", z_gate)
    x_major = x_conv.T.reshape(heads_local, head_width, tok_rows)
    z_major = z_late.T
    pieces_out = []
    for block_index in range(stretch_count):
        intra_part, cumul_keep, entry_part, decay_part = saved_parts[block_index]
        first_row = block_index * STRETCH
        state_in = entry_part + jnp.exp(decay_part)[:, None, None] * incoming
        from_state = read_state(c_mat[first_row : first_row + STRETCH], state_in)
        pieces_out.append(intra_part + jnp.exp(cumul_keep)[:, None, :] * from_state)
    ssd_out = jnp.concatenate(pieces_out, axis=2) + skip_gain[:, None, None] * x_major.astype(
        jnp.float32
    )
    gated = ssd_out.reshape(channels, tok_rows) * silu_act(z_major.astype(jnp.float32))
    gated = with_layout_constraint(gated, Layout(major_to_minor=(0, 1)))
    square_sum = butterfly_sum(jnp.sum(gated * gated, axis=0), "tensor")
    width_all = channels * lax.axis_size("tensor")
    mixed_major = (
        gated * lax.rsqrt(square_sum / width_all + EPSILON)[None, :] * norm_gain[:, None]
    ).astype(jnp.bfloat16)
    mixed_seq = mixed_major.T
    local_ends = seg_ends - lax.axis_index("seq") * tok_rows
    summaries = jnp.take(mixed_seq, local_ends, axis=0)
    pool_heads_local = POOL_HEADS // lax.axis_size("tensor")
    pool_width = channels // pool_heads_local
    scale_factor = 1.0 / math.sqrt(pool_width)
    pools_all = queries_all.shape[0]
    segs_local = summaries.shape[0]
    queries = queries_all.reshape(pools_all, pool_heads_local, pool_width)
    seg_index = lax.axis_index("seq") * segs_local + lax.iota(jnp.int32, segs_local)
    inside = (seg_index[None, :] >= start_all[:, None]) & (seg_index[None, :] < stop_all[:, None])
    keys_block = summaries.reshape(segs_local, pool_heads_local, pool_width)
    logits = (
        jnp.einsum("pad,rad->apr", queries, keys_block, preferred_element_type=jnp.float32)
        * scale_factor
    )
    logits = jnp.where(inside[None], logits, MASKED)
    peak = jnp.max(logits, axis=2).astype(jnp.bfloat16).astype(jnp.float32)
    expo = jnp.where(inside[None], jnp.exp(logits - peak[:, :, None]), 0.0)
    denom = jnp.sum(expo, axis=2)
    numer = jnp.einsum(
        "apr,rad->pad", expo.astype(jnp.bfloat16), keys_block, preferred_element_type=jnp.float32
    )
    denom_high = denom.astype(jnp.bfloat16)
    denom_low = (denom - denom_high.astype(jnp.float32)).astype(jnp.bfloat16)
    parts = jnp.concatenate(
        [
            numer.reshape(pools_all, channels).astype(jnp.bfloat16),
            peak.T.astype(jnp.bfloat16),
            denom_high.T,
            denom_low.T,
        ],
        axis=1,
    )
    parts = parts.reshape(seq_count, pools_local, channels + 3 * pool_heads_local)
    place = lax.axis_index("seq")
    gathered = [lax.dynamic_index_in_dim(parts, place, 0, False)]
    for shift in range(1, seq_count):
        chunk = lax.dynamic_index_in_dim(parts, (place + shift) % seq_count, 0, False)
        gathered.append(
            lax.ppermute(
                chunk, "seq", [(i, (i + shift) % seq_count) for i in range(seq_count)]
            )
        )
    parts = jnp.stack(gathered).astype(jnp.float32)
    numer_parts = parts[:, :, :channels].reshape(
        seq_count, pools_local, pool_heads_local, pool_width
    )
    stats_parts = parts[:, :, channels:].reshape(seq_count, pools_local, 3, pool_heads_local)
    peak_parts = stats_parts[:, :, 0]
    denom_parts = stats_parts[:, :, 1] + stats_parts[:, :, 2]
    peak_all = jnp.max(peak_parts, axis=0)
    rescale = jnp.exp(peak_parts - peak_all[None])
    denom_all = jnp.sum(rescale * denom_parts, axis=0)
    numer_all = jnp.sum(rescale[:, :, :, None] * numer_parts, axis=0)
    pooled = (numer_all / denom_all[:, :, None]).reshape(pools_local, channels)
    return (mixed_seq, pooled)


def solution(mesh):
    in_specs = (
        P(("groups", "seq"), "tensor"),
        P(("groups", "seq"), "tensor"),
        P(("groups", "seq"), None),
        P("tensor", ("groups", "seq")),
        P("tensor", ("groups", "seq")),
        P("tensor"),
        P(None, "tensor"),
        P(),
        P("tensor"),
        P(("groups", "seq")),
        P(("groups", "seq"), "tensor"),
        P(("groups", "seq")),
        P(("groups", "seq")),
    )
    out_specs = (P(("groups", "seq"), "tensor"), P(("groups", "seq"), "tensor"))
    return jax.shard_map(local, mesh=mesh, in_specs=in_specs, out_specs=out_specs, check_vma=False)
```

```python
import math

import jax
import jax.numpy as jnp
from jax import lax
from jax.experimental.layout import Layout, with_layout_constraint
from jax.sharding import PartitionSpec as P

STRETCH = 256
POOL_HEADS = 32


EPSILON = 1e-05
MASKED = -1e30


def passed_along(value, axis, steps):
    count = lax.axis_size(axis)
    leading, last = (max(0, -steps), min(count, count - steps))
    return lax.ppermute(value, axis, [(source, source + steps) for source in range(leading, last)])


def silu_act(values):
    return values / (1.0 + jnp.exp(-values))


def causal_conv(before, current, weights):
    kernel_width = weights.shape[0]
    length = current.shape[0]
    padded = jnp.concatenate([before, current], axis=0)
    summed = jnp.zeros(current.shape, jnp.float32)
    for offset in range(kernel_width):
        summed = summed + padded[offset : offset + length].astype(jnp.float32) * weights[
            offset
        ].astype(jnp.float32)
    return silu_act(summed).astype(jnp.bfloat16)


def stretch_local(x_block, b_block, c_block, step_block, keep_block):
    block_len = x_block.shape[0]
    cumul_keep = jnp.cumsum(keep_block, axis=1)
    lower_mask = lax.broadcasted_iota(jnp.int32, (block_len, block_len), 0) >= lax.broadcasted_iota(
        jnp.int32, (block_len, block_len), 1
    )
    inner_prod = jnp.einsum("is,js->ij", c_block, b_block, preferred_element_type=jnp.float32)
    spread = cumul_keep[:, :, None] - cumul_keep[:, None, :]
    decay_mask = jnp.where(lower_mask[None], jnp.exp(jnp.where(lower_mask[None], spread, 0.0)), 0.0)
    mixing = (decay_mask * inner_prod[None] * step_block[:, None, :]).astype(jnp.bfloat16)
    intra_part = jnp.einsum("hij,jhp->hpi", mixing, x_block, preferred_element_type=jnp.float32)
    tail_weight = jnp.exp(cumul_keep[:, -1:] - cumul_keep) * step_block
    weighted = (tail_weight.T[:, :, None] * x_block.astype(jnp.float32)).astype(jnp.bfloat16)
    stretch_state = jnp.einsum("jhp,js->hps", weighted, b_block, preferred_element_type=jnp.float32)
    return (intra_part, stretch_state, cumul_keep)


def combine(earlier, later):
    return (earlier[0] * jnp.exp(later[1])[:, None, None] + later[0], earlier[1] + later[1])


def exclusive_scan(state, decay, axis, rider):
    count = lax.axis_size(axis)
    window = (state, decay)
    before = (jnp.zeros_like(state), jnp.zeros_like(decay))
    shift = 1
    while shift < count:
        sent_state = passed_along(window[0].astype(jnp.bfloat16), axis, shift)
        sent_decay = passed_along(window[1], axis, shift)
        if shift == 1:
            sent_state, rider = lax.optimization_barrier((sent_state, rider))
        received = (sent_state.astype(jnp.float32), sent_decay)
        before = combine(received, before)
        if shift * 2 < count:
            window = combine(received, window)
        shift *= 2
    return before[0], rider


def butterfly_sum(value, axis):
    count = lax.axis_size(axis)
    if count & (count - 1):
        return lax.psum(value, axis)
    stride = 1
    while stride < count:
        partner = lax.ppermute(value, axis, [(i, i ^ stride) for i in range(count)])
        value = value + partner
        stride *= 2
    return value


def read_state(c_block, state_in):
    state_high = state_in.astype(jnp.bfloat16)
    state_low = (state_in - state_high.astype(jnp.float32)).astype(jnp.bfloat16)
    high_part = jnp.einsum("hps,is->hpi", state_high, c_block, preferred_element_type=jnp.float32)
    low_part = jnp.einsum("hps,is->hpi", state_low, c_block, preferred_element_type=jnp.float32)
    return high_part + low_part


def local(
    x_in,
    z_gate,
    bc_in,
    step_size,
    log_keep,
    skip_gain,
    conv_x,
    conv_bc,
    norm_gain,
    seg_ends,
    pool_query,
    pool_start,
    pool_stop,
):
    tok_rows = x_in.shape[0]
    channels = x_in.shape[1]
    heads_local = step_size.shape[0]
    head_width = channels // heads_local
    state_width = bc_in.shape[1] // 2
    rim_rows = conv_x.shape[0] - 1
    seq_count = lax.axis_size("seq")
    pools_local = pool_query.shape[0]
    bounds = jnp.stack([pool_start, pool_stop], axis=1)
    bounds_split = jnp.concatenate([bounds // 64, bounds % 64], axis=1).astype(jnp.bfloat16)
    query_rows = jnp.concatenate([pool_query, bounds_split], axis=1)
    query_rows = jnp.concatenate(
        [query_rows]
        + [
            lax.ppermute(query_rows, "seq", [(i, (i + shift) % seq_count) for i in range(seq_count)])
            for shift in range(1, seq_count)
        ],
        axis=0,
    )
    queries_all = query_rows[:, :channels]
    bounds_all = query_rows[:, channels:].astype(jnp.int32)
    start_all = bounds_all[:, 0] * 64 + bounds_all[:, 2]
    stop_all = bounds_all[:, 1] * 64 + bounds_all[:, 3]
    edge_rows = jnp.concatenate([x_in[tok_rows - rim_rows :], bc_in[tok_rows - rim_rows :]], axis=1)
    before = passed_along(edge_rows, "seq", 1)
    x_conv = causal_conv(before[:, :channels], x_in, conv_x)
    x_conv = with_layout_constraint(x_conv, Layout(major_to_minor=(0, 1)))
    bc_conv = causal_conv(before[:, channels:], bc_in, conv_bc)
    b_mat = bc_conv[:, :state_width]
    c_mat = bc_conv[:, state_width:]
    x_heads = x_conv.reshape(tok_rows, heads_local, head_width)
    stretch_count = tok_rows // STRETCH
    entry_state = jnp.zeros((heads_local, head_width, state_width), jnp.float32)
    decay_total = jnp.zeros((heads_local,), jnp.float32)
    saved_parts = []
    for block_index in range(stretch_count):
        first_row = block_index * STRETCH
        last_row = first_row + STRETCH
        intra_part, stretch_state, cumul_keep = stretch_local(
            x_heads[first_row:last_row],
            b_mat[first_row:last_row],
            c_mat[first_row:last_row],
            step_size[:, first_row:last_row],
            log_keep[:, first_row:last_row],
        )
        saved_parts.append((intra_part, cumul_keep, entry_state, decay_total))
        entry_state = jnp.exp(cumul_keep[:, -1])[:, None, None] * entry_state + stretch_state
        decay_total = decay_total + cumul_keep[:, -1]
    incoming, z_late = exclusive_scan(entry_state, decay_total, "seq", z_gate)
    x_major = x_conv.T.reshape(heads_local, head_width, tok_rows)
    z_major = z_late.T
    pieces_out = []
    for block_index in range(stretch_count):
        intra_part, cumul_keep, entry_part, decay_part = saved_parts[block_index]
        first_row = block_index * STRETCH
        state_in = entry_part + jnp.exp(decay_part)[:, None, None] * incoming
        from_state = read_state(c_mat[first_row : first_row + STRETCH], state_in)
        pieces_out.append(intra_part + jnp.exp(cumul_keep)[:, None, :] * from_state)
    ssd_out = jnp.concatenate(pieces_out, axis=2) + skip_gain[:, None, None] * x_major.astype(
        jnp.float32
    )
    gated = ssd_out.reshape(channels, tok_rows) * silu_act(z_major.astype(jnp.float32))
    gated = with_layout_constraint(gated, Layout(major_to_minor=(0, 1)))
    square_sum = butterfly_sum(jnp.sum(gated * gated, axis=0), "tensor")
    width_all = channels * lax.axis_size("tensor")
    mixed_major = (
        gated * lax.rsqrt(square_sum / width_all + EPSILON)[None, :] * norm_gain[:, None]
    ).astype(jnp.bfloat16)
    mixed_seq = mixed_major.T
    local_ends = seg_ends - lax.axis_index("seq") * tok_rows
    summaries = jnp.take(mixed_seq, local_ends, axis=0)
    pool_heads_local = POOL_HEADS // lax.axis_size("tensor")
    pool_width = channels // pool_heads_local
    scale_factor = 1.0 / math.sqrt(pool_width)
    pools_all = queries_all.shape[0]
    segs_local = summaries.shape[0]
    queries = queries_all.reshape(pools_all, pool_heads_local, pool_width)
    seg_index = lax.axis_index("seq") * segs_local + lax.iota(jnp.int32, segs_local)
    inside = (seg_index[None, :] >= start_all[:, None]) & (seg_index[None, :] < stop_all[:, None])
    keys_block = summaries.reshape(segs_local, pool_heads_local, pool_width)
    logits = (
        jnp.einsum("pad,rad->apr", queries, keys_block, preferred_element_type=jnp.float32)
        * scale_factor
    )
    logits = jnp.where(inside[None], logits, MASKED)
    peak = jnp.max(logits, axis=2).astype(jnp.bfloat16).astype(jnp.float32)
    expo = jnp.where(inside[None], jnp.exp(logits - peak[:, :, None]), 0.0)
    denom = jnp.sum(expo, axis=2)
    numer = jnp.einsum(
        "apr,rad->pad", expo.astype(jnp.bfloat16), keys_block, preferred_element_type=jnp.float32
    )
    denom_high = denom.astype(jnp.bfloat16)
    denom_low = (denom - denom_high.astype(jnp.float32)).astype(jnp.bfloat16)
    parts = jnp.concatenate(
        [
            numer.reshape(pools_all, channels).astype(jnp.bfloat16),
            peak.T.astype(jnp.bfloat16),
            denom_high.T,
            denom_low.T,
        ],
        axis=1,
    )
    parts = parts.reshape(seq_count, pools_local, channels + 3 * pool_heads_local)
    gathered = [parts[0]]
    for shift in range(1, seq_count):
        gathered.append(
            lax.ppermute(
                parts[shift], "seq", [(i, (i - shift) % seq_count) for i in range(seq_count)]
            )
        )
    parts = jnp.stack(gathered).astype(jnp.float32)
    numer_parts = parts[:, :, :channels].reshape(
        seq_count, pools_local, pool_heads_local, pool_width
    )
    stats_parts = parts[:, :, channels:].reshape(seq_count, pools_local, 3, pool_heads_local)
    peak_parts = stats_parts[:, :, 0]
    denom_parts = stats_parts[:, :, 1] + stats_parts[:, :, 2]
    peak_all = jnp.max(peak_parts, axis=0)
    rescale = jnp.exp(peak_parts - peak_all[None])
    denom_all = jnp.sum(rescale * denom_parts, axis=0)
    numer_all = jnp.sum(rescale[:, :, :, None] * numer_parts, axis=0)
    pooled = (numer_all / denom_all[:, :, None]).reshape(pools_local, channels)
    return (mixed_seq, pooled)


def solution(mesh):
    in_specs = (
        P(("groups", "seq"), "tensor"),
        P(("groups", "seq"), "tensor"),
        P(("groups", "seq"), None),
        P("tensor", ("groups", "seq")),
        P("tensor", ("groups", "seq")),
        P("tensor"),
        P(None, "tensor"),
        P(),
        P("tensor"),
        P(("groups", "seq")),
        P(("groups", "seq"), "tensor"),
        P(("groups", "seq")),
        P(("groups", "seq")),
    )
    out_specs = (P(("groups", "seq"), "tensor"), P(("groups", "seq"), "tensor"))
    return jax.shard_map(local, mesh=mesh, in_specs=in_specs, out_specs=out_specs, check_vma=False)
```

```python
import math

import jax
import jax.numpy as jnp
from jax import lax
from jax.experimental.layout import Layout, with_layout_constraint
from jax.sharding import PartitionSpec as P

STRETCH = 256
POOL_HEADS = 32


EPSILON = 1e-05
MASKED = -1e30


def passed_along(value, axis, steps):
    count = lax.axis_size(axis)
    leading, last = (max(0, -steps), min(count, count - steps))
    return lax.ppermute(value, axis, [(source, source + steps) for source in range(leading, last)])


def silu_act(values):
    return values / (1.0 + jnp.exp(-values))


def causal_conv(before, current, weights):
    kernel_width = weights.shape[0]
    length = current.shape[0]
    padded = jnp.concatenate([before, current], axis=0)
    summed = jnp.zeros(current.shape, jnp.float32)
    for offset in range(kernel_width):
        summed = summed + padded[offset : offset + length].astype(jnp.float32) * weights[
            offset
        ].astype(jnp.float32)
    return silu_act(summed).astype(jnp.bfloat16)


def stretch_local(x_block, b_block, c_block, step_block, keep_block):
    block_len = x_block.shape[0]
    cumul_keep = jnp.cumsum(keep_block, axis=1)
    lower_mask = lax.broadcasted_iota(jnp.int32, (block_len, block_len), 0) >= lax.broadcasted_iota(
        jnp.int32, (block_len, block_len), 1
    )
    inner_prod = jnp.einsum("is,js->ij", c_block, b_block, preferred_element_type=jnp.float32)
    spread = cumul_keep[:, :, None] - cumul_keep[:, None, :]
    decay_mask = jnp.where(lower_mask[None], jnp.exp(jnp.where(lower_mask[None], spread, 0.0)), 0.0)
    mixing = (decay_mask * inner_prod[None] * step_block[:, None, :]).astype(jnp.bfloat16)
    intra_part = jnp.einsum("hij,jhp->hpi", mixing, x_block, preferred_element_type=jnp.float32)
    tail_weight = jnp.exp(cumul_keep[:, -1:] - cumul_keep) * step_block
    weighted = (tail_weight.T[:, :, None] * x_block.astype(jnp.float32)).astype(jnp.bfloat16)
    stretch_state = jnp.einsum("jhp,js->hps", weighted, b_block, preferred_element_type=jnp.float32)
    return (intra_part, stretch_state, cumul_keep)


def combine(earlier, later):
    return (earlier[0] * jnp.exp(later[1])[:, None, None] + later[0], earlier[1] + later[1])


def exclusive_scan(state, decay, axis, rider):
    count = lax.axis_size(axis)
    window = (state, decay)
    before = (jnp.zeros_like(state), jnp.zeros_like(decay))
    shift = 1
    while shift < count:
        sent_state = passed_along(window[0].astype(jnp.bfloat16), axis, shift)
        sent_decay = passed_along(window[1], axis, shift)
        if shift == 1:
            sent_state, rider = lax.optimization_barrier((sent_state, rider))
        received = (sent_state.astype(jnp.float32), sent_decay)
        before = combine(received, before)
        if shift * 2 < count:
            window = combine(received, window)
        shift *= 2
    return before[0], rider


def butterfly_sum(value, axis):
    count = lax.axis_size(axis)
    if count & (count - 1):
        return lax.psum(value, axis)
    stride = 1
    while stride < count:
        partner = lax.ppermute(value, axis, [(i, i ^ stride) for i in range(count)])
        value = value + partner
        stride *= 2
    return value


def read_state(c_block, state_in):
    state_high = state_in.astype(jnp.bfloat16)
    state_low = (state_in - state_high.astype(jnp.float32)).astype(jnp.bfloat16)
    high_part = jnp.einsum("hps,is->hpi", state_high, c_block, preferred_element_type=jnp.float32)
    low_part = jnp.einsum("hps,is->hpi", state_low, c_block, preferred_element_type=jnp.float32)
    return high_part + low_part


def local(
    x_in,
    z_gate,
    bc_in,
    step_size,
    log_keep,
    skip_gain,
    conv_x,
    conv_bc,
    norm_gain,
    seg_ends,
    pool_query,
    pool_start,
    pool_stop,
):
    tok_rows = x_in.shape[0]
    channels = x_in.shape[1]
    heads_local = step_size.shape[0]
    head_width = channels // heads_local
    state_width = bc_in.shape[1] // 2
    rim_rows = conv_x.shape[0] - 1
    seq_count = lax.axis_size("seq")
    pools_local = pool_query.shape[0]
    bounds = jnp.stack([pool_start, pool_stop], axis=1)
    bounds_split = jnp.concatenate([bounds // 64, bounds % 64], axis=1).astype(jnp.bfloat16)
    query_rows = jnp.concatenate([pool_query, bounds_split], axis=1)
    query_rows = jnp.broadcast_to(query_rows[None], (seq_count,) + query_rows.shape)
    query_rows = lax.all_to_all(
        query_rows.reshape(seq_count * pools_local, -1), "seq", 0, 0, tiled=True
    )
    queries_all = query_rows[:, :channels]
    bounds_all = query_rows[:, channels:].astype(jnp.int32)
    start_all = bounds_all[:, 0] * 64 + bounds_all[:, 2]
    stop_all = bounds_all[:, 1] * 64 + bounds_all[:, 3]
    edge_rows = jnp.concatenate([x_in[tok_rows - rim_rows :], bc_in[tok_rows - rim_rows :]], axis=1)
    before = passed_along(edge_rows, "seq", 1)
    x_conv = causal_conv(before[:, :channels], x_in, conv_x)
    x_conv = with_layout_constraint(x_conv, Layout(major_to_minor=(0, 1)))
    bc_conv = causal_conv(before[:, channels:], bc_in, conv_bc)
    b_mat = bc_conv[:, :state_width]
    c_mat = bc_conv[:, state_width:]
    x_heads = x_conv.reshape(tok_rows, heads_local, head_width)
    stretch_count = tok_rows // STRETCH
    entry_state = jnp.zeros((heads_local, head_width, state_width), jnp.float32)
    decay_total = jnp.zeros((heads_local,), jnp.float32)
    saved_parts = []
    for block_index in range(stretch_count):
        first_row = block_index * STRETCH
        last_row = first_row + STRETCH
        intra_part, stretch_state, cumul_keep = stretch_local(
            x_heads[first_row:last_row],
            b_mat[first_row:last_row],
            c_mat[first_row:last_row],
            step_size[:, first_row:last_row],
            log_keep[:, first_row:last_row],
        )
        saved_parts.append((intra_part, cumul_keep, entry_state, decay_total))
        entry_state = jnp.exp(cumul_keep[:, -1])[:, None, None] * entry_state + stretch_state
        decay_total = decay_total + cumul_keep[:, -1]
    incoming, z_late = exclusive_scan(entry_state, decay_total, "seq", z_gate)
    x_major = x_conv.T.reshape(heads_local, head_width, tok_rows)
    z_major = z_late.T
    pieces_out = []
    for block_index in range(stretch_count):
        intra_part, cumul_keep, entry_part, decay_part = saved_parts[block_index]
        first_row = block_index * STRETCH
        state_in = entry_part + jnp.exp(decay_part)[:, None, None] * incoming
        from_state = read_state(c_mat[first_row : first_row + STRETCH], state_in)
        pieces_out.append(intra_part + jnp.exp(cumul_keep)[:, None, :] * from_state)
    ssd_out = jnp.concatenate(pieces_out, axis=2) + skip_gain[:, None, None] * x_major.astype(
        jnp.float32
    )
    gated = ssd_out.reshape(channels, tok_rows) * silu_act(z_major.astype(jnp.float32))
    gated = with_layout_constraint(gated, Layout(major_to_minor=(0, 1)))
    square_sum = butterfly_sum(jnp.sum(gated * gated, axis=0), "tensor")
    width_all = channels * lax.axis_size("tensor")
    row_scale = lax.rsqrt(square_sum / width_all + EPSILON)
    mixed_major = (gated * row_scale[None, :] * norm_gain[:, None]).astype(jnp.bfloat16)
    mixed_seq = mixed_major.T
    local_ends = seg_ends - lax.axis_index("seq") * tok_rows
    summaries = (
        jnp.take(gated, local_ends, axis=1)
        * jnp.take(row_scale, local_ends)[None, :]
        * norm_gain[:, None]
    ).astype(jnp.bfloat16).T
    pool_heads_local = POOL_HEADS // lax.axis_size("tensor")
    pool_width = channels // pool_heads_local
    scale_factor = 1.0 / math.sqrt(pool_width)
    pools_all = queries_all.shape[0]
    segs_local = summaries.shape[0]
    queries = queries_all.reshape(pools_all, pool_heads_local, pool_width)
    seg_index = lax.axis_index("seq") * segs_local + lax.iota(jnp.int32, segs_local)
    inside = (seg_index[None, :] >= start_all[:, None]) & (seg_index[None, :] < stop_all[:, None])
    keys_block = summaries.reshape(segs_local, pool_heads_local, pool_width)
    logits = (
        jnp.einsum("pad,rad->apr", queries, keys_block, preferred_element_type=jnp.float32)
        * scale_factor
    )
    logits = jnp.where(inside[None], logits, MASKED)
    peak = jnp.max(logits, axis=2).astype(jnp.bfloat16).astype(jnp.float32)
    expo = jnp.where(inside[None], jnp.exp(logits - peak[:, :, None]), 0.0)
    denom = jnp.sum(expo, axis=2)
    numer = jnp.einsum(
        "apr,rad->pad", expo.astype(jnp.bfloat16), keys_block, preferred_element_type=jnp.float32
    )
    denom_high = denom.astype(jnp.bfloat16)
    denom_low = (denom - denom_high.astype(jnp.float32)).astype(jnp.bfloat16)
    parts = jnp.concatenate(
        [
            numer.reshape(pools_all, channels).astype(jnp.bfloat16),
            peak.T.astype(jnp.bfloat16),
            denom_high.T,
            denom_low.T,
        ],
        axis=1,
    )
    parts = parts.reshape(seq_count, pools_local, channels + 3 * pool_heads_local)
    place = lax.axis_index("seq")
    gathered = [lax.dynamic_index_in_dim(parts, place, 0, False)]
    for shift in range(1, seq_count):
        chunk = lax.dynamic_index_in_dim(parts, (place + shift) % seq_count, 0, False)
        gathered.append(
            lax.ppermute(
                chunk, "seq", [(i, (i + shift) % seq_count) for i in range(seq_count)]
            )
        )
    parts = jnp.stack(gathered).astype(jnp.float32)
    numer_parts = parts[:, :, :channels].reshape(
        seq_count, pools_local, pool_heads_local, pool_width
    )
    stats_parts = parts[:, :, channels:].reshape(seq_count, pools_local, 3, pool_heads_local)
    peak_parts = stats_parts[:, :, 0]
    denom_parts = stats_parts[:, :, 1] + stats_parts[:, :, 2]
    peak_all = jnp.max(peak_parts, axis=0)
    rescale = jnp.exp(peak_parts - peak_all[None])
    denom_all = jnp.sum(rescale * denom_parts, axis=0)
    numer_all = jnp.sum(rescale[:, :, :, None] * numer_parts, axis=0)
    pooled = (numer_all / denom_all[:, :, None]).reshape(pools_local, channels)
    return (mixed_seq, pooled)


def solution(mesh):
    in_specs = (
        P(("groups", "seq"), "tensor"),
        P(("groups", "seq"), "tensor"),
        P(("groups", "seq"), None),
        P("tensor", ("groups", "seq")),
        P("tensor", ("groups", "seq")),
        P("tensor"),
        P(None, "tensor"),
        P(),
        P("tensor"),
        P(("groups", "seq")),
        P(("groups", "seq"), "tensor"),
        P(("groups", "seq")),
        P(("groups", "seq")),
    )
    out_specs = (P(("groups", "seq"), "tensor"), P(("groups", "seq"), "tensor"))
    return jax.shard_map(local, mesh=mesh, in_specs=in_specs, out_specs=out_specs, check_vma=False)
```

```python
import math

import jax
import jax.numpy as jnp
from jax import lax
from jax.experimental.layout import Layout, with_layout_constraint
from jax.sharding import PartitionSpec as P

STRETCH = 256
POOL_HEADS = 32


EPSILON = 1e-05
MASKED = -1e30


def passed_along(value, axis, steps):
    count = lax.axis_size(axis)
    leading, last = (max(0, -steps), min(count, count - steps))
    return lax.ppermute(value, axis, [(source, source + steps) for source in range(leading, last)])


def silu_act(values):
    return values / (1.0 + jnp.exp(-values))


def causal_conv(before, current, weights):
    kernel_width = weights.shape[0]
    length = current.shape[0]
    padded = jnp.concatenate([before, current], axis=0)
    summed = jnp.zeros(current.shape, jnp.float32)
    for offset in range(kernel_width):
        summed = summed + padded[offset : offset + length].astype(jnp.float32) * weights[
            offset
        ].astype(jnp.float32)
    return silu_act(summed).astype(jnp.bfloat16)


def stretch_local(x_block, b_block, c_block, step_block, keep_block):
    block_len = x_block.shape[0]
    cumul_keep = jnp.cumsum(keep_block, axis=1)
    lower_mask = lax.broadcasted_iota(jnp.int32, (block_len, block_len), 0) >= lax.broadcasted_iota(
        jnp.int32, (block_len, block_len), 1
    )
    inner_prod = jnp.einsum("is,js->ij", c_block, b_block, preferred_element_type=jnp.float32)
    spread = cumul_keep[:, :, None] - cumul_keep[:, None, :]
    decay_mask = jnp.where(lower_mask[None], jnp.exp(jnp.where(lower_mask[None], spread, 0.0)), 0.0)
    mixing = (decay_mask * inner_prod[None] * step_block[:, None, :]).astype(jnp.bfloat16)
    intra_part = jnp.einsum("hij,jhp->hpi", mixing, x_block, preferred_element_type=jnp.float32)
    tail_weight = jnp.exp(cumul_keep[:, -1:] - cumul_keep) * step_block
    weighted = (tail_weight.T[:, :, None] * x_block.astype(jnp.float32)).astype(jnp.bfloat16)
    stretch_state = jnp.einsum("jhp,js->hps", weighted, b_block, preferred_element_type=jnp.float32)
    return (intra_part, stretch_state, cumul_keep)


def combine(earlier, later):
    return (earlier[0] * jnp.exp(later[1])[:, None, None] + later[0], earlier[1] + later[1])


def exclusive_scan(state, decay, axis, rider):
    count = lax.axis_size(axis)
    window = (state, decay)
    before = (jnp.zeros_like(state), jnp.zeros_like(decay))
    shift = 1
    while shift < count:
        sent_state = passed_along(window[0].astype(jnp.bfloat16), axis, shift)
        sent_decay = passed_along(window[1], axis, shift)
        if shift == 1:
            sent_state, rider = lax.optimization_barrier((sent_state, rider))
        received = (sent_state.astype(jnp.float32), sent_decay)
        before = combine(received, before)
        if shift * 2 < count:
            window = combine(received, window)
        shift *= 2
    return before[0], rider


def butterfly_sum(value, axis):
    count = lax.axis_size(axis)
    if count & (count - 1):
        return lax.psum(value, axis)
    stride = 1
    while stride < count:
        partner = lax.ppermute(value, axis, [(i, i ^ stride) for i in range(count)])
        value = value + partner
        stride *= 2
    return value


def read_state(c_block, state_in):
    state_high = state_in.astype(jnp.bfloat16)
    state_low = (state_in - state_high.astype(jnp.float32)).astype(jnp.bfloat16)
    high_part = jnp.einsum("hps,is->hpi", state_high, c_block, preferred_element_type=jnp.float32)
    low_part = jnp.einsum("hps,is->hpi", state_low, c_block, preferred_element_type=jnp.float32)
    return high_part + low_part


def local(
    x_in,
    z_gate,
    bc_in,
    step_size,
    log_keep,
    skip_gain,
    conv_x,
    conv_bc,
    norm_gain,
    seg_ends,
    pool_query,
    pool_start,
    pool_stop,
):
    tok_rows = x_in.shape[0]
    channels = x_in.shape[1]
    heads_local = step_size.shape[0]
    head_width = channels // heads_local
    state_width = bc_in.shape[1] // 2
    rim_rows = conv_x.shape[0] - 1
    seq_count = lax.axis_size("seq")
    pools_local = pool_query.shape[0]
    bounds = jnp.stack([pool_start, pool_stop], axis=1)
    bounds_split = jnp.concatenate([bounds // 64, bounds % 64], axis=1).astype(jnp.bfloat16)
    query_rows = jnp.concatenate([pool_query, bounds_split], axis=1)
    query_rows = jnp.broadcast_to(query_rows[None], (seq_count,) + query_rows.shape)
    query_rows = lax.all_to_all(
        query_rows.reshape(seq_count * pools_local, -1), "seq", 0, 0, tiled=True
    )
    queries_all = query_rows[:, :channels]
    bounds_all = query_rows[:, channels:].astype(jnp.int32)
    start_all = bounds_all[:, 0] * 64 + bounds_all[:, 2]
    stop_all = bounds_all[:, 1] * 64 + bounds_all[:, 3]
    edge_rows = jnp.concatenate([x_in[tok_rows - rim_rows :], bc_in[tok_rows - rim_rows :]], axis=1)
    before = passed_along(edge_rows, "seq", 1)
    x_conv = causal_conv(before[:, :channels], x_in, conv_x)
    x_conv = with_layout_constraint(x_conv, Layout(major_to_minor=(0, 1)))
    bc_conv = causal_conv(before[:, channels:], bc_in, conv_bc)
    b_mat = bc_conv[:, :state_width]
    c_mat = bc_conv[:, state_width:]
    x_heads = x_conv.reshape(tok_rows, heads_local, head_width)
    stretch_count = tok_rows // STRETCH
    entry_state = jnp.zeros((heads_local, head_width, state_width), jnp.float32)
    decay_total = jnp.zeros((heads_local,), jnp.float32)
    saved_parts = []
    for block_index in range(stretch_count):
        first_row = block_index * STRETCH
        last_row = first_row + STRETCH
        intra_part, stretch_state, cumul_keep = stretch_local(
            x_heads[first_row:last_row],
            b_mat[first_row:last_row],
            c_mat[first_row:last_row],
            step_size[:, first_row:last_row],
            log_keep[:, first_row:last_row],
        )
        saved_parts.append((intra_part, cumul_keep, entry_state, decay_total))
        entry_state = jnp.exp(cumul_keep[:, -1])[:, None, None] * entry_state + stretch_state
        decay_total = decay_total + cumul_keep[:, -1]
    incoming, z_late = exclusive_scan(entry_state, decay_total, "seq", z_gate)
    x_major = x_conv.T.reshape(heads_local, head_width, tok_rows)
    z_major = z_late.T
    pieces_out = []
    for block_index in range(stretch_count):
        intra_part, cumul_keep, entry_part, decay_part = saved_parts[block_index]
        first_row = block_index * STRETCH
        state_in = entry_part + jnp.exp(decay_part)[:, None, None] * incoming
        from_state = read_state(c_mat[first_row : first_row + STRETCH], state_in)
        pieces_out.append(intra_part + jnp.exp(cumul_keep)[:, None, :] * from_state)
    ssd_out = jnp.concatenate(pieces_out, axis=2) + skip_gain[:, None, None] * x_major.astype(
        jnp.float32
    )
    gated = ssd_out.reshape(channels, tok_rows) * silu_act(z_major.astype(jnp.float32))
    gated = with_layout_constraint(gated, Layout(major_to_minor=(0, 1)))
    square_sum = butterfly_sum(jnp.sum(gated * gated, axis=0), "tensor")
    width_all = channels * lax.axis_size("tensor")
    mixed_major = (
        gated * lax.rsqrt(square_sum / width_all + EPSILON)[None, :] * norm_gain[:, None]
    ).astype(jnp.bfloat16)
    mixed_seq = mixed_major.T
    local_ends = seg_ends - lax.axis_index("seq") * tok_rows
    picks = (
        lax.broadcasted_iota(jnp.int32, (tok_rows, local_ends.shape[0]), 0) == local_ends[None, :]
    ).astype(jnp.bfloat16)
    summaries = (
        jnp.einsum("ct,ts->sc", mixed_major, picks, preferred_element_type=jnp.float32)
    ).astype(jnp.bfloat16)
    pool_heads_local = POOL_HEADS // lax.axis_size("tensor")
    pool_width = channels // pool_heads_local
    scale_factor = 1.0 / math.sqrt(pool_width)
    pools_all = queries_all.shape[0]
    segs_local = summaries.shape[0]
    queries = queries_all.reshape(pools_all, pool_heads_local, pool_width)
    seg_index = lax.axis_index("seq") * segs_local + lax.iota(jnp.int32, segs_local)
    inside = (seg_index[None, :] >= start_all[:, None]) & (seg_index[None, :] < stop_all[:, None])
    keys_block = summaries.reshape(segs_local, pool_heads_local, pool_width)
    logits = (
        jnp.einsum("pad,rad->apr", queries, keys_block, preferred_element_type=jnp.float32)
        * scale_factor
    )
    logits = jnp.where(inside[None], logits, MASKED)
    peak = jnp.max(logits, axis=2).astype(jnp.bfloat16).astype(jnp.float32)
    expo = jnp.where(inside[None], jnp.exp(logits - peak[:, :, None]), 0.0)
    denom = jnp.sum(expo, axis=2)
    numer = jnp.einsum(
        "apr,rad->pad", expo.astype(jnp.bfloat16), keys_block, preferred_element_type=jnp.float32
    )
    denom_high = denom.astype(jnp.bfloat16)
    denom_low = (denom - denom_high.astype(jnp.float32)).astype(jnp.bfloat16)
    parts = jnp.concatenate(
        [
            numer.reshape(pools_all, channels).astype(jnp.bfloat16),
            peak.T.astype(jnp.bfloat16),
            denom_high.T,
            denom_low.T,
        ],
        axis=1,
    )
    parts = parts.reshape(seq_count, pools_local, channels + 3 * pool_heads_local)
    place = lax.axis_index("seq")
    gathered = [lax.dynamic_index_in_dim(parts, place, 0, False)]
    for shift in range(1, seq_count):
        chunk = lax.dynamic_index_in_dim(parts, (place + shift) % seq_count, 0, False)
        gathered.append(
            lax.ppermute(
                chunk, "seq", [(i, (i + shift) % seq_count) for i in range(seq_count)]
            )
        )
    parts = jnp.stack(gathered).astype(jnp.float32)
    numer_parts = parts[:, :, :channels].reshape(
        seq_count, pools_local, pool_heads_local, pool_width
    )
    stats_parts = parts[:, :, channels:].reshape(seq_count, pools_local, 3, pool_heads_local)
    peak_parts = stats_parts[:, :, 0]
    denom_parts = stats_parts[:, :, 1] + stats_parts[:, :, 2]
    peak_all = jnp.max(peak_parts, axis=0)
    rescale = jnp.exp(peak_parts - peak_all[None])
    denom_all = jnp.sum(rescale * denom_parts, axis=0)
    numer_all = jnp.sum(rescale[:, :, :, None] * numer_parts, axis=0)
    pooled = (numer_all / denom_all[:, :, None]).reshape(pools_local, channels)
    return (mixed_seq, pooled)


def solution(mesh):
    in_specs = (
        P(("groups", "seq"), "tensor"),
        P(("groups", "seq"), "tensor"),
        P(("groups", "seq"), None),
        P("tensor", ("groups", "seq")),
        P("tensor", ("groups", "seq")),
        P("tensor"),
        P(None, "tensor"),
        P(),
        P("tensor"),
        P(("groups", "seq")),
        P(("groups", "seq"), "tensor"),
        P(("groups", "seq")),
        P(("groups", "seq")),
    )
    out_specs = (P(("groups", "seq"), "tensor"), P(("groups", "seq"), "tensor"))
    return jax.shard_map(local, mesh=mesh, in_specs=in_specs, out_specs=out_specs, check_vma=False)
```

```python
import math

import jax
import jax.numpy as jnp
from jax import lax
from jax.experimental.layout import Layout, with_layout_constraint
from jax.sharding import PartitionSpec as P

STRETCH = 256
POOL_HEADS = 32


EPSILON = 1e-05
MASKED = -1e30


def passed_along(value, axis, steps):
    count = lax.axis_size(axis)
    leading, last = (max(0, -steps), min(count, count - steps))
    return lax.ppermute(value, axis, [(source, source + steps) for source in range(leading, last)])


def silu_act(values):
    return values / (1.0 + jnp.exp(-values))


def causal_conv(before, current, weights):
    kernel_width = weights.shape[0]
    length = current.shape[0]
    padded = jnp.concatenate([before, current], axis=0)
    summed = jnp.zeros(current.shape, jnp.float32)
    for offset in range(kernel_width):
        summed = summed + padded[offset : offset + length].astype(jnp.float32) * weights[
            offset
        ].astype(jnp.float32)
    return silu_act(summed).astype(jnp.bfloat16)


def stretch_local(x_block, b_block, c_block, step_block, keep_block):
    block_len = x_block.shape[0]
    cumul_keep = jnp.cumsum(keep_block, axis=1)
    lower_mask = lax.broadcasted_iota(jnp.int32, (block_len, block_len), 0) >= lax.broadcasted_iota(
        jnp.int32, (block_len, block_len), 1
    )
    inner_prod = jnp.einsum("is,js->ij", c_block, b_block, preferred_element_type=jnp.float32)
    spread = cumul_keep[:, :, None] - cumul_keep[:, None, :]
    decay_mask = jnp.where(lower_mask[None], jnp.exp(jnp.where(lower_mask[None], spread, 0.0)), 0.0)
    mixing = (decay_mask * inner_prod[None] * step_block[:, None, :]).astype(jnp.bfloat16)
    intra_part = jnp.einsum("hij,jhp->hpi", mixing, x_block, preferred_element_type=jnp.float32)
    tail_weight = jnp.exp(cumul_keep[:, -1:] - cumul_keep) * step_block
    weighted = (tail_weight.T[:, :, None] * x_block.astype(jnp.float32)).astype(jnp.bfloat16)
    stretch_state = jnp.einsum("jhp,js->hps", weighted, b_block, preferred_element_type=jnp.float32)
    return (intra_part, stretch_state, cumul_keep)


def combine(earlier, later):
    return (earlier[0] * jnp.exp(later[1])[:, None, None] + later[0], earlier[1] + later[1])


def exclusive_scan(state, decays_all, axis, rider):
    count = lax.axis_size(axis)
    place = lax.axis_index(axis)
    order = lax.iota(jnp.int32, count)

    def span_decay(first, last):
        inside = (order >= first) & (order <= last)
        return jnp.sum(jnp.where(inside[:, None], decays_all, 0.0), axis=0)

    window = state
    before = jnp.zeros_like(state)
    shift = 1
    while shift < count:
        received = passed_along(window.astype(jnp.bfloat16), axis, shift)
        if shift == 1:
            received, rider = lax.optimization_barrier((received, rider))
        received = received.astype(jnp.float32)
        before_decay = span_decay(place - shift + 1, place - 1)
        before = received * jnp.exp(before_decay)[:, None, None] + before
        if shift * 2 < count:
            window_decay = span_decay(place - shift + 1, place)
            window = received * jnp.exp(window_decay)[:, None, None] + window
        shift *= 2
    return before, rider


def butterfly_sum(value, axis):
    count = lax.axis_size(axis)
    if count & (count - 1):
        return lax.psum(value, axis)
    stride = 1
    while stride < count:
        partner = lax.ppermute(value, axis, [(i, i ^ stride) for i in range(count)])
        value = value + partner
        stride *= 2
    return value


def read_state(c_block, state_in):
    state_high = state_in.astype(jnp.bfloat16)
    state_low = (state_in - state_high.astype(jnp.float32)).astype(jnp.bfloat16)
    high_part = jnp.einsum("hps,is->hpi", state_high, c_block, preferred_element_type=jnp.float32)
    low_part = jnp.einsum("hps,is->hpi", state_low, c_block, preferred_element_type=jnp.float32)
    return high_part + low_part


def local(
    x_in,
    z_gate,
    bc_in,
    step_size,
    log_keep,
    skip_gain,
    conv_x,
    conv_bc,
    norm_gain,
    seg_ends,
    pool_query,
    pool_start,
    pool_stop,
):
    tok_rows = x_in.shape[0]
    channels = x_in.shape[1]
    heads_local = step_size.shape[0]
    head_width = channels // heads_local
    state_width = bc_in.shape[1] // 2
    rim_rows = conv_x.shape[0] - 1
    seq_count = lax.axis_size("seq")
    pools_local = pool_query.shape[0]
    decay_local = jnp.sum(log_keep, axis=1)
    decay_high = decay_local.astype(jnp.bfloat16)
    decay_rest = decay_local - decay_high.astype(jnp.float32)
    decay_mid = decay_rest.astype(jnp.bfloat16)
    decay_low = (decay_rest - decay_mid.astype(jnp.float32)).astype(jnp.bfloat16)
    bounds = jnp.stack([pool_start, pool_stop], axis=1)
    bounds_split = jnp.concatenate([bounds // 64, bounds % 64], axis=1).astype(jnp.bfloat16)
    query_rows = jnp.concatenate([pool_query, bounds_split], axis=1)
    query_width = query_rows.shape[1]
    decay_row = jnp.concatenate([decay_high, decay_mid, decay_low])
    decay_row = jnp.pad(decay_row, (0, query_width - decay_row.shape[0]))
    query_rows = jnp.concatenate([query_rows, decay_row[None, :]], axis=0)
    query_rows = jnp.broadcast_to(query_rows[None], (seq_count,) + query_rows.shape)
    query_rows = lax.all_to_all(
        query_rows.reshape(seq_count * (pools_local + 1), -1), "seq", 0, 0, tiled=True
    ).reshape(seq_count, pools_local + 1, query_width)
    decay_parts = query_rows[:, pools_local, : 3 * heads_local].astype(jnp.float32)
    decays_all = (
        decay_parts[:, :heads_local]
        + decay_parts[:, heads_local : 2 * heads_local]
        + decay_parts[:, 2 * heads_local :]
    )
    query_rows = query_rows[:, :pools_local].reshape(seq_count * pools_local, query_width)
    queries_all = query_rows[:, :channels]
    bounds_all = query_rows[:, channels:].astype(jnp.int32)
    start_all = bounds_all[:, 0] * 64 + bounds_all[:, 2]
    stop_all = bounds_all[:, 1] * 64 + bounds_all[:, 3]
    edge_rows = jnp.concatenate([x_in[tok_rows - rim_rows :], bc_in[tok_rows - rim_rows :]], axis=1)
    before = passed_along(edge_rows, "seq", 1)
    x_conv = causal_conv(before[:, :channels], x_in, conv_x)
    x_conv = with_layout_constraint(x_conv, Layout(major_to_minor=(0, 1)))
    bc_conv = causal_conv(before[:, channels:], bc_in, conv_bc)
    b_mat = bc_conv[:, :state_width]
    c_mat = bc_conv[:, state_width:]
    x_heads = x_conv.reshape(tok_rows, heads_local, head_width)
    stretch_count = tok_rows // STRETCH
    entry_state = jnp.zeros((heads_local, head_width, state_width), jnp.float32)
    decay_total = jnp.zeros((heads_local,), jnp.float32)
    saved_parts = []
    for block_index in range(stretch_count):
        first_row = block_index * STRETCH
        last_row = first_row + STRETCH
        intra_part, stretch_state, cumul_keep = stretch_local(
            x_heads[first_row:last_row],
            b_mat[first_row:last_row],
            c_mat[first_row:last_row],
            step_size[:, first_row:last_row],
            log_keep[:, first_row:last_row],
        )
        saved_parts.append((intra_part, cumul_keep, entry_state, decay_total))
        entry_state = jnp.exp(cumul_keep[:, -1])[:, None, None] * entry_state + stretch_state
        decay_total = decay_total + cumul_keep[:, -1]
    incoming, z_late = exclusive_scan(entry_state, decays_all, "seq", z_gate)
    x_major = x_conv.T.reshape(heads_local, head_width, tok_rows)
    z_major = z_late.T
    pieces_out = []
    for block_index in range(stretch_count):
        intra_part, cumul_keep, entry_part, decay_part = saved_parts[block_index]
        first_row = block_index * STRETCH
        state_in = entry_part + jnp.exp(decay_part)[:, None, None] * incoming
        from_state = read_state(c_mat[first_row : first_row + STRETCH], state_in)
        pieces_out.append(intra_part + jnp.exp(cumul_keep)[:, None, :] * from_state)
    ssd_out = jnp.concatenate(pieces_out, axis=2) + skip_gain[:, None, None] * x_major.astype(
        jnp.float32
    )
    gated = ssd_out.reshape(channels, tok_rows) * silu_act(z_major.astype(jnp.float32))
    gated = with_layout_constraint(gated, Layout(major_to_minor=(0, 1)))
    square_sum = butterfly_sum(jnp.sum(gated * gated, axis=0), "tensor")
    width_all = channels * lax.axis_size("tensor")
    mixed_major = (
        gated * lax.rsqrt(square_sum / width_all + EPSILON)[None, :] * norm_gain[:, None]
    ).astype(jnp.bfloat16)
    mixed_seq = mixed_major.T
    local_ends = seg_ends - lax.axis_index("seq") * tok_rows
    summaries = jnp.take(mixed_seq, local_ends, axis=0)
    pool_heads_local = POOL_HEADS // lax.axis_size("tensor")
    pool_width = channels // pool_heads_local
    scale_factor = 1.0 / math.sqrt(pool_width)
    pools_all = queries_all.shape[0]
    segs_local = summaries.shape[0]
    queries = queries_all.reshape(pools_all, pool_heads_local, pool_width)
    seg_index = lax.axis_index("seq") * segs_local + lax.iota(jnp.int32, segs_local)
    inside = (seg_index[None, :] >= start_all[:, None]) & (seg_index[None, :] < stop_all[:, None])
    keys_block = summaries.reshape(segs_local, pool_heads_local, pool_width)
    logits = (
        jnp.einsum("pad,rad->apr", queries, keys_block, preferred_element_type=jnp.float32)
        * scale_factor
    )
    logits = jnp.where(inside[None], logits, MASKED)
    peak = jnp.max(logits, axis=2).astype(jnp.bfloat16).astype(jnp.float32)
    expo = jnp.where(inside[None], jnp.exp(logits - peak[:, :, None]), 0.0)
    denom = jnp.sum(expo, axis=2)
    numer = jnp.einsum(
        "apr,rad->pad", expo.astype(jnp.bfloat16), keys_block, preferred_element_type=jnp.float32
    )
    denom_high = denom.astype(jnp.bfloat16)
    denom_low = (denom - denom_high.astype(jnp.float32)).astype(jnp.bfloat16)
    parts = jnp.concatenate(
        [
            numer.reshape(pools_all, channels).astype(jnp.bfloat16),
            peak.T.astype(jnp.bfloat16),
            denom_high.T,
            denom_low.T,
        ],
        axis=1,
    )
    parts = parts.reshape(seq_count, pools_local, channels + 3 * pool_heads_local)
    place = lax.axis_index("seq")
    gathered = [lax.dynamic_index_in_dim(parts, place, 0, False)]
    for shift in range(1, seq_count):
        chunk = lax.dynamic_index_in_dim(parts, (place + shift) % seq_count, 0, False)
        gathered.append(
            lax.ppermute(
                chunk, "seq", [(i, (i + shift) % seq_count) for i in range(seq_count)]
            )
        )
    parts = jnp.stack(gathered).astype(jnp.float32)
    numer_parts = parts[:, :, :channels].reshape(
        seq_count, pools_local, pool_heads_local, pool_width
    )
    stats_parts = parts[:, :, channels:].reshape(seq_count, pools_local, 3, pool_heads_local)
    peak_parts = stats_parts[:, :, 0]
    denom_parts = stats_parts[:, :, 1] + stats_parts[:, :, 2]
    peak_all = jnp.max(peak_parts, axis=0)
    rescale = jnp.exp(peak_parts - peak_all[None])
    denom_all = jnp.sum(rescale * denom_parts, axis=0)
    numer_all = jnp.sum(rescale[:, :, :, None] * numer_parts, axis=0)
    pooled = (numer_all / denom_all[:, :, None]).reshape(pools_local, channels)
    return (mixed_seq, pooled)


def solution(mesh):
    in_specs = (
        P(("groups", "seq"), "tensor"),
        P(("groups", "seq"), "tensor"),
        P(("groups", "seq"), None),
        P("tensor", ("groups", "seq")),
        P("tensor", ("groups", "seq")),
        P("tensor"),
        P(None, "tensor"),
        P(),
        P("tensor"),
        P(("groups", "seq")),
        P(("groups", "seq"), "tensor"),
        P(("groups", "seq")),
        P(("groups", "seq")),
    )
    out_specs = (P(("groups", "seq"), "tensor"), P(("groups", "seq"), "tensor"))
    return jax.shard_map(local, mesh=mesh, in_specs=in_specs, out_specs=out_specs, check_vma=False)
```

```python
import math

import jax
import jax.numpy as jnp
from jax import lax
from jax.experimental.layout import Layout, with_layout_constraint
from jax.sharding import PartitionSpec as P

STRETCH = 256
POOL_HEADS = 32


EPSILON = 1e-05
MASKED = -1e30


def passed_along(value, axis, steps):
    count = lax.axis_size(axis)
    leading, last = (max(0, -steps), min(count, count - steps))
    return lax.ppermute(value, axis, [(source, source + steps) for source in range(leading, last)])


def silu_act(values):
    return values / (1.0 + jnp.exp(-values))


def causal_conv(before, current, weights):
    kernel_width = weights.shape[0]
    length = current.shape[0]
    padded = jnp.concatenate([before, current], axis=0)
    summed = jnp.zeros(current.shape, jnp.float32)
    for offset in range(kernel_width):
        summed = summed + padded[offset : offset + length].astype(jnp.float32) * weights[
            offset
        ].astype(jnp.float32)
    return silu_act(summed).astype(jnp.bfloat16)


def stretch_local(x_block, b_block, c_block, step_block, keep_block):
    block_len = x_block.shape[0]
    cumul_keep = jnp.cumsum(keep_block, axis=1)
    lower_mask = lax.broadcasted_iota(jnp.int32, (block_len, block_len), 0) >= lax.broadcasted_iota(
        jnp.int32, (block_len, block_len), 1
    )
    inner_prod = jnp.einsum("is,js->ij", c_block, b_block, preferred_element_type=jnp.float32)
    spread = cumul_keep[:, :, None] - cumul_keep[:, None, :]
    decay_mask = jnp.where(lower_mask[None], jnp.exp(jnp.where(lower_mask[None], spread, 0.0)), 0.0)
    mixing = (decay_mask * inner_prod[None] * step_block[:, None, :]).astype(jnp.bfloat16)
    intra_part = jnp.einsum("hij,jhp->hpi", mixing, x_block, preferred_element_type=jnp.float32)
    tail_weight = jnp.exp(cumul_keep[:, -1:] - cumul_keep) * step_block
    weighted = (tail_weight.T[:, :, None] * x_block.astype(jnp.float32)).astype(jnp.bfloat16)
    stretch_state = jnp.einsum("jhp,js->hps", weighted, b_block, preferred_element_type=jnp.float32)
    return (intra_part, stretch_state, cumul_keep)


def combine(earlier, later):
    return (earlier[0] * jnp.exp(later[1])[:, None, None] + later[0], earlier[1] + later[1])


def exclusive_scan(state, decay, axis, rider):
    count = lax.axis_size(axis)
    window = (state, decay)
    before = (jnp.zeros_like(state), jnp.zeros_like(decay))
    shift = 1
    while shift < count:
        sent_state = passed_along(window[0].astype(jnp.bfloat16), axis, shift)
        sent_decay = passed_along(window[1], axis, shift)
        if shift == 1:
            sent_state, rider = lax.optimization_barrier((sent_state, rider))
        received = (sent_state.astype(jnp.float32), sent_decay)
        before = combine(received, before)
        if shift * 2 < count:
            window = combine(received, window)
        shift *= 2
    return before[0], rider


def butterfly_sum(value, axis):
    count = lax.axis_size(axis)
    if count & (count - 1):
        return lax.psum(value, axis)
    stride = 1
    while stride < count:
        partner = lax.ppermute(value, axis, [(i, i ^ stride) for i in range(count)])
        value = value + partner
        stride *= 2
    return value


def read_state(c_block, state_in):
    state_high = state_in.astype(jnp.bfloat16)
    state_low = (state_in - state_high.astype(jnp.float32)).astype(jnp.bfloat16)
    high_part = jnp.einsum("hps,is->hpi", state_high, c_block, preferred_element_type=jnp.float32)
    low_part = jnp.einsum("hps,is->hpi", state_low, c_block, preferred_element_type=jnp.float32)
    return high_part + low_part


def local(
    x_in,
    z_gate,
    bc_in,
    step_size,
    log_keep,
    skip_gain,
    conv_x,
    conv_bc,
    norm_gain,
    seg_ends,
    pool_query,
    pool_start,
    pool_stop,
):
    tok_rows = x_in.shape[0]
    channels = x_in.shape[1]
    heads_local = step_size.shape[0]
    head_width = channels // heads_local
    state_width = bc_in.shape[1] // 2
    rim_rows = conv_x.shape[0] - 1
    seq_count = lax.axis_size("seq")
    pools_local = pool_query.shape[0]
    bounds = jnp.stack([pool_start, pool_stop], axis=1)
    bounds_split = jnp.concatenate([bounds // 64, bounds % 64], axis=1).astype(jnp.bfloat16)
    query_rows = jnp.concatenate([pool_query, bounds_split], axis=1)
    query_rows = jnp.broadcast_to(query_rows[None], (seq_count,) + query_rows.shape)
    query_rows = lax.all_to_all(
        query_rows.reshape(seq_count * pools_local, -1), "seq", 0, 0, tiled=True
    )
    queries_all = query_rows[:, :channels]
    bounds_all = query_rows[:, channels:].astype(jnp.int32)
    start_all = bounds_all[:, 0] * 64 + bounds_all[:, 2]
    stop_all = bounds_all[:, 1] * 64 + bounds_all[:, 3]
    edge_rows = jnp.concatenate([x_in[tok_rows - rim_rows :], bc_in[tok_rows - rim_rows :]], axis=1)
    before = passed_along(edge_rows, "seq", 1)
    x_conv = causal_conv(before[:, :channels], x_in, conv_x)
    x_conv = with_layout_constraint(x_conv, Layout(major_to_minor=(0, 1)))
    bc_conv = causal_conv(before[:, channels:], bc_in, conv_bc)
    b_mat = bc_conv[:, :state_width]
    c_mat = bc_conv[:, state_width:]
    x_heads = x_conv.reshape(tok_rows, heads_local, head_width)
    stretch_count = tok_rows // STRETCH
    entry_state = jnp.zeros((heads_local, head_width, state_width), jnp.float32)
    decay_total = jnp.zeros((heads_local,), jnp.float32)
    saved_parts = []
    for block_index in range(stretch_count):
        first_row = block_index * STRETCH
        last_row = first_row + STRETCH
        intra_part, stretch_state, cumul_keep = stretch_local(
            x_heads[first_row:last_row],
            b_mat[first_row:last_row],
            c_mat[first_row:last_row],
            step_size[:, first_row:last_row],
            log_keep[:, first_row:last_row],
        )
        saved_parts.append((intra_part, cumul_keep, entry_state, decay_total))
        entry_state = jnp.exp(cumul_keep[:, -1])[:, None, None] * entry_state + stretch_state
        decay_total = decay_total + cumul_keep[:, -1]
    incoming, z_late = exclusive_scan(entry_state, decay_total, "seq", z_gate)
    x_major = x_conv.T.reshape(heads_local, head_width, tok_rows)
    z_major = z_late.T
    pieces_out = []
    for block_index in range(stretch_count):
        intra_part, cumul_keep, entry_part, decay_part = saved_parts[block_index]
        first_row = block_index * STRETCH
        state_in = entry_part + jnp.exp(decay_part)[:, None, None] * incoming
        from_state = read_state(c_mat[first_row : first_row + STRETCH], state_in)
        pieces_out.append(intra_part + jnp.exp(cumul_keep)[:, None, :] * from_state)
    ssd_out = jnp.concatenate(pieces_out, axis=2) + skip_gain[:, None, None] * x_major.astype(
        jnp.float32
    )
    gated = ssd_out.reshape(channels, tok_rows) * silu_act(z_major.astype(jnp.float32))
    gated = with_layout_constraint(gated, Layout(major_to_minor=(0, 1)))
    square_sum = butterfly_sum(jnp.sum(gated * gated, axis=0), "tensor")
    width_all = channels * lax.axis_size("tensor")
    mixed_major = (
        gated * lax.rsqrt(square_sum / width_all + EPSILON)[None, :] * norm_gain[:, None]
    ).astype(jnp.bfloat16)
    mixed_seq = mixed_major.T
    local_ends = seg_ends - lax.axis_index("seq") * tok_rows
    summaries = jnp.take(mixed_seq, local_ends, axis=0)
    pool_heads_local = POOL_HEADS // lax.axis_size("tensor")
    pool_width = channels // pool_heads_local
    scale_factor = 1.0 / math.sqrt(pool_width)
    pools_all = queries_all.shape[0]
    segs_local = summaries.shape[0]
    seg_index = lax.axis_index("seq") * segs_local + lax.iota(jnp.int32, segs_local)
    inside = (seg_index[None, :] >= start_all[:, None]) & (seg_index[None, :] < stop_all[:, None])
    head_of = lax.broadcasted_iota(jnp.int32, (pool_heads_local, channels), 1) // pool_width
    head_mask = head_of == lax.broadcasted_iota(jnp.int32, (pool_heads_local, channels), 0)
    keys_masked = jnp.where(head_mask[:, None, :], summaries[None, :, :], jnp.zeros((), summaries.dtype))
    logits = (
        jnp.einsum("pc,asc->aps", queries_all, keys_masked, preferred_element_type=jnp.float32)
        * scale_factor
    )
    logits = jnp.where(inside[None], logits, MASKED)
    peak = jnp.max(logits, axis=2).astype(jnp.bfloat16).astype(jnp.float32)
    expo = jnp.where(inside[None], jnp.exp(logits - peak[:, :, None]), 0.0)
    denom = jnp.sum(expo, axis=2)
    numer = jnp.einsum(
        "aps,asc->pc", expo.astype(jnp.bfloat16), keys_masked, preferred_element_type=jnp.float32
    )
    denom_high = denom.astype(jnp.bfloat16)
    denom_low = (denom - denom_high.astype(jnp.float32)).astype(jnp.bfloat16)
    parts = jnp.concatenate(
        [
            numer.reshape(pools_all, channels).astype(jnp.bfloat16),
            peak.T.astype(jnp.bfloat16),
            denom_high.T,
            denom_low.T,
        ],
        axis=1,
    )
    parts = parts.reshape(seq_count, pools_local, channels + 3 * pool_heads_local)
    place = lax.axis_index("seq")
    gathered = [lax.dynamic_index_in_dim(parts, place, 0, False)]
    for shift in range(1, seq_count):
        chunk = lax.dynamic_index_in_dim(parts, (place + shift) % seq_count, 0, False)
        gathered.append(
            lax.ppermute(
                chunk, "seq", [(i, (i + shift) % seq_count) for i in range(seq_count)]
            )
        )
    parts = jnp.stack(gathered).astype(jnp.float32)
    numer_parts = parts[:, :, :channels].reshape(
        seq_count, pools_local, pool_heads_local, pool_width
    )
    stats_parts = parts[:, :, channels:].reshape(seq_count, pools_local, 3, pool_heads_local)
    peak_parts = stats_parts[:, :, 0]
    denom_parts = stats_parts[:, :, 1] + stats_parts[:, :, 2]
    peak_all = jnp.max(peak_parts, axis=0)
    rescale = jnp.exp(peak_parts - peak_all[None])
    denom_all = jnp.sum(rescale * denom_parts, axis=0)
    numer_all = jnp.sum(rescale[:, :, :, None] * numer_parts, axis=0)
    pooled = (numer_all / denom_all[:, :, None]).reshape(pools_local, channels)
    return (mixed_seq, pooled)


def solution(mesh):
    in_specs = (
        P(("groups", "seq"), "tensor"),
        P(("groups", "seq"), "tensor"),
        P(("groups", "seq"), None),
        P("tensor", ("groups", "seq")),
        P("tensor", ("groups", "seq")),
        P("tensor"),
        P(None, "tensor"),
        P(),
        P("tensor"),
        P(("groups", "seq")),
        P(("groups", "seq"), "tensor"),
        P(("groups", "seq")),
        P(("groups", "seq")),
    )
    out_specs = (P(("groups", "seq"), "tensor"), P(("groups", "seq"), "tensor"))
    return jax.shard_map(local, mesh=mesh, in_specs=in_specs, out_specs=out_specs, check_vma=False)
```

```python
import math

import jax
import jax.numpy as jnp
from jax import lax
from jax.experimental.layout import Layout, with_layout_constraint
from jax.sharding import PartitionSpec as P

STRETCH = 256
POOL_HEADS = 32


EPSILON = 1e-05
MASKED = -1e30


def passed_along(value, axis, steps):
    count = lax.axis_size(axis)
    leading, last = (max(0, -steps), min(count, count - steps))
    return lax.ppermute(value, axis, [(source, source + steps) for source in range(leading, last)])


def silu_act(values):
    return values / (1.0 + jnp.exp(-values))


def causal_conv(before, current, weights):
    kernel_width = weights.shape[0]
    length = current.shape[0]
    padded = jnp.concatenate([before, current], axis=0)
    summed = jnp.zeros(current.shape, jnp.float32)
    for offset in range(kernel_width):
        summed = summed + padded[offset : offset + length].astype(jnp.float32) * weights[
            offset
        ].astype(jnp.float32)
    return silu_act(summed).astype(jnp.bfloat16)


def stretch_local(x_block, b_block, c_block, step_block, keep_block):
    block_len = x_block.shape[0]
    cumul_keep = jnp.cumsum(keep_block, axis=1)
    lower_mask = lax.broadcasted_iota(jnp.int32, (block_len, block_len), 0) >= lax.broadcasted_iota(
        jnp.int32, (block_len, block_len), 1
    )
    inner_prod = jnp.einsum("is,js->ij", c_block, b_block, preferred_element_type=jnp.float32)
    spread = cumul_keep[:, :, None] - cumul_keep[:, None, :]
    decay_mask = jnp.where(lower_mask[None], jnp.exp(jnp.where(lower_mask[None], spread, 0.0)), 0.0)
    mixing = (decay_mask * inner_prod[None] * step_block[:, None, :]).astype(jnp.bfloat16)
    intra_part = jnp.einsum("hij,jhp->hpi", mixing, x_block, preferred_element_type=jnp.float32)
    tail_weight = jnp.exp(cumul_keep[:, -1:] - cumul_keep) * step_block
    weighted = (tail_weight.T[:, :, None] * x_block.astype(jnp.float32)).astype(jnp.bfloat16)
    stretch_state = jnp.einsum("jhp,js->hps", weighted, b_block, preferred_element_type=jnp.float32)
    return (intra_part, stretch_state, cumul_keep)


def combine(earlier, later):
    return (earlier[0] * jnp.exp(later[1])[:, None, None] + later[0], earlier[1] + later[1])


def exclusive_scan(state, decay, axis, rider):
    count = lax.axis_size(axis)
    window = (state, decay)
    before = (jnp.zeros_like(state), jnp.zeros_like(decay))
    shift = 1
    while shift < count:
        sent_state = passed_along(window[0].astype(jnp.bfloat16), axis, shift)
        sent_decay = passed_along(window[1], axis, shift)
        if shift == 1:
            sent_state, rider = lax.optimization_barrier((sent_state, rider))
        received = (sent_state.astype(jnp.float32), sent_decay)
        before = combine(received, before)
        if shift * 2 < count:
            window = combine(received, window)
        shift *= 2
    return before[0], rider


def butterfly_sum(value, axis):
    count = lax.axis_size(axis)
    if count & (count - 1):
        return lax.psum(value, axis)
    stride = 1
    while stride < count:
        partner = lax.ppermute(value, axis, [(i, i ^ stride) for i in range(count)])
        value = value + partner
        stride *= 2
    return value


def read_state(c_block, state_in):
    state_high = state_in.astype(jnp.bfloat16)
    state_low = (state_in - state_high.astype(jnp.float32)).astype(jnp.bfloat16)
    high_part = jnp.einsum("hps,is->hpi", state_high, c_block, preferred_element_type=jnp.float32)
    low_part = jnp.einsum("hps,is->hpi", state_low, c_block, preferred_element_type=jnp.float32)
    return high_part + low_part


def local(
    x_in,
    z_gate,
    bc_in,
    step_size,
    log_keep,
    skip_gain,
    conv_x,
    conv_bc,
    norm_gain,
    seg_ends,
    pool_query,
    pool_start,
    pool_stop,
):
    tok_rows = x_in.shape[0]
    channels = x_in.shape[1]
    heads_local = step_size.shape[0]
    head_width = channels // heads_local
    state_width = bc_in.shape[1] // 2
    rim_rows = conv_x.shape[0] - 1
    seq_count = lax.axis_size("seq")
    pools_local = pool_query.shape[0]
    bounds = jnp.stack([pool_start, pool_stop], axis=1)
    bounds_split = jnp.concatenate([bounds // 64, bounds % 64], axis=1).astype(jnp.bfloat16)
    query_rows = jnp.concatenate([pool_query, bounds_split], axis=1)
    query_rows = jnp.broadcast_to(query_rows[None], (seq_count,) + query_rows.shape)
    query_rows = lax.all_to_all(
        query_rows.reshape(seq_count * pools_local, -1), "seq", 0, 0, tiled=True
    )
    queries_all = query_rows[:, :channels]
    bounds_all = query_rows[:, channels:].astype(jnp.int32)
    start_all = bounds_all[:, 0] * 64 + bounds_all[:, 2]
    stop_all = bounds_all[:, 1] * 64 + bounds_all[:, 3]
    edge_rows = jnp.concatenate([x_in[tok_rows - rim_rows :], bc_in[tok_rows - rim_rows :]], axis=1)
    before = passed_along(edge_rows, "seq", 1)
    x_conv = causal_conv(before[:, :channels], x_in, conv_x)
    x_conv = with_layout_constraint(x_conv, Layout(major_to_minor=(0, 1)))
    bc_conv = causal_conv(before[:, channels:], bc_in, conv_bc)
    b_mat = bc_conv[:, :state_width]
    c_mat = bc_conv[:, state_width:]
    x_heads = x_conv.reshape(tok_rows, heads_local, head_width)
    stretch_count = tok_rows // STRETCH
    entry_state = jnp.zeros((heads_local, head_width, state_width), jnp.float32)
    decay_total = jnp.zeros((heads_local,), jnp.float32)
    saved_parts = []
    for block_index in range(stretch_count):
        first_row = block_index * STRETCH
        last_row = first_row + STRETCH
        intra_part, stretch_state, cumul_keep = stretch_local(
            x_heads[first_row:last_row],
            b_mat[first_row:last_row],
            c_mat[first_row:last_row],
            step_size[:, first_row:last_row],
            log_keep[:, first_row:last_row],
        )
        saved_parts.append((intra_part, cumul_keep, entry_state, decay_total))
        entry_state = jnp.exp(cumul_keep[:, -1])[:, None, None] * entry_state + stretch_state
        decay_total = decay_total + cumul_keep[:, -1]
    incoming, z_late = exclusive_scan(entry_state, decay_total, "seq", z_gate)
    x_major = x_conv.T.reshape(heads_local, head_width, tok_rows)
    z_major = z_late.T
    pieces_out = []
    for block_index in range(stretch_count):
        intra_part, cumul_keep, entry_part, decay_part = saved_parts[block_index]
        first_row = block_index * STRETCH
        state_in = entry_part + jnp.exp(decay_part)[:, None, None] * incoming
        from_state = read_state(c_mat[first_row : first_row + STRETCH], state_in)
        pieces_out.append(intra_part + jnp.exp(cumul_keep)[:, None, :] * from_state)
    ssd_out = jnp.concatenate(pieces_out, axis=2) + skip_gain[:, None, None] * x_major.astype(
        jnp.float32
    )
    gated = ssd_out.reshape(channels, tok_rows) * silu_act(z_major.astype(jnp.float32))
    gated = with_layout_constraint(gated, Layout(major_to_minor=(0, 1)))
    square_sum = butterfly_sum(jnp.sum(gated * gated, axis=0), "tensor")
    width_all = channels * lax.axis_size("tensor")
    mixed_major = (
        gated * lax.rsqrt(square_sum / width_all + EPSILON)[None, :] * norm_gain[:, None]
    ).astype(jnp.bfloat16)
    mixed_seq = mixed_major.T
    local_ends = seg_ends - lax.axis_index("seq") * tok_rows
    picks = (
        lax.broadcasted_iota(jnp.int32, (tok_rows, local_ends.shape[0]), 0) == local_ends[None, :]
    ).astype(jnp.bfloat16)
    summaries = (
        jnp.einsum("ct,ts->sc", mixed_major, picks, preferred_element_type=jnp.float32)
    ).astype(jnp.bfloat16)
    pool_heads_local = POOL_HEADS // lax.axis_size("tensor")
    pool_width = channels // pool_heads_local
    scale_factor = 1.0 / math.sqrt(pool_width)
    pools_all = queries_all.shape[0]
    segs_local = summaries.shape[0]
    seg_index = lax.axis_index("seq") * segs_local + lax.iota(jnp.int32, segs_local)
    inside = (seg_index[None, :] >= start_all[:, None]) & (seg_index[None, :] < stop_all[:, None])
    head_of = lax.broadcasted_iota(jnp.int32, (pool_heads_local, channels), 1) // pool_width
    head_mask = head_of == lax.broadcasted_iota(jnp.int32, (pool_heads_local, channels), 0)
    keys_masked = jnp.where(head_mask[:, None, :], summaries[None, :, :], jnp.zeros((), summaries.dtype))
    logits = (
        jnp.einsum("pc,asc->aps", queries_all, keys_masked, preferred_element_type=jnp.float32)
        * scale_factor
    )
    logits = jnp.where(inside[None], logits, MASKED)
    peak = jnp.max(logits, axis=2).astype(jnp.bfloat16).astype(jnp.float32)
    expo = jnp.where(inside[None], jnp.exp(logits - peak[:, :, None]), 0.0)
    denom = jnp.sum(expo, axis=2)
    numer = jnp.einsum(
        "aps,asc->pc", expo.astype(jnp.bfloat16), keys_masked, preferred_element_type=jnp.float32
    )
    denom_high = denom.astype(jnp.bfloat16)
    denom_low = (denom - denom_high.astype(jnp.float32)).astype(jnp.bfloat16)
    parts = jnp.concatenate(
        [
            numer.reshape(pools_all, channels).astype(jnp.bfloat16),
            peak.T.astype(jnp.bfloat16),
            denom_high.T,
            denom_low.T,
        ],
        axis=1,
    )
    parts = parts.reshape(seq_count, pools_local, channels + 3 * pool_heads_local)
    place = lax.axis_index("seq")
    gathered = [lax.dynamic_index_in_dim(parts, place, 0, False)]
    for shift in range(1, seq_count):
        chunk = lax.dynamic_index_in_dim(parts, (place + shift) % seq_count, 0, False)
        gathered.append(
            lax.ppermute(
                chunk, "seq", [(i, (i + shift) % seq_count) for i in range(seq_count)]
            )
        )
    parts = jnp.stack(gathered).astype(jnp.float32)
    numer_parts = parts[:, :, :channels].reshape(
        seq_count, pools_local, pool_heads_local, pool_width
    )
    stats_parts = parts[:, :, channels:].reshape(seq_count, pools_local, 3, pool_heads_local)
    peak_parts = stats_parts[:, :, 0]
    denom_parts = stats_parts[:, :, 1] + stats_parts[:, :, 2]
    peak_all = jnp.max(peak_parts, axis=0)
    rescale = jnp.exp(peak_parts - peak_all[None])
    denom_all = jnp.sum(rescale * denom_parts, axis=0)
    numer_all = jnp.sum(rescale[:, :, :, None] * numer_parts, axis=0)
    pooled = (numer_all / denom_all[:, :, None]).reshape(pools_local, channels)
    return (mixed_seq, pooled)


def solution(mesh):
    in_specs = (
        P(("groups", "seq"), "tensor"),
        P(("groups", "seq"), "tensor"),
        P(("groups", "seq"), None),
        P("tensor", ("groups", "seq")),
        P("tensor", ("groups", "seq")),
        P("tensor"),
        P(None, "tensor"),
        P(),
        P("tensor"),
        P(("groups", "seq")),
        P(("groups", "seq"), "tensor"),
        P(("groups", "seq")),
        P(("groups", "seq")),
    )
    out_specs = (P(("groups", "seq"), "tensor"), P(("groups", "seq"), "tensor"))
    return jax.shard_map(local, mesh=mesh, in_specs=in_specs, out_specs=out_specs, check_vma=False)
```

```python
import math

import jax
import jax.numpy as jnp
from jax import lax
from jax.experimental.layout import Layout, with_layout_constraint
from jax.sharding import PartitionSpec as P

STRETCH = 256
POOL_HEADS = 32


EPSILON = 1e-05
MASKED = -1e30


def passed_along(value, axis, steps):
    count = lax.axis_size(axis)
    leading, last = (max(0, -steps), min(count, count - steps))
    return lax.ppermute(value, axis, [(source, source + steps) for source in range(leading, last)])


def silu_act(values):
    return values / (1.0 + jnp.exp(-values))


def causal_conv(before, current, weights):
    kernel_width = weights.shape[0]
    length = current.shape[0]
    padded = jnp.concatenate([before, current], axis=0)
    summed = jnp.zeros(current.shape, jnp.float32)
    for offset in range(kernel_width):
        summed = summed + padded[offset : offset + length].astype(jnp.float32) * weights[
            offset
        ].astype(jnp.float32)
    return silu_act(summed).astype(jnp.bfloat16)


def stretch_local(x_block, b_block, c_block, step_block, keep_block):
    block_len = x_block.shape[0]
    cumul_keep = jnp.cumsum(keep_block, axis=1)
    lower_mask = lax.broadcasted_iota(jnp.int32, (block_len, block_len), 0) >= lax.broadcasted_iota(
        jnp.int32, (block_len, block_len), 1
    )
    inner_prod = jnp.einsum("is,js->ij", c_block, b_block, preferred_element_type=jnp.float32)
    spread = cumul_keep[:, :, None] - cumul_keep[:, None, :]
    decay_mask = jnp.where(lower_mask[None], jnp.exp(jnp.where(lower_mask[None], spread, 0.0)), 0.0)
    mixing = (decay_mask * inner_prod[None] * step_block[:, None, :]).astype(jnp.bfloat16)
    intra_part = jnp.einsum("hij,jhp->hpi", mixing, x_block, preferred_element_type=jnp.float32)
    tail_weight = jnp.exp(cumul_keep[:, -1:] - cumul_keep) * step_block
    weighted = (tail_weight.T[:, :, None] * x_block.astype(jnp.float32)).astype(jnp.bfloat16)
    stretch_state = jnp.einsum("jhp,js->hps", weighted, b_block, preferred_element_type=jnp.float32)
    return (intra_part, stretch_state, cumul_keep)


def combine(earlier, later):
    return (earlier[0] * jnp.exp(later[1])[:, None, None] + later[0], earlier[1] + later[1])


def exclusive_scan(state, decay, axis, rider):
    count = lax.axis_size(axis)
    window = (state, decay)
    before = (jnp.zeros_like(state), jnp.zeros_like(decay))
    shift = 1
    while shift < count:
        sent_state = passed_along(window[0].astype(jnp.bfloat16), axis, shift)
        sent_decay = passed_along(window[1], axis, shift)
        if shift == 1:
            sent_state, rider = lax.optimization_barrier((sent_state, rider))
        received = (sent_state.astype(jnp.float32), sent_decay)
        before = combine(received, before)
        if shift * 2 < count:
            window = combine(received, window)
        shift *= 2
    return before[0], rider


def butterfly_sum(value, axis):
    count = lax.axis_size(axis)
    if count & (count - 1):
        return lax.psum(value, axis)
    stride = 1
    while stride < count:
        partner = lax.ppermute(value, axis, [(i, i ^ stride) for i in range(count)])
        value = value + partner
        stride *= 2
    return value


def read_state(c_block, state_in):
    state_high = state_in.astype(jnp.bfloat16)
    state_low = (state_in - state_high.astype(jnp.float32)).astype(jnp.bfloat16)
    high_part = jnp.einsum("hps,is->hpi", state_high, c_block, preferred_element_type=jnp.float32)
    low_part = jnp.einsum("hps,is->hpi", state_low, c_block, preferred_element_type=jnp.float32)
    return high_part + low_part


def local(
    x_in,
    z_gate,
    bc_in,
    step_size,
    log_keep,
    skip_gain,
    conv_x,
    conv_bc,
    norm_gain,
    seg_ends,
    pool_query,
    pool_start,
    pool_stop,
):
    tok_rows = x_in.shape[0]
    channels = x_in.shape[1]
    heads_local = step_size.shape[0]
    head_width = channels // heads_local
    state_width = bc_in.shape[1] // 2
    rim_rows = conv_x.shape[0] - 1
    seq_count = lax.axis_size("seq")
    pools_local = pool_query.shape[0]
    bounds = jnp.stack([pool_start, pool_stop], axis=1)
    bounds_split = jnp.concatenate([bounds // 64, bounds % 64], axis=1).astype(jnp.bfloat16)
    query_rows = jnp.concatenate([pool_query, bounds_split], axis=1)
    query_rows = jnp.broadcast_to(query_rows[None], (seq_count,) + query_rows.shape)
    query_rows = lax.all_to_all(
        query_rows.reshape(seq_count * pools_local, -1), "seq", 0, 0, tiled=True
    )
    queries_all = query_rows[:, :channels]
    bounds_all = query_rows[:, channels:].astype(jnp.int32)
    start_all = bounds_all[:, 0] * 64 + bounds_all[:, 2]
    stop_all = bounds_all[:, 1] * 64 + bounds_all[:, 3]
    edge_rows = jnp.concatenate([x_in[tok_rows - rim_rows :], bc_in[tok_rows - rim_rows :]], axis=1)
    before = passed_along(edge_rows, "seq", 1)
    x_conv = causal_conv(before[:, :channels], x_in, conv_x)
    x_conv = with_layout_constraint(x_conv, Layout(major_to_minor=(0, 1)))
    bc_conv = causal_conv(before[:, channels:], bc_in, conv_bc)
    b_mat = bc_conv[:, :state_width]
    c_mat = bc_conv[:, state_width:]
    x_heads = x_conv.reshape(tok_rows, heads_local, head_width)
    stretch_count = tok_rows // STRETCH
    entry_state = jnp.zeros((heads_local, head_width, state_width), jnp.float32)
    decay_total = jnp.zeros((heads_local,), jnp.float32)
    saved_parts = []
    for block_index in range(stretch_count):
        first_row = block_index * STRETCH
        last_row = first_row + STRETCH
        intra_part, stretch_state, cumul_keep = stretch_local(
            x_heads[first_row:last_row],
            b_mat[first_row:last_row],
            c_mat[first_row:last_row],
            step_size[:, first_row:last_row],
            log_keep[:, first_row:last_row],
        )
        saved_parts.append((intra_part, cumul_keep, entry_state, decay_total))
        entry_state = jnp.exp(cumul_keep[:, -1])[:, None, None] * entry_state + stretch_state
        decay_total = decay_total + cumul_keep[:, -1]
    incoming, z_late = exclusive_scan(entry_state, decay_total, "seq", z_gate)
    x_major = x_conv.T.reshape(heads_local, head_width, tok_rows)
    z_major = z_late.T
    pieces_out = []
    for block_index in range(stretch_count):
        intra_part, cumul_keep, entry_part, decay_part = saved_parts[block_index]
        first_row = block_index * STRETCH
        state_in = entry_part + jnp.exp(decay_part)[:, None, None] * incoming
        from_state = read_state(c_mat[first_row : first_row + STRETCH], state_in)
        pieces_out.append(intra_part + jnp.exp(cumul_keep)[:, None, :] * from_state)
    ssd_out = jnp.concatenate(pieces_out, axis=2) + skip_gain[:, None, None] * x_major.astype(
        jnp.float32
    )
    gated = ssd_out.reshape(channels, tok_rows) * silu_act(z_major.astype(jnp.float32))
    gated = with_layout_constraint(gated, Layout(major_to_minor=(0, 1)))
    square_sum = butterfly_sum(jnp.sum(gated * gated, axis=0), "tensor")
    width_all = channels * lax.axis_size("tensor")
    mixed_major = (
        gated * lax.rsqrt(square_sum / width_all + EPSILON)[None, :] * norm_gain[:, None]
    ).astype(jnp.bfloat16)
    mixed_seq = mixed_major.T
    local_ends = seg_ends - lax.axis_index("seq") * tok_rows
    summaries = jnp.take(mixed_seq, local_ends, axis=0)
    pool_heads_local = POOL_HEADS // lax.axis_size("tensor")
    pool_width = channels // pool_heads_local
    scale_factor = 1.0 / math.sqrt(pool_width)
    pools_all = queries_all.shape[0]
    segs_local = summaries.shape[0]
    seg_index = lax.axis_index("seq") * segs_local + lax.iota(jnp.int32, segs_local)
    inside = (seg_index[None, :] >= start_all[:, None]) & (seg_index[None, :] < stop_all[:, None])
    head_of = lax.broadcasted_iota(jnp.int32, (pool_heads_local, channels), 1) // pool_width
    head_mask = head_of == lax.broadcasted_iota(jnp.int32, (pool_heads_local, channels), 0)
    keys_masked = jnp.where(head_mask[:, None, :], summaries[None, :, :], jnp.zeros((), summaries.dtype))
    logits = (
        jnp.einsum("pc,asc->aps", queries_all, keys_masked, preferred_element_type=jnp.float32)
        * scale_factor
    )
    logits = jnp.where(inside[None], logits, MASKED)
    peak = jnp.max(logits, axis=2).astype(jnp.bfloat16).astype(jnp.float32)
    expo = jnp.where(inside[None], jnp.exp(logits - peak[:, :, None]), 0.0)
    denom = jnp.sum(expo, axis=2)
    numer = jnp.einsum(
        "aps,asc->pc", expo.astype(jnp.bfloat16), keys_masked, preferred_element_type=jnp.float32
    )
    denom_high = denom.astype(jnp.bfloat16)
    denom_low = (denom - denom_high.astype(jnp.float32)).astype(jnp.bfloat16)
    stats = jnp.concatenate([peak.T.astype(jnp.bfloat16), denom_high.T, denom_low.T], axis=1)
    stats = stats.reshape(seq_count, -1)
    stats = jnp.pad(stats, ((0, 0), (0, channels - stats.shape[1])))
    parts = jnp.concatenate(
        [
            numer.reshape(seq_count, pools_local, channels).astype(jnp.bfloat16),
            stats[:, None, :],
        ],
        axis=1,
    )
    place = lax.axis_index("seq")
    gathered = [lax.dynamic_index_in_dim(parts, place, 0, False)]
    for shift in range(1, seq_count):
        chunk = lax.dynamic_index_in_dim(parts, (place + shift) % seq_count, 0, False)
        gathered.append(
            lax.ppermute(
                chunk, "seq", [(i, (i + shift) % seq_count) for i in range(seq_count)]
            )
        )
    parts = jnp.stack(gathered).astype(jnp.float32)
    numer_parts = parts[:, :pools_local].reshape(
        seq_count, pools_local, pool_heads_local, pool_width
    )
    stats_parts = parts[:, pools_local, : pools_local * 3 * pool_heads_local].reshape(
        seq_count, pools_local, 3, pool_heads_local
    )
    peak_parts = stats_parts[:, :, 0]
    denom_parts = stats_parts[:, :, 1] + stats_parts[:, :, 2]
    peak_all = jnp.max(peak_parts, axis=0)
    rescale = jnp.exp(peak_parts - peak_all[None])
    denom_all = jnp.sum(rescale * denom_parts, axis=0)
    numer_all = jnp.sum(rescale[:, :, :, None] * numer_parts, axis=0)
    pooled = (numer_all / denom_all[:, :, None]).reshape(pools_local, channels)
    return (mixed_seq, pooled)


def solution(mesh):
    in_specs = (
        P(("groups", "seq"), "tensor"),
        P(("groups", "seq"), "tensor"),
        P(("groups", "seq"), None),
        P("tensor", ("groups", "seq")),
        P("tensor", ("groups", "seq")),
        P("tensor"),
        P(None, "tensor"),
        P(),
        P("tensor"),
        P(("groups", "seq")),
        P(("groups", "seq"), "tensor"),
        P(("groups", "seq")),
        P(("groups", "seq")),
    )
    out_specs = (P(("groups", "seq"), "tensor"), P(("groups", "seq"), "tensor"))
    return jax.shard_map(local, mesh=mesh, in_specs=in_specs, out_specs=out_specs, check_vma=False)
```

```python
import math

import jax
import jax.numpy as jnp
from jax import lax
from jax.experimental.layout import Layout, with_layout_constraint
from jax.sharding import PartitionSpec as P

STRETCH = 256
POOL_HEADS = 32


EPSILON = 1e-05
MASKED = -1e30


def passed_along(value, axis, steps):
    count = lax.axis_size(axis)
    leading, last = (max(0, -steps), min(count, count - steps))
    return lax.ppermute(value, axis, [(source, source + steps) for source in range(leading, last)])


def silu_act(values):
    return values / (1.0 + jnp.exp(-values))


def causal_conv(before, current, weights):
    kernel_width = weights.shape[0]
    length = current.shape[0]
    padded = jnp.concatenate([before, current], axis=0)
    summed = jnp.zeros(current.shape, jnp.float32)
    for offset in range(kernel_width):
        summed = summed + padded[offset : offset + length].astype(jnp.float32) * weights[
            offset
        ].astype(jnp.float32)
    return silu_act(summed).astype(jnp.bfloat16)


def stretch_local(x_block, b_block, c_block, step_block, keep_block):
    block_len = x_block.shape[0]
    cumul_keep = jnp.cumsum(keep_block, axis=1)
    lower_mask = lax.broadcasted_iota(jnp.int32, (block_len, block_len), 0) >= lax.broadcasted_iota(
        jnp.int32, (block_len, block_len), 1
    )
    inner_prod = jnp.einsum("is,js->ij", c_block, b_block, preferred_element_type=jnp.float32)
    spread = cumul_keep[:, :, None] - cumul_keep[:, None, :]
    decay_mask = jnp.where(lower_mask[None], jnp.exp(jnp.where(lower_mask[None], spread, 0.0)), 0.0)
    mixing = (decay_mask * inner_prod[None] * step_block[:, None, :]).astype(jnp.bfloat16)
    intra_part = jnp.einsum("hij,jhp->hpi", mixing, x_block, preferred_element_type=jnp.float32)
    tail_weight = jnp.exp(cumul_keep[:, -1:] - cumul_keep) * step_block
    weighted = (tail_weight.T[:, :, None] * x_block.astype(jnp.float32)).astype(jnp.bfloat16)
    stretch_state = jnp.einsum("jhp,js->hps", weighted, b_block, preferred_element_type=jnp.float32)
    return (intra_part, stretch_state, cumul_keep)


def combine(earlier, later):
    return (earlier[0] * jnp.exp(later[1])[:, None, None] + later[0], earlier[1] + later[1])


def exclusive_scan(state, decay, axis, rider):
    count = lax.axis_size(axis)
    window = (state, decay)
    before = (jnp.zeros_like(state), jnp.zeros_like(decay))
    shift = 1
    while shift < count:
        sent_state = passed_along(window[0].astype(jnp.bfloat16), axis, shift)
        sent_decay = passed_along(window[1], axis, shift)
        if shift == 1:
            sent_state, rider = lax.optimization_barrier((sent_state, rider))
        received = (sent_state.astype(jnp.float32), sent_decay)
        before = combine(received, before)
        if shift * 2 < count:
            window = combine(received, window)
        shift *= 2
    return before[0], rider


def butterfly_sum(value, axis):
    count = lax.axis_size(axis)
    if count & (count - 1):
        return lax.psum(value, axis)
    stride = 1
    while stride < count:
        partner = lax.ppermute(value, axis, [(i, i ^ stride) for i in range(count)])
        value = value + partner
        stride *= 2
    return value


def read_state(c_block, state_in):
    state_high = state_in.astype(jnp.bfloat16)
    state_low = (state_in - state_high.astype(jnp.float32)).astype(jnp.bfloat16)
    high_part = jnp.einsum("hps,is->hpi", state_high, c_block, preferred_element_type=jnp.float32)
    low_part = jnp.einsum("hps,is->hpi", state_low, c_block, preferred_element_type=jnp.float32)
    return high_part + low_part


def local(
    x_in,
    z_gate,
    bc_in,
    step_size,
    log_keep,
    skip_gain,
    conv_x,
    conv_bc,
    norm_gain,
    seg_ends,
    pool_query,
    pool_start,
    pool_stop,
):
    tok_rows = x_in.shape[0]
    channels = x_in.shape[1]
    heads_local = step_size.shape[0]
    head_width = channels // heads_local
    state_width = bc_in.shape[1] // 2
    rim_rows = conv_x.shape[0] - 1
    seq_count = lax.axis_size("seq")
    pools_local = pool_query.shape[0]
    bounds = jnp.stack([pool_start, pool_stop], axis=1)
    bounds_split = jnp.concatenate([bounds // 64, bounds % 64], axis=1).astype(jnp.bfloat16)
    query_rows = jnp.concatenate([pool_query, bounds_split], axis=1)
    edge_rows = jnp.concatenate([x_in[tok_rows - rim_rows :], bc_in[tok_rows - rim_rows :]], axis=1)
    before = passed_along(edge_rows, "seq", 1)
    x_conv = causal_conv(before[:, :channels], x_in, conv_x)
    x_conv = with_layout_constraint(x_conv, Layout(major_to_minor=(0, 1)))
    bc_conv = causal_conv(before[:, channels:], bc_in, conv_bc)
    b_mat = bc_conv[:, :state_width]
    c_mat = bc_conv[:, state_width:]
    x_heads = x_conv.reshape(tok_rows, heads_local, head_width)
    stretch_count = tok_rows // STRETCH
    entry_state = jnp.zeros((heads_local, head_width, state_width), jnp.float32)
    decay_total = jnp.zeros((heads_local,), jnp.float32)
    saved_parts = []
    for block_index in range(stretch_count):
        first_row = block_index * STRETCH
        last_row = first_row + STRETCH
        intra_part, stretch_state, cumul_keep = stretch_local(
            x_heads[first_row:last_row],
            b_mat[first_row:last_row],
            c_mat[first_row:last_row],
            step_size[:, first_row:last_row],
            log_keep[:, first_row:last_row],
        )
        saved_parts.append((intra_part, cumul_keep, entry_state, decay_total))
        entry_state = jnp.exp(cumul_keep[:, -1])[:, None, None] * entry_state + stretch_state
        decay_total = decay_total + cumul_keep[:, -1]
    incoming, z_late = exclusive_scan(entry_state, decay_total, "seq", z_gate)
    incoming, query_rows = lax.optimization_barrier((incoming, query_rows))
    query_rows = jnp.broadcast_to(query_rows[None], (seq_count,) + query_rows.shape)
    query_rows = lax.all_to_all(
        query_rows.reshape(seq_count * pools_local, -1), "seq", 0, 0, tiled=True
    )
    queries_all = query_rows[:, :channels]
    bounds_all = query_rows[:, channels:].astype(jnp.int32)
    start_all = bounds_all[:, 0] * 64 + bounds_all[:, 2]
    stop_all = bounds_all[:, 1] * 64 + bounds_all[:, 3]
    x_major = x_conv.T.reshape(heads_local, head_width, tok_rows)
    z_major = z_late.T
    pieces_out = []
    for block_index in range(stretch_count):
        intra_part, cumul_keep, entry_part, decay_part = saved_parts[block_index]
        first_row = block_index * STRETCH
        state_in = entry_part + jnp.exp(decay_part)[:, None, None] * incoming
        from_state = read_state(c_mat[first_row : first_row + STRETCH], state_in)
        pieces_out.append(intra_part + jnp.exp(cumul_keep)[:, None, :] * from_state)
    ssd_out = jnp.concatenate(pieces_out, axis=2) + skip_gain[:, None, None] * x_major.astype(
        jnp.float32
    )
    gated = ssd_out.reshape(channels, tok_rows) * silu_act(z_major.astype(jnp.float32))
    gated = with_layout_constraint(gated, Layout(major_to_minor=(0, 1)))
    square_sum = butterfly_sum(jnp.sum(gated * gated, axis=0), "tensor")
    width_all = channels * lax.axis_size("tensor")
    mixed_major = (
        gated * lax.rsqrt(square_sum / width_all + EPSILON)[None, :] * norm_gain[:, None]
    ).astype(jnp.bfloat16)
    mixed_seq = mixed_major.T
    local_ends = seg_ends - lax.axis_index("seq") * tok_rows
    summaries = jnp.take(mixed_seq, local_ends, axis=0)
    pool_heads_local = POOL_HEADS // lax.axis_size("tensor")
    pool_width = channels // pool_heads_local
    scale_factor = 1.0 / math.sqrt(pool_width)
    pools_all = queries_all.shape[0]
    segs_local = summaries.shape[0]
    seg_index = lax.axis_index("seq") * segs_local + lax.iota(jnp.int32, segs_local)
    inside = (seg_index[None, :] >= start_all[:, None]) & (seg_index[None, :] < stop_all[:, None])
    head_of = lax.broadcasted_iota(jnp.int32, (pool_heads_local, channels), 1) // pool_width
    head_mask = head_of == lax.broadcasted_iota(jnp.int32, (pool_heads_local, channels), 0)
    keys_masked = jnp.where(head_mask[:, None, :], summaries[None, :, :], jnp.zeros((), summaries.dtype))
    logits = (
        jnp.einsum("pc,asc->aps", queries_all, keys_masked, preferred_element_type=jnp.float32)
        * scale_factor
    )
    logits = jnp.where(inside[None], logits, MASKED)
    peak = jnp.max(logits, axis=2).astype(jnp.bfloat16).astype(jnp.float32)
    expo = jnp.where(inside[None], jnp.exp(logits - peak[:, :, None]), 0.0)
    denom = jnp.sum(expo, axis=2)
    numer = jnp.einsum(
        "aps,asc->pc", expo.astype(jnp.bfloat16), keys_masked, preferred_element_type=jnp.float32
    )
    denom_high = denom.astype(jnp.bfloat16)
    denom_low = (denom - denom_high.astype(jnp.float32)).astype(jnp.bfloat16)
    parts = jnp.concatenate(
        [
            numer.reshape(pools_all, channels).astype(jnp.bfloat16),
            peak.T.astype(jnp.bfloat16),
            denom_high.T,
            denom_low.T,
        ],
        axis=1,
    )
    parts = parts.reshape(seq_count, pools_local, channels + 3 * pool_heads_local)
    place = lax.axis_index("seq")
    gathered = [lax.dynamic_index_in_dim(parts, place, 0, False)]
    for shift in range(1, seq_count):
        chunk = lax.dynamic_index_in_dim(parts, (place + shift) % seq_count, 0, False)
        gathered.append(
            lax.ppermute(
                chunk, "seq", [(i, (i + shift) % seq_count) for i in range(seq_count)]
            )
        )
    parts = jnp.stack(gathered).astype(jnp.float32)
    numer_parts = parts[:, :, :channels].reshape(
        seq_count, pools_local, pool_heads_local, pool_width
    )
    stats_parts = parts[:, :, channels:].reshape(seq_count, pools_local, 3, pool_heads_local)
    peak_parts = stats_parts[:, :, 0]
    denom_parts = stats_parts[:, :, 1] + stats_parts[:, :, 2]
    peak_all = jnp.max(peak_parts, axis=0)
    rescale = jnp.exp(peak_parts - peak_all[None])
    denom_all = jnp.sum(rescale * denom_parts, axis=0)
    numer_all = jnp.sum(rescale[:, :, :, None] * numer_parts, axis=0)
    pooled = (numer_all / denom_all[:, :, None]).reshape(pools_local, channels)
    return (mixed_seq, pooled)


def solution(mesh):
    in_specs = (
        P(("groups", "seq"), "tensor"),
        P(("groups", "seq"), "tensor"),
        P(("groups", "seq"), None),
        P("tensor", ("groups", "seq")),
        P("tensor", ("groups", "seq")),
        P("tensor"),
        P(None, "tensor"),
        P(),
        P("tensor"),
        P(("groups", "seq")),
        P(("groups", "seq"), "tensor"),
        P(("groups", "seq")),
        P(("groups", "seq")),
    )
    out_specs = (P(("groups", "seq"), "tensor"), P(("groups", "seq"), "tensor"))
    return jax.shard_map(local, mesh=mesh, in_specs=in_specs, out_specs=out_specs, check_vma=False)
```
